32 devices in a mesh: cohort: 2 (over x), row: 16 (over z, y, core).
Axes of the slice: x: 2, y: 2, z: 4, core: 2. Of those that a mesh axis runs over, the one named last changes fastest.
Arguments:
- embeddings: bfloat16 [192, 16384], P(None, ('cohort', 'row')), parts along dimension 1, may hold values from -0.4375 to 0.4375
- local_scale: bfloat16 [16384], P(('cohort', 'row')), parts along dimension 0, may hold values from 0.69921875 to 2
- degree_scale: float32 [16384], P(('cohort', 'row')), parts along dimension 0, may hold values from 0.5 to 2
- lanczos_block: float32 [16, 16384], P(None, ('cohort', 'row')), parts along dimension 1, may hold values from -25 to 25
- previous_block: float32 [16, 16384], P(None, ('cohort', 'row')), parts along dimension 1, may hold values from -6 to 6
- previous_coupling: float32 [32, 16], P('cohort'), parts along dimension 0, may hold values from -1.5 to 1.5
- tile_plan: int32 [128, 2], P(('cohort', 'row')), parts along dimension 0, may hold values from 0 to 7, as said below
- tile_counts: int32 [32], P(('cohort', 'row')), parts along dimension 0, may hold values from 0 to 4, as said below
Outputs:
- result: float32 [16, 16384], P(None, ('cohort', 'row')), parts along dimension 1
- coupling: float32 [32, 16], P('cohort'), parts along dimension 0
The draws below stay inside these ranges and needn't reach their ends.
There are 2 independent parts, one for each index of `cohort`. The reference program is written for one: setup_inputs(seed, part) draws one part's arguments, and reference() takes and returns one part's arrays. A program takes and returns all parts, laid end to end along the dimension named above; each array names one. Nothing has to cross between parts.
Inputs may be any that keep to these rules, and one draw needn't show every extreme that they name: Device d's rows of tile_plan (rows d * 4 to d * 4 + 3) start with tile_counts[d] live block pairs, each with row block no larger than column block; all live pairs over all devices are distinct; every other row holds one and the same pair, with row block no larger than column block, that is live on no device. `tile_counts`: the counts sum to 27; some device holds exactly 4.
All inputs are finite; a program needn't handle non-finite values.
Results may differ from the reference program's by a relative error of at most 0.002.
Values may be sent and summed in bfloat16 or wider, within the bound.
No kernel may reach another device: no remote copies, remote signals or barrier semaphores. Data moves between devices by JAX's collectives and lax.ppermute only.
A program may use at most 64 MiB of HBM per device.

```python
import math
import jax
import jax.numpy as jnp
from jax import lax

E = 192
LANCZOS = 16
BLK = 1024
OWNERS = 16
NTOT = 8192
NBLK = 8
TILES = 36
KEEP = 27
TMAX = 4


def draw_lanczos_block(key, part):
    key_offset, key_noise, key_rows = jax.random.split(key, 3)
    position = jnp.arange(NTOT, dtype=jnp.float32) / NTOT
    rising = 1.0 + 2.0 * position
    offsets = jax.random.uniform(key_offset, (LANCZOS, 1), jnp.float32, -0.12, 0.12)
    noise = jnp.clip(jax.random.normal(key_noise, (LANCZOS, NTOT), jnp.float32), -4.0, 4.0)
    row_scale = jnp.exp(jax.random.uniform(key_rows, (1, NTOT), jnp.float32, 0.0, 0.7))
    return (offsets + noise * rising[None, :] * row_scale).astype(jnp.float32)


def plan_tables(key):
    folded = jax.random.fold_in(key, 7)
    key_shuffle, key_devices = jax.random.split(folded)
    upper_rows, upper_cols = jnp.triu_indices(NBLK)
    shuffled = jax.random.permutation(key_shuffle, TILES)
    row_blocks = upper_rows[shuffled].astype(jnp.int32)
    col_blocks = upper_cols[shuffled].astype(jnp.int32)
    unused_row = row_blocks[KEEP]
    unused_col = col_blocks[KEEP]
    busy_count = max(OWNERS // 8, 1)
    remainder = KEEP - busy_count * TMAX
    base_count = remainder // (OWNERS - busy_count)
    extra_count = remainder % (OWNERS - busy_count)
    device_rank = jnp.arange(OWNERS, dtype=jnp.int32)
    pattern = jnp.where(device_rank < busy_count, TMAX, base_count + (device_rank - busy_count < extra_count).astype(jnp.int32))
    counts = pattern[jax.random.permutation(key_devices, OWNERS)].astype(jnp.int32)
    first_tile = jnp.cumsum(counts) - counts
    position = jnp.arange(TMAX, dtype=jnp.int32)
    tile_index = jnp.minimum(first_tile[:, None] + position[None, :], TILES - 1)
    is_live = position[None, :] < counts[:, None]
    plan = jnp.stack([jnp.where(is_live, row_blocks[tile_index], unused_row), jnp.where(is_live, col_blocks[tile_index], unused_col)], axis=-1)
    return (plan.reshape(OWNERS * TMAX, 2).astype(jnp.int32), counts)


def draw_tile_plan(key, part):
    return plan_tables(key)[0]


def draw_tile_counts(key, part):
    return plan_tables(key)[1]


def level_of(rng, extent, cuts, smallest, high):
    def one(dim, blocks):
        heights = jax.random.uniform(jax.random.fold_in(jax.random.fold_in(rng, 6), dim), (blocks,), jnp.float32, smallest / len(cuts), high / len(cuts))
        return jnp.repeat(jnp.exp(heights), extent[dim] // blocks).reshape((-1,) + (1,) * (len(extent) - dim - 1))

    gain = one(*cuts[0])
    for cut in cuts[1:]:
        gain = gain * one(*cut)
    return gain


def scatter_about(rng, shape, deviation, bound, pieces=(), kind=jnp.bfloat16):
    drawn = deviation * jax.random.normal(rng, shape, jnp.float32)
    if pieces:
        drawn = drawn * level_of(rng, shape, pieces, -0.22, 0.18)
    return jnp.clip(drawn, -bound, bound).astype(kind)


def setup_inputs(seed: int = 0, part: int = 0) -> dict:
    keys = jax.random.split(jax.random.key(seed), 9)
    part_keys = jax.random.split(jax.random.fold_in(keys[8], part), 9)
    embeddings = scatter_about(part_keys[0], (E, NTOT), E ** -0.5, 0.4375, ((1, 16),))
    local_scale = jnp.clip(jnp.exp(math.log(2.0) - 1.0509388 * jax.random.uniform(part_keys[1], (NTOT,), jnp.float32) ** level_of(part_keys[1], (NTOT,), ((0, 16),), -0.2, 0.2)), 0.69921875, 2.0).astype(jnp.bfloat16)
    degree_scale = jnp.clip(jnp.exp(math.log(2.0) - 1.3862944 * jax.random.uniform(part_keys[2], (NTOT,), jnp.float32) ** level_of(part_keys[2], (NTOT,), ((0, 16),), -0.2, 0.2)), 0.5, 2.0)
    lanczos_block = draw_lanczos_block(jax.random.fold_in(jax.random.fold_in(keys[8], part), 71), part)
    previous_block = scatter_about(part_keys[4], (LANCZOS, NTOT), 1.0, 6.0, ((1, 16),), jnp.float32)
    previous_coupling = scatter_about(part_keys[5], (LANCZOS, LANCZOS), LANCZOS ** -0.5, 1.5, (), jnp.float32)
    tile_plan = draw_tile_plan(jax.random.fold_in(jax.random.fold_in(keys[8], part), 71), part)
    tile_counts = draw_tile_counts(jax.random.fold_in(jax.random.fold_in(keys[8], part), 71), part)
    return dict(embeddings=embeddings, local_scale=local_scale, degree_scale=degree_scale, lanczos_block=lanczos_block, previous_block=previous_block, previous_coupling=previous_coupling, tile_plan=tile_plan, tile_counts=tile_counts)


def affinity(left_x, left_width, right_x, right_width):
    inner_prod = lax.dot_general(left_x, right_x, (((0,), (0,)), ((), ())), preferred_element_type=jnp.float32)
    left_norm = lax.optimization_barrier(jnp.sum(jnp.square(left_x.astype(jnp.float32)), axis=0))
    right_norm = lax.optimization_barrier(jnp.sum(jnp.square(right_x.astype(jnp.float32)), axis=0))
    distance = left_norm[:, None] + right_norm[None, :] - 2.0 * inner_prod
    spread = left_width.astype(jnp.float32)[:, None] * right_width.astype(jnp.float32)[None, :]
    return jnp.exp(-distance / spread).astype(jnp.bfloat16)

def build_mask(tile_plan, tile_counts, block_total):
    capacity = tile_plan.shape[0] // tile_counts.shape[0]
    positions = jnp.arange(tile_plan.shape[0], dtype=jnp.int32) % capacity
    is_live = (positions < jnp.repeat(tile_counts, capacity)).astype(jnp.float32)
    block_ids = jnp.arange(block_total, dtype=jnp.int32)
    row_onehot = (tile_plan[:, 0:1] == block_ids[None, :]).astype(jnp.float32) * is_live[:, None]
    col_onehot = (tile_plan[:, 1:2] == block_ids[None, :]).astype(jnp.float32)
    upper_tri = jnp.dot(row_onehot.T, col_onehot, precision=lax.Precision.HIGHEST)
    return jnp.maximum(upper_tri, upper_tri.T)

def reference(embeddings, local_scale, degree_scale, lanczos_block, previous_block, previous_coupling, tile_plan, tile_counts):
    block_total = NTOT // BLK
    pair_mask = build_mask(tile_plan, tile_counts, block_total)
    weighted = (degree_scale[None, :] * lanczos_block).astype(jnp.bfloat16)

    def one_block(block_index):
        begin_at = block_index * BLK
        rows_x = lax.dynamic_slice_in_dim(embeddings, begin_at, BLK, 1)
        rows_width = lax.dynamic_slice_in_dim(local_scale, begin_at, BLK, 0)
        weights = affinity(rows_x, rows_width, embeddings, local_scale)
        kept_mask = jnp.repeat(pair_mask[block_index], BLK).astype(jnp.bfloat16)
        masked = weighted * kept_mask[None, :]
        return lax.dot_general(masked, weights, (((1,), (1,)), ((), ())), preferred_element_type=jnp.float32)
    blocks_out = lax.map(one_block, jnp.arange(block_total, dtype=jnp.int32))
    summed = jnp.transpose(blocks_out, (1, 0, 2)).reshape(LANCZOS, NTOT)
    scaled = summed * (degree_scale[None, :] / math.sqrt(NTOT))
    partial_value = lax.dot_general(lanczos_block, scaled, (((1,), (1,)), ((), ())), precision=lax.Precision.HIGHEST)
    coupling = partial_value / NTOT
    projected = lax.dot_general(coupling, lanczos_block, (((0,), (0,)), ((), ())), precision=lax.Precision.HIGHEST)
    result = scaled - projected - jnp.dot(previous_coupling, previous_block, precision=lax.Precision.HIGHEST)
    return (result, coupling)
```

```python
import math

import jax
import jax.numpy as jnp
from jax import lax
from jax.experimental import pallas as pl
from jax.experimental.pallas import tpu as pltpu
from jax.sharding import PartitionSpec as P

LANCZOS = 16
BLK = 1024


HIGHEST = lax.Precision.HIGHEST


def affinity_kernel(mask_ref, xo_ref, no_ref, ro_ref, xc_ref, nc_ref, rc_ref, wc_ref, out_ref):
    c = pl.program_id(0)

    @pl.when(c == 0)
    def _():
        out_ref[...] = jnp.zeros_like(out_ref)

    @pl.when(mask_ref[c] != 0)
    def _():
        inner = jnp.dot(xo_ref[...], xc_ref[...], preferred_element_type=jnp.float32)
        distance = (no_ref[...] + nc_ref[...]) - 2.0 * inner
        weights = jnp.exp(-distance * (ro_ref[...] * rc_ref[...])).astype(jnp.bfloat16)
        out_ref[...] += lax.dot_general(
            wc_ref[...], weights, (((1,), (1,)), ((), ())), preferred_element_type=jnp.float32
        )


def own_rows_product(mask_row, x_own, norm_own, recip_own, gathered, norm_all, recip_all, width):
    own = x_own.shape[1]
    total = gathered.shape[1]
    lanes_row = width // LANCZOS
    grid_spec = pltpu.PrefetchScalarGridSpec(
        num_scalar_prefetch=1,
        grid=(total // BLK,),
        in_specs=[
            pl.BlockSpec((own, width), lambda c, m: (0, 0)),
            pl.BlockSpec((own, 1), lambda c, m: (0, 0)),
            pl.BlockSpec((own, 1), lambda c, m: (0, 0)),
            pl.BlockSpec((width, BLK), lambda c, m: (0, c)),
            pl.BlockSpec((1, BLK), lambda c, m: (0, c)),
            pl.BlockSpec((1, BLK), lambda c, m: (0, c)),
            pl.BlockSpec((LANCZOS, BLK), lambda c, m: (lanes_row, c)),
        ],
        out_specs=pl.BlockSpec((LANCZOS, own), lambda c, m: (0, 0)),
    )
    return pl.pallas_call(
        affinity_kernel,
        grid_spec=grid_spec,
        out_shape=jax.ShapeDtypeStruct((LANCZOS, own), jnp.float32),
    )(mask_row, x_own.T, norm_own, recip_own, gathered, norm_all, recip_all, gathered)


def shards(
    embeddings,
    local_scale,
    degree_scale,
    lanczos_block,
    previous_block,
    previous_coupling,
    tile_plan,
    tile_counts,
):
    width, own = embeddings.shape
    devices = lax.axis_size("row")
    total_rows = devices * own
    slots = tile_plan.shape[0]
    weighted = (degree_scale[None, :] * lanczos_block).astype(jnp.bfloat16)
    plan_row = jnp.concatenate([tile_plan.reshape(-1), tile_counts]).astype(jnp.bfloat16)
    plan_row = jnp.pad(plan_row, (0, own - plan_row.shape[0]))
    packed = jnp.concatenate(
        [embeddings, weighted, local_scale[None, :], plan_row[None, :]], axis=0
    )
    gathered = lax.all_gather(packed, "row", axis=1, tiled=True)

    plans = gathered[width + LANCZOS + 1].reshape(devices, own)[:, : 2 * slots + 1]
    plans = plans.astype(jnp.int32)
    counts = plans[:, 2 * slots]
    pairs = plans[:, : 2 * slots].reshape(devices, slots, 2)
    live = jnp.arange(slots, dtype=jnp.int32)[None, :] < counts[:, None]
    row_block = pairs[..., 0].reshape(-1)
    col_block = pairs[..., 1].reshape(-1)
    live = live.reshape(-1)
    my_block = (lax.axis_index("row") * own) // BLK
    block_ids = jnp.arange(total_rows // BLK, dtype=jnp.int32)
    hit = live[:, None] & (
        ((row_block[:, None] == my_block) & (col_block[:, None] == block_ids[None, :]))
        | ((col_block[:, None] == my_block) & (row_block[:, None] == block_ids[None, :]))
    )
    mask_row = jnp.any(hit, axis=0).astype(jnp.int32)

    x_all = gathered[:width]
    norm_all = jnp.sum(jnp.square(x_all.astype(jnp.float32)), axis=0)[None, :]
    recip_all = (1.0 / gathered[width + LANCZOS].astype(jnp.float32))[None, :]
    norm_own = jnp.sum(jnp.square(embeddings.astype(jnp.float32)), axis=0)[:, None]
    recip_own = (1.0 / local_scale.astype(jnp.float32))[:, None]

    summed = own_rows_product(
        mask_row, embeddings, norm_own, recip_own, gathered, norm_all, recip_all, width
    )
    scaled = summed * (degree_scale[None, :] / math.sqrt(total_rows))
    partial_value = lax.dot_general(
        lanczos_block, scaled, (((1,), (1,)), ((), ())), precision=HIGHEST
    )
    coupling = lax.psum(partial_value, "row") / total_rows
    projected = lax.dot_general(
        coupling, lanczos_block, (((0,), (0,)), ((), ())), precision=HIGHEST
    )
    result = scaled - projected - jnp.dot(previous_coupling, previous_block, precision=HIGHEST)
    return (result, coupling)


def solution(mesh):
    in_specs = (
        P(None, ("cohort", "row")),
        P(("cohort", "row")),
        P(("cohort", "row")),
        P(None, ("cohort", "row")),
        P(None, ("cohort", "row")),
        P("cohort", None),
        P(("cohort", "row"), None),
        P(("cohort", "row")),
    )
    out_specs = (P(None, ("cohort", "row")), P("cohort", None))
    return jax.shard_map(shards, mesh=mesh, in_specs=in_specs, out_specs=out_specs, check_vma=False)
```

```python
import math

import jax
import jax.numpy as jnp
from jax import lax
from jax.experimental import pallas as pl
from jax.experimental.pallas import tpu as pltpu
from jax.sharding import PartitionSpec as P

LANCZOS = 16
BLK = 1024


HIGHEST = lax.Precision.HIGHEST


def affinity_kernel(mask_ref, xo_ref, no_ref, ro_ref, xc_ref, nc_ref, rc_ref, wc_ref, out_ref):
    c = pl.program_id(0)

    @pl.when(c == 0)
    def _():
        out_ref[...] = jnp.zeros_like(out_ref)

    @pl.when(mask_ref[c] != 0)
    def _():
        inner = jnp.dot(xo_ref[...], xc_ref[...], preferred_element_type=jnp.float32)
        distance = (no_ref[...] + nc_ref[...]) - 2.0 * inner
        weights = jnp.exp(-distance * (ro_ref[...] * rc_ref[...])).astype(jnp.bfloat16)
        out_ref[...] += lax.dot_general(
            wc_ref[...], weights, (((1,), (1,)), ((), ())), preferred_element_type=jnp.float32
        )


def own_rows_product(mask_row, x_own, norm_own, recip_own, gathered, norm_all, recip_all, width):
    own = x_own.shape[1]
    total = gathered.shape[1]
    lanes_row = width // LANCZOS
    grid_spec = pltpu.PrefetchScalarGridSpec(
        num_scalar_prefetch=1,
        grid=(total // BLK,),
        in_specs=[
            pl.BlockSpec((own, width), lambda c, m: (0, 0)),
            pl.BlockSpec((own, 1), lambda c, m: (0, 0)),
            pl.BlockSpec((own, 1), lambda c, m: (0, 0)),
            pl.BlockSpec((width, BLK), lambda c, m: (0, c)),
            pl.BlockSpec((1, BLK), lambda c, m: (0, c)),
            pl.BlockSpec((1, BLK), lambda c, m: (0, c)),
            pl.BlockSpec((LANCZOS, BLK), lambda c, m: (lanes_row, c)),
        ],
        out_specs=pl.BlockSpec((LANCZOS, own), lambda c, m: (0, 0)),
    )
    return pl.pallas_call(
        affinity_kernel,
        grid_spec=grid_spec,
        out_shape=jax.ShapeDtypeStruct((LANCZOS, own), jnp.float32),
    )(mask_row, x_own.T, norm_own, recip_own, gathered, norm_all, recip_all, gathered)


def sum_over_rows(value):
    devices = lax.axis_size("row")
    if devices & (devices - 1):
        return lax.psum(value, "row")
    stride = 1
    while stride < devices:
        value = value + lax.ppermute(value, "row", [(i, i ^ stride) for i in range(devices)])
        stride *= 2
    return value


def shards(
    embeddings,
    local_scale,
    degree_scale,
    lanczos_block,
    previous_block,
    previous_coupling,
    tile_plan,
    tile_counts,
):
    width, own = embeddings.shape
    devices = lax.axis_size("row")
    total_rows = devices * own
    slots = tile_plan.shape[0]
    weighted = (degree_scale[None, :] * lanczos_block).astype(jnp.bfloat16)
    plan_row = jnp.concatenate([tile_plan.reshape(-1), tile_counts]).astype(jnp.bfloat16)
    plan_row = jnp.pad(plan_row, (0, own - plan_row.shape[0]))
    packed = jnp.concatenate(
        [embeddings, weighted, local_scale[None, :], plan_row[None, :]], axis=0
    )
    gathered = lax.all_gather(packed, "row", axis=1, tiled=True)

    plans = gathered[width + LANCZOS + 1].reshape(devices, own)[:, : 2 * slots + 1]
    plans = plans.astype(jnp.int32)
    counts = plans[:, 2 * slots]
    pairs = plans[:, : 2 * slots].reshape(devices, slots, 2)
    live = jnp.arange(slots, dtype=jnp.int32)[None, :] < counts[:, None]
    row_block = pairs[..., 0].reshape(-1)
    col_block = pairs[..., 1].reshape(-1)
    live = live.reshape(-1)
    my_block = (lax.axis_index("row") * own) // BLK
    block_ids = jnp.arange(total_rows // BLK, dtype=jnp.int32)
    hit = live[:, None] & (
        ((row_block[:, None] == my_block) & (col_block[:, None] == block_ids[None, :]))
        | ((col_block[:, None] == my_block) & (row_block[:, None] == block_ids[None, :]))
    )
    mask_row = jnp.any(hit, axis=0).astype(jnp.int32)

    x_all = gathered[:width]
    norm_all = jnp.sum(jnp.square(x_all.astype(jnp.float32)), axis=0)[None, :]
    recip_all = (1.0 / gathered[width + LANCZOS].astype(jnp.float32))[None, :]
    norm_own = jnp.sum(jnp.square(embeddings.astype(jnp.float32)), axis=0)[:, None]
    recip_own = (1.0 / local_scale.astype(jnp.float32))[:, None]

    summed = own_rows_product(
        mask_row, embeddings, norm_own, recip_own, gathered, norm_all, recip_all, width
    )
    scaled = summed * (degree_scale[None, :] / math.sqrt(total_rows))
    partial_value = lax.dot_general(
        lanczos_block, scaled, (((1,), (1,)), ((), ())), precision=HIGHEST
    )
    coupling = sum_over_rows(partial_value) / total_rows
    projected = lax.dot_general(
        coupling, lanczos_block, (((0,), (0,)), ((), ())), precision=HIGHEST
    )
    result = scaled - projected - jnp.dot(previous_coupling, previous_block, precision=HIGHEST)
    return (result, coupling)


def solution(mesh):
    in_specs = (
        P(None, ("cohort", "row")),
        P(("cohort", "row")),
        P(("cohort", "row")),
        P(None, ("cohort", "row")),
        P(None, ("cohort", "row")),
        P("cohort", None),
        P(("cohort", "row"), None),
        P(("cohort", "row")),
    )
    out_specs = (P(None, ("cohort", "row")), P("cohort", None))
    return jax.shard_map(shards, mesh=mesh, in_specs=in_specs, out_specs=out_specs, check_vma=False)
```

```python
import math

import jax
import jax.numpy as jnp
from jax import lax
from jax.experimental import pallas as pl
from jax.experimental.pallas import tpu as pltpu
from jax.sharding import PartitionSpec as P

LANCZOS = 16
BLK = 1024


HIGHEST = lax.Precision.HIGHEST


def affinity_kernel(flag_ref, xo_ref, no_ref, ro_ref, xc_ref, nc_ref, rc_ref, wc_ref, out_ref):
    s = pl.program_id(0)

    @pl.when(s == 0)
    def _():
        out_ref[...] = jnp.zeros_like(out_ref)

    @pl.when(flag_ref[s] != 0)
    def _():
        inner = jnp.dot(xo_ref[...], xc_ref[0], preferred_element_type=jnp.float32)
        distance = (no_ref[...] + nc_ref[0]) - 2.0 * inner
        weights = jnp.exp(-distance * (ro_ref[...] * rc_ref[0])).astype(jnp.bfloat16)
        out_ref[...] += lax.dot_general(
            wc_ref[0], weights, (((1,), (1,)), ((), ())), preferred_element_type=jnp.float32
        )


def own_rows_product(flags, x_own, norm_own, recip_own, pieces, norm_all, recip_all, width):
    own = x_own.shape[1]
    slots = pieces.shape[0]
    lanes_row = width // LANCZOS
    grid_spec = pltpu.PrefetchScalarGridSpec(
        num_scalar_prefetch=1,
        grid=(slots,),
        in_specs=[
            pl.BlockSpec((own, width), lambda s, m: (0, 0)),
            pl.BlockSpec((own, 1), lambda s, m: (0, 0)),
            pl.BlockSpec((own, 1), lambda s, m: (0, 0)),
            pl.BlockSpec((1, width, own), lambda s, m: (s, 0, 0)),
            pl.BlockSpec((1, 1, own), lambda s, m: (s, 0, 0)),
            pl.BlockSpec((1, 1, own), lambda s, m: (s, 0, 0)),
            pl.BlockSpec((1, LANCZOS, own), lambda s, m: (s, lanes_row, 0)),
        ],
        out_specs=pl.BlockSpec((LANCZOS, own), lambda s, m: (0, 0)),
    )
    return pl.pallas_call(
        affinity_kernel,
        grid_spec=grid_spec,
        out_shape=jax.ShapeDtypeStruct((LANCZOS, own), jnp.float32),
    )(flags, x_own.T, norm_own, recip_own, pieces, norm_all, recip_all, pieces)


def gather_pieces(packed):
    devices = lax.axis_size("row")
    me = lax.axis_index("row")
    if devices != 16:
        pieces = lax.all_gather(packed, "row", axis=0, tiled=False)
        return pieces, jnp.arange(devices, dtype=jnp.int32)
    up = [(r, r + 4) for r in range(12)]
    down = [(r, r - 4) for r in range(4, 16)]
    across = [(r, r ^ 2) for r in range(16)]
    twin = [(r, r ^ 1) for r in range(16)]
    z = me // 4
    partner = me ^ 2

    up1 = lax.ppermute(packed, "row", up)
    down1 = lax.ppermute(packed, "row", down)
    across1 = lax.ppermute(packed, "row", across)
    up2 = lax.ppermute(up1, "row", up)
    down2 = lax.ppermute(down1, "row", down)
    across2 = lax.ppermute(jnp.stack([up1, down1]), "row", across)
    pick2 = jnp.where(z >= 2, up2, down2)
    up3 = lax.ppermute(up2, "row", up)
    down3 = lax.ppermute(down2, "row", down)
    across3 = lax.ppermute(pick2, "row", across)
    pick3 = jnp.where(z == 3, up3, down3)
    across4 = lax.ppermute(pick3, "row", across)

    ends = (z == 0) | (z == 3)
    line1 = jnp.where(z >= 1, up1, down1)
    line2 = jnp.where(z >= 2, up2, jnp.where(z == 1, down1, down2))
    line3 = jnp.where(z == 3, up3, jnp.where(z == 2, down1, jnp.where(z == 1, down2, down3)))
    other2 = jnp.where(z >= 1, across2[0], across2[1])
    other3 = jnp.where(ends, across4, across2[1])
    mine = jnp.stack([packed, line1, line2, line3, across1, across3, other2, other3])
    origin = jnp.stack([
        me,
        jnp.where(z >= 1, me - 4, me + 4),
        jnp.where(z >= 2, me - 8, jnp.where(z == 1, me + 4, me + 8)),
        jnp.where(z == 3, me - 12, jnp.where(z == 2, me + 4, jnp.where(z == 1, me + 8, me + 12))),
        partner,
        jnp.where(z >= 2, partner - 8, partner + 8),
        jnp.where(z >= 1, partner - 4, partner + 4),
        jnp.where(z == 3, partner - 12, jnp.where(z == 0, partner + 12, partner + 4)),
    ]).astype(jnp.int32)
    theirs = lax.ppermute(mine, "row", twin)
    return jnp.concatenate([mine, theirs]), jnp.concatenate([origin, origin ^ 1])


def sum_over_rows(value):
    devices = lax.axis_size("row")
    if devices & (devices - 1):
        return lax.psum(value, "row")
    stride = 1
    while stride < devices:
        value = value + lax.ppermute(value, "row", [(i, i ^ stride) for i in range(devices)])
        stride *= 2
    return value


def shards(
    embeddings,
    local_scale,
    degree_scale,
    lanczos_block,
    previous_block,
    previous_coupling,
    tile_plan,
    tile_counts,
):
    width, own = embeddings.shape
    devices = lax.axis_size("row")
    total_rows = devices * own
    slots = tile_plan.shape[0]
    weighted = (degree_scale[None, :] * lanczos_block).astype(jnp.bfloat16)
    plan_row = jnp.concatenate([tile_plan.reshape(-1), tile_counts]).astype(jnp.bfloat16)
    plan_row = jnp.pad(plan_row, (0, own - plan_row.shape[0]))
    packed = jnp.concatenate(
        [embeddings, weighted, local_scale[None, :], plan_row[None, :]], axis=0
    )
    pieces, origin = gather_pieces(packed)

    plans = pieces[:, width + LANCZOS + 1, : 2 * slots + 1].astype(jnp.int32)
    counts = plans[:, 2 * slots]
    pairs = plans[:, : 2 * slots].reshape(devices, slots, 2)
    live = jnp.arange(slots, dtype=jnp.int32)[None, :] < counts[:, None]
    row_block = pairs[..., 0].reshape(-1)
    col_block = pairs[..., 1].reshape(-1)
    live = live.reshape(-1)
    my_block = (lax.axis_index("row") * own) // BLK
    block_ids = jnp.arange(total_rows // BLK, dtype=jnp.int32)
    hit = live[:, None] & (
        ((row_block[:, None] == my_block) & (col_block[:, None] == block_ids[None, :]))
        | ((col_block[:, None] == my_block) & (row_block[:, None] == block_ids[None, :]))
    )
    mask_row = jnp.any(hit, axis=0).astype(jnp.int32)
    flags = mask_row[(origin * own) // BLK]

    norm_all = jnp.sum(jnp.square(pieces[:, :width].astype(jnp.float32)), axis=1)[:, None, :]
    recip_all = (1.0 / pieces[:, width + LANCZOS].astype(jnp.float32))[:, None, :]
    norm_own = jnp.sum(jnp.square(embeddings.astype(jnp.float32)), axis=0)[:, None]
    recip_own = (1.0 / local_scale.astype(jnp.float32))[:, None]

    summed = own_rows_product(
        flags, embeddings, norm_own, recip_own, pieces, norm_all, recip_all, width
    )
    scaled = summed * (degree_scale[None, :] / math.sqrt(total_rows))
    partial_value = lax.dot_general(
        lanczos_block, scaled, (((1,), (1,)), ((), ())), precision=HIGHEST
    )
    coupling = sum_over_rows(partial_value) / total_rows
    projected = lax.dot_general(
        coupling, lanczos_block, (((0,), (0,)), ((), ())), precision=HIGHEST
    )
    result = scaled - projected - jnp.dot(previous_coupling, previous_block, precision=HIGHEST)
    return (result, coupling)


def solution(mesh):
    in_specs = (
        P(None, ("cohort", "row")),
        P(("cohort", "row")),
        P(("cohort", "row")),
        P(None, ("cohort", "row")),
        P(None, ("cohort", "row")),
        P("cohort", None),
        P(("cohort", "row"), None),
        P(("cohort", "row")),
    )
    out_specs = (P(None, ("cohort", "row")), P("cohort", None))
    return jax.shard_map(shards, mesh=mesh, in_specs=in_specs, out_specs=out_specs, check_vma=False)
```

```python
import functools
import math

import jax
import jax.numpy as jnp
from jax import lax
from jax.experimental import pallas as pl
from jax.experimental.pallas import tpu as pltpu
from jax.sharding import PartitionSpec as P

LANCZOS = 16
BLK = 1024


HIGHEST = lax.Precision.HIGHEST


def piece_kernel(width, rows, shapes, sel_ref, xo_ref, no_ref, ro_ref, *refs):
    out_ref = refs[-1]
    views = []
    for ref, shape in zip(refs[:-1], shapes):
        views += [ref.at[i * rows : (i + 1) * rows, :] for i in range(shape[0] // rows)]
    for slot, piece in enumerate(views):

        @pl.when(sel_ref[slot] != 0)
        def _():
            x_cols = piece[:width, :]
            x_wide = x_cols.astype(jnp.float32)
            norm_cols = jnp.sum(x_wide * x_wide, axis=0, keepdims=True)
            recip_cols = 1.0 / piece[width + LANCZOS : width + LANCZOS + 1, :].astype(jnp.float32)
            inner = jnp.dot(xo_ref[...], x_cols, preferred_element_type=jnp.float32)
            distance = (no_ref[...] + norm_cols) - 2.0 * inner
            weights = jnp.exp(-distance * (ro_ref[...] * recip_cols)).astype(jnp.bfloat16)
            out_ref[slot] = lax.dot_general(
                piece[width : width + LANCZOS, :],
                weights,
                (((1,), (1,)), ((), ())),
                preferred_element_type=jnp.float32,
            )

        @pl.when(sel_ref[slot] == 0)
        def _():
            out_ref[slot] = jnp.zeros(out_ref.shape[1:], jnp.float32)


def piece_products(sel, own_terms, pieces, width, rows):
    x_own_t, norm_own, recip_own = own_terms
    own = x_own_t.shape[0]
    shapes = [p.shape for p in pieces]
    slots = sum(sh[0] // rows for sh in shapes)
    vmem = pl.BlockSpec(memory_space=pltpu.VMEM)
    return pl.pallas_call(
        functools.partial(piece_kernel, width, rows, shapes),
        in_specs=[pl.BlockSpec(memory_space=pltpu.SMEM)] + [vmem] * (3 + len(pieces)),
        out_specs=vmem,
        out_shape=jax.ShapeDtypeStruct((slots, LANCZOS, own), jnp.float32),
    )(sel.astype(jnp.int32), x_own_t, norm_own, recip_own, *pieces)


def gather_products(packed, own_terms, width):
    devices = lax.axis_size("row")
    me = lax.axis_index("row")
    rows = packed.shape[0]
    if devices != 16:
        pieces = lax.all_gather(packed, "row", axis=0, tiled=True)
        sel = jnp.ones((devices,), jnp.int32)
        parts = piece_products(sel, own_terms, [pieces], width, rows)
        return [parts], [jnp.arange(devices, dtype=jnp.int32)], [sel], [pieces]
    up = [(r, r + 4) for r in range(12)]
    down = [(r, r - 4) for r in range(4, 16)]
    across = [(r, r ^ 2) for r in range(16)]
    twin = [(r, r ^ 1) for r in range(16)]
    z = me // 4
    partner = me ^ 2
    ends = (z == 0) | (z == 3)
    one = jnp.ones((), bool)

    def run(pieces, sel, origin):
        sel = jnp.stack(sel).astype(jnp.int32)
        return piece_products(sel, own_terms, pieces, width, rows), jnp.stack(origin).astype(jnp.int32), sel

    results = [run([packed], [one], [me])]
    up1 = lax.ppermute(packed, "row", up)
    down1 = lax.ppermute(packed, "row", down)
    across1 = lax.ppermute(packed, "row", across)
    results.append(run([up1, down1, across1], [z >= 1, z <= 2, one], [me - 4, me + 4, partner]))
    up2 = lax.ppermute(up1, "row", up)
    down2 = lax.ppermute(down1, "row", down)
    across2 = lax.ppermute(jnp.concatenate([up1, down1]), "row", across)
    results.append(run(
        [up2, down2, across2],
        [z >= 2, z <= 1, z >= 1, z <= 2],
        [me - 8, me + 8, partner - 4, partner + 4],
    ))
    pick2 = jnp.where(z >= 2, up2, down2)
    up3 = lax.ppermute(up2, "row", up)
    down3 = lax.ppermute(down2, "row", down)
    across3 = lax.ppermute(pick2, "row", across)
    results.append(run(
        [up3, down3, across3],
        [z == 3, z == 0, one],
        [me - 12, me + 12, jnp.where(z >= 2, partner - 8, partner + 8)],
    ))
    pick3 = jnp.where(z == 3, up3, down3)
    across4 = lax.ppermute(pick3, "row", across)
    results.append(run([across4], [ends], [jnp.where(z == 3, partner - 12, partner + 12)]))

    line1 = jnp.where(z >= 1, up1, down1)
    line2 = jnp.where(z >= 2, up2, jnp.where(z == 1, down1, down2))
    line3 = jnp.where(z == 3, up3, jnp.where(z == 2, down1, jnp.where(z == 1, down2, down3)))
    other2 = jnp.where(z >= 1, across2[:rows], across2[rows:])
    other3 = jnp.where(ends, across4, across2[rows:])
    mine = jnp.concatenate([packed, line1, line2, line3, across1, across3, other2, other3])
    origin = jnp.stack([
        me,
        jnp.where(z >= 1, me - 4, me + 4),
        jnp.where(z >= 2, me - 8, jnp.where(z == 1, me + 4, me + 8)),
        jnp.where(z == 3, me - 12, jnp.where(z == 2, me + 4, jnp.where(z == 1, me + 8, me + 12))),
        partner,
        jnp.where(z >= 2, partner - 8, partner + 8),
        jnp.where(z >= 1, partner - 4, partner + 4),
        jnp.where(z == 3, partner - 12, jnp.where(z == 0, partner + 12, partner + 4)),
    ]).astype(jnp.int32)
    theirs = lax.ppermute(mine, "row", twin)
    results.append(run([theirs], [one] * 8, list(origin ^ 1)))
    parts, origins, sels = zip(*results)
    return list(parts), list(origins), list(sels), [mine, theirs]


def sum_over_rows(value):
    devices = lax.axis_size("row")
    if devices & (devices - 1):
        return lax.psum(value, "row")
    stride = 1
    while stride < devices:
        value = value + lax.ppermute(value, "row", [(i, i ^ stride) for i in range(devices)])
        stride *= 2
    return value


def shards(
    embeddings,
    local_scale,
    degree_scale,
    lanczos_block,
    previous_block,
    previous_coupling,
    tile_plan,
    tile_counts,
):
    width, own = embeddings.shape
    devices = lax.axis_size("row")
    total_rows = devices * own
    slots = tile_plan.shape[0]
    weighted = (degree_scale[None, :] * lanczos_block).astype(jnp.bfloat16)
    plan_row = jnp.concatenate([tile_plan.reshape(-1), tile_counts]).astype(jnp.bfloat16)
    plan_row = jnp.pad(plan_row, (0, own - plan_row.shape[0]))
    packed = jnp.concatenate(
        [embeddings, weighted, local_scale[None, :], plan_row[None, :]], axis=0
    )
    packed = jnp.pad(packed, ((0, -packed.shape[0] % 16), (0, 0)))
    x_own_t = embeddings.T
    norm_own = jnp.sum(jnp.square(embeddings.astype(jnp.float32)), axis=0)[:, None]
    recip_own = (1.0 / local_scale.astype(jnp.float32))[:, None]
    parts, origins, sels, pieces = gather_products(packed, (x_own_t, norm_own, recip_own), width)

    plans = jnp.concatenate(
        [p.reshape(-1, packed.shape[0], own)[:, width + LANCZOS + 1, : 2 * slots + 1] for p in pieces]
    ).astype(jnp.int32)
    counts = plans[:, 2 * slots]
    pairs = plans[:, : 2 * slots].reshape(devices, slots, 2)
    live = jnp.arange(slots, dtype=jnp.int32)[None, :] < counts[:, None]
    row_block = pairs[..., 0].reshape(-1)
    col_block = pairs[..., 1].reshape(-1)
    live = live.reshape(-1)
    my_block = (lax.axis_index("row") * own) // BLK
    block_ids = jnp.arange(total_rows // BLK, dtype=jnp.int32)
    hit = live[:, None] & (
        ((row_block[:, None] == my_block) & (col_block[:, None] == block_ids[None, :]))
        | ((col_block[:, None] == my_block) & (row_block[:, None] == block_ids[None, :]))
    )
    mask_row = jnp.any(hit, axis=0)

    summed = jnp.zeros((LANCZOS, own), jnp.float32)
    for part, origin, sel in zip(parts, origins, sels):
        source = jnp.clip(origin, 0, devices - 1)
        keep = (sel != 0) & mask_row[(source * own) // BLK]
        summed = summed + jnp.sum(jnp.where(keep[:, None, None], part, 0.0), axis=0)
    scaled = summed * (degree_scale[None, :] / math.sqrt(total_rows))
    partial_value = lax.dot_general(
        lanczos_block, scaled, (((1,), (1,)), ((), ())), precision=HIGHEST
    )
    coupling = sum_over_rows(partial_value) / total_rows
    projected = lax.dot_general(
        coupling, lanczos_block, (((0,), (0,)), ((), ())), precision=HIGHEST
    )
    result = scaled - projected - jnp.dot(previous_coupling, previous_block, precision=HIGHEST)
    return (result, coupling)


def solution(mesh):
    in_specs = (
        P(None, ("cohort", "row")),
        P(("cohort", "row")),
        P(("cohort", "row")),
        P(None, ("cohort", "row")),
        P(None, ("cohort", "row")),
        P("cohort", None),
        P(("cohort", "row"), None),
        P(("cohort", "row")),
    )
    out_specs = (P(None, ("cohort", "row")), P("cohort", None))
    return jax.shard_map(shards, mesh=mesh, in_specs=in_specs, out_specs=out_specs, check_vma=False)
```

```python
import functools
import math

import jax
import jax.numpy as jnp
from jax import lax
from jax.experimental import pallas as pl
from jax.experimental.pallas import tpu as pltpu
from jax.sharding import PartitionSpec as P

LANCZOS = 16
BLK = 1024


HIGHEST = lax.Precision.HIGHEST


def affinity_kernel(
    width, flag_ref, xo_ref, no_ref, ro_ref, xa_ref, wa_ref, xb_ref, wb_ref, out_ref
):
    s = pl.program_id(0)
    halves = pl.num_programs(0)

    @pl.when(s == 0)
    def _():
        out_ref[...] = jnp.zeros_like(out_ref)

    for slot, x_ref, w_ref in ((s, xa_ref, wa_ref), (s + halves, xb_ref, wb_ref)):

        @pl.when(flag_ref[slot] != 0)
        def _():
            x_cols = x_ref[0, :width, :]
            x_wide = x_cols.astype(jnp.float32)
            norm_cols = jnp.sum(x_wide * x_wide, axis=0, keepdims=True)
            recip_cols = 1.0 / w_ref[0, LANCZOS : LANCZOS + 1, :].astype(jnp.float32)
            twice_inner = jnp.dot(xo_ref[...], x_cols, preferred_element_type=jnp.float32)
            distance = (no_ref[...] + norm_cols) - twice_inner
            weights = jnp.exp2(distance * (ro_ref[...] * recip_cols)).astype(jnp.bfloat16)
            out_ref[...] += lax.dot_general(
                w_ref[0, :LANCZOS, :], weights, (((1,), (1,)), ((), ())),
                preferred_element_type=jnp.float32,
            )


def own_rows_product(flags, x_own, norm_own, recip_own, mine, theirs, width):
    own = x_own.shape[1]
    rows = mine.shape[1]
    half = mine.shape[0]
    lanes_row = width // LANCZOS
    x_spec = pl.BlockSpec((1, rows, own), lambda s, m: (s, 0, 0))
    w_spec = pl.BlockSpec((1, 2 * LANCZOS, own), lambda s, m: (s, lanes_row // 2, 0))
    grid_spec = pltpu.PrefetchScalarGridSpec(
        num_scalar_prefetch=1,
        grid=(half,),
        in_specs=[
            pl.BlockSpec((own, width), lambda s, m: (0, 0)),
            pl.BlockSpec((own, 1), lambda s, m: (0, 0)),
            pl.BlockSpec((own, 1), lambda s, m: (0, 0)),
            x_spec, w_spec, x_spec, w_spec,
        ],
        out_specs=pl.BlockSpec((LANCZOS, own), lambda s, m: (0, 0)),
    )
    twice_own_t = (x_own * 2).T
    log2e = 1.0 / math.log(2.0)
    return pl.pallas_call(
        functools.partial(affinity_kernel, width),
        grid_spec=grid_spec,
        out_shape=jax.ShapeDtypeStruct((LANCZOS, own), jnp.float32),
    )(flags, twice_own_t, norm_own, recip_own * -log2e, mine, mine, theirs, theirs)


def gather_pieces(packed):
    devices = lax.axis_size("row")
    me = lax.axis_index("row")
    if devices != 16:
        pieces = lax.all_gather(packed, "row", axis=0, tiled=False)
        return pieces[: devices // 2], pieces[devices // 2 :], jnp.arange(devices, dtype=jnp.int32)
    up = [(r, r + 4) for r in range(12)]
    down = [(r, r - 4) for r in range(4, 16)]
    across = [(r, r ^ 2) for r in range(16)]
    twin = [(r, r ^ 1) for r in range(16)]
    z = me // 4
    partner = me ^ 2

    up1 = lax.ppermute(packed, "row", up)
    down1 = lax.ppermute(packed, "row", down)
    across1 = lax.ppermute(packed, "row", across)
    up2 = lax.ppermute(up1, "row", up)
    down2 = lax.ppermute(down1, "row", down)
    across2 = lax.ppermute(jnp.stack([up1, down1]), "row", across)
    pick2 = jnp.where(z >= 2, up2, down2)
    up3 = lax.ppermute(up2, "row", up)
    down3 = lax.ppermute(down2, "row", down)
    across3 = lax.ppermute(pick2, "row", across)
    pick3 = jnp.where(z == 3, up3, down3)
    across4 = lax.ppermute(pick3, "row", across)

    ends = (z == 0) | (z == 3)
    line1 = jnp.where(z >= 1, up1, down1)
    line2 = jnp.where(z >= 2, up2, jnp.where(z == 1, down1, down2))
    line3 = jnp.where(z == 3, up3, jnp.where(z == 2, down1, jnp.where(z == 1, down2, down3)))
    other2 = jnp.where(z >= 1, across2[0], across2[1])
    other3 = jnp.where(ends, across4, across2[1])
    mine = jnp.stack([packed, line1, line2, line3, across1, across3, other2, other3])
    origin = jnp.stack([
        me,
        jnp.where(z >= 1, me - 4, me + 4),
        jnp.where(z >= 2, me - 8, jnp.where(z == 1, me + 4, me + 8)),
        jnp.where(z == 3, me - 12, jnp.where(z == 2, me + 4, jnp.where(z == 1, me + 8, me + 12))),
        partner,
        jnp.where(z >= 2, partner - 8, partner + 8),
        jnp.where(z >= 1, partner - 4, partner + 4),
        jnp.where(z == 3, partner - 12, jnp.where(z == 0, partner + 12, partner + 4)),
    ]).astype(jnp.int32)
    theirs = lax.ppermute(mine, "row", twin)
    return mine, theirs, jnp.concatenate([origin, origin ^ 1])


def sum_over_rows(value):
    devices = lax.axis_size("row")
    if devices & (devices - 1):
        return lax.psum(value, "row")
    stride = 1
    while stride < devices:
        value = value + lax.ppermute(value, "row", [(i, i ^ stride) for i in range(devices)])
        stride *= 2
    return value


def shards(
    embeddings,
    local_scale,
    degree_scale,
    lanczos_block,
    previous_block,
    previous_coupling,
    tile_plan,
    tile_counts,
):
    width, own = embeddings.shape
    devices = lax.axis_size("row")
    total_rows = devices * own
    slots = tile_plan.shape[0]
    weighted = (degree_scale[None, :] * lanczos_block).astype(jnp.bfloat16)
    plan_row = jnp.concatenate([tile_plan.reshape(-1), tile_counts]).astype(jnp.bfloat16)
    plan_row = jnp.pad(plan_row, (0, own - plan_row.shape[0]))
    packed = jnp.concatenate(
        [embeddings, weighted, local_scale[None, :], plan_row[None, :]], axis=0
    )
    packed = jnp.pad(packed, ((0, -packed.shape[0] % (2 * LANCZOS)), (0, 0)))
    mine, theirs, origin = gather_pieces(packed)

    plans = jnp.concatenate([mine, theirs])[:, width + LANCZOS + 1, : 2 * slots + 1]
    plans = plans.astype(jnp.int32)
    counts = plans[:, 2 * slots]
    pairs = plans[:, : 2 * slots].reshape(devices, slots, 2)
    live = jnp.arange(slots, dtype=jnp.int32)[None, :] < counts[:, None]
    row_block = pairs[..., 0].reshape(-1)
    col_block = pairs[..., 1].reshape(-1)
    live = live.reshape(-1)
    my_block = (lax.axis_index("row") * own) // BLK
    block_ids = jnp.arange(total_rows // BLK, dtype=jnp.int32)
    hit = live[:, None] & (
        ((row_block[:, None] == my_block) & (col_block[:, None] == block_ids[None, :]))
        | ((col_block[:, None] == my_block) & (row_block[:, None] == block_ids[None, :]))
    )
    mask_row = jnp.any(hit, axis=0).astype(jnp.int32)
    flags = mask_row[(origin * own) // BLK]

    norm_own = jnp.sum(jnp.square(embeddings.astype(jnp.float32)), axis=0)[:, None]
    recip_own = (1.0 / local_scale.astype(jnp.float32))[:, None]

    summed = own_rows_product(flags, embeddings, norm_own, recip_own, mine, theirs, width)
    scaled = summed * (degree_scale[None, :] / math.sqrt(total_rows))
    partial_value = lax.dot_general(
        lanczos_block, scaled, (((1,), (1,)), ((), ())), precision=HIGHEST
    )
    coupling = sum_over_rows(partial_value) / total_rows
    projected = lax.dot_general(
        coupling, lanczos_block, (((0,), (0,)), ((), ())), precision=HIGHEST
    )
    result = scaled - projected - jnp.dot(previous_coupling, previous_block, precision=HIGHEST)
    return (result, coupling)


def solution(mesh):
    in_specs = (
        P(None, ("cohort", "row")),
        P(("cohort", "row")),
        P(("cohort", "row")),
        P(None, ("cohort", "row")),
        P(None, ("cohort", "row")),
        P("cohort", None),
        P(("cohort", "row"), None),
        P(("cohort", "row")),
    )
    out_specs = (P(None, ("cohort", "row")), P("cohort", None))
    return jax.shard_map(shards, mesh=mesh, in_specs=in_specs, out_specs=out_specs, check_vma=False)
```

```python
import functools
import math

import jax
import jax.numpy as jnp
from jax import lax
from jax.experimental import pallas as pl
from jax.experimental.pallas import tpu as pltpu
from jax.sharding import PartitionSpec as P

LANCZOS = 16
BLK = 1024


HIGHEST = lax.Precision.HIGHEST


def affinity_kernel(width, flag_ref, xo_ref, no_ref, ro_ref, x_ref, w_ref, out_ref):
    s = pl.program_id(0)

    @pl.when(s == 0)
    def _():
        out_ref[...] = jnp.zeros_like(out_ref)

    @pl.when(flag_ref[s] != 0)
    def _():
        x_cols = x_ref[0, :width, :]
        x_wide = x_cols.astype(jnp.float32)
        norm_cols = jnp.sum(x_wide * x_wide, axis=0, keepdims=True)
        recip_cols = 1.0 / w_ref[0, LANCZOS : LANCZOS + 1, :].astype(jnp.float32)
        twice_inner = jnp.dot(xo_ref[...], x_cols, preferred_element_type=jnp.float32)
        distance = (no_ref[...] + norm_cols) - twice_inner
        weights = jnp.exp2(distance * (ro_ref[...] * recip_cols)).astype(jnp.bfloat16)
        out_ref[...] += lax.dot_general(
            w_ref[0, :LANCZOS, :], weights, (((1,), (1,)), ((), ())),
            preferred_element_type=jnp.float32,
        )


def own_rows_product(flags, own_terms, mine, width):
    twice_own_t, norm_own, recip_own = own_terms
    own = twice_own_t.shape[0]
    rows = mine.shape[1]
    half = mine.shape[0]
    lanes_row = width // LANCZOS
    x_spec = pl.BlockSpec((1, rows, own), lambda s, m: (s, 0, 0))
    w_spec = pl.BlockSpec((1, 2 * LANCZOS, own), lambda s, m: (s, lanes_row // 2, 0))
    grid_spec = pltpu.PrefetchScalarGridSpec(
        num_scalar_prefetch=1,
        grid=(half,),
        in_specs=[
            pl.BlockSpec((own, width), lambda s, m: (0, 0)),
            pl.BlockSpec((own, 1), lambda s, m: (0, 0)),
            pl.BlockSpec((own, 1), lambda s, m: (0, 0)),
            x_spec, w_spec,
        ],
        out_specs=pl.BlockSpec((LANCZOS, own), lambda s, m: (0, 0)),
    )
    return pl.pallas_call(
        functools.partial(affinity_kernel, width),
        grid_spec=grid_spec,
        out_shape=jax.ShapeDtypeStruct((LANCZOS, own), jnp.float32),
    )(flags, twice_own_t, norm_own, recip_own, mine, mine)


def gather_pieces(packed):
    devices = lax.axis_size("row")
    me = lax.axis_index("row")
    if devices != 16:
        pieces = lax.all_gather(packed, "row", axis=0, tiled=False)
        return pieces, None, jnp.arange(devices, dtype=jnp.int32), None
    up = [(r, r + 4) for r in range(12)]
    down = [(r, r - 4) for r in range(4, 16)]
    across = [(r, r ^ 2) for r in range(16)]
    twin = [(r, r ^ 1) for r in range(16)]
    z = me // 4
    partner = me ^ 2

    up1 = lax.ppermute(packed, "row", up)
    down1 = lax.ppermute(packed, "row", down)
    across1 = lax.ppermute(packed, "row", across)
    up2 = lax.ppermute(up1, "row", up)
    down2 = lax.ppermute(down1, "row", down)
    across2 = lax.ppermute(jnp.stack([up1, down1]), "row", across)
    pick2 = jnp.where(z >= 2, up2, down2)
    up3 = lax.ppermute(up2, "row", up)
    down3 = lax.ppermute(down2, "row", down)
    across3 = lax.ppermute(pick2, "row", across)
    pick3 = jnp.where(z == 3, up3, down3)
    across4 = lax.ppermute(pick3, "row", across)

    ends = (z == 0) | (z == 3)
    line1 = jnp.where(z >= 1, up1, down1)
    line2 = jnp.where(z >= 2, up2, jnp.where(z == 1, down1, down2))
    line3 = jnp.where(z == 3, up3, jnp.where(z == 2, down1, jnp.where(z == 1, down2, down3)))
    other2 = jnp.where(z >= 1, across2[0], across2[1])
    other3 = jnp.where(ends, across4, across2[1])
    mine = jnp.stack([packed, line1, line2, line3, across1, across3, other2, other3])
    origin = jnp.stack([
        me,
        jnp.where(z >= 1, me - 4, me + 4),
        jnp.where(z >= 2, me - 8, jnp.where(z == 1, me + 4, me + 8)),
        jnp.where(z == 3, me - 12, jnp.where(z == 2, me + 4, jnp.where(z == 1, me + 8, me + 12))),
        partner,
        jnp.where(z >= 2, partner - 8, partner + 8),
        jnp.where(z >= 1, partner - 4, partner + 4),
        jnp.where(z == 3, partner - 12, jnp.where(z == 0, partner + 12, partner + 4)),
    ]).astype(jnp.int32)
    theirs = lax.ppermute(mine, "row", twin)
    return mine, theirs, origin, origin ^ 1


def sum_over_rows(value):
    devices = lax.axis_size("row")
    if devices & (devices - 1):
        return lax.psum(value, "row")
    stride = 1
    while stride < devices:
        value = value + lax.ppermute(value, "row", [(i, i ^ stride) for i in range(devices)])
        stride *= 2
    return value


def shards(
    embeddings,
    local_scale,
    degree_scale,
    lanczos_block,
    previous_block,
    previous_coupling,
    tile_plan,
    tile_counts,
):
    width, own = embeddings.shape
    devices = lax.axis_size("row")
    total_rows = devices * own
    slots = tile_plan.shape[0]
    weighted = (degree_scale[None, :] * lanczos_block).astype(jnp.bfloat16)
    plan_row = jnp.concatenate([tile_plan.reshape(-1), tile_counts]).astype(jnp.bfloat16)
    plan_row = jnp.pad(plan_row, (0, own - plan_row.shape[0]))
    packed = jnp.concatenate(
        [embeddings, weighted, local_scale[None, :], plan_row[None, :]], axis=0
    )
    packed = jnp.pad(packed, ((0, -packed.shape[0] % (2 * LANCZOS)), (0, 0)))
    mine, theirs, origin, their_origin = gather_pieces(packed)

    plan_at = width + LANCZOS + 1
    plans = mine[:, plan_at, : 2 * slots + 1]
    if theirs is not None:
        twin = [(r, r ^ 1) for r in range(devices)]
        plans = jnp.concatenate([plans, lax.ppermute(plans, "row", twin)])
    plans = plans.astype(jnp.int32)
    counts = plans[:, 2 * slots]
    pairs = plans[:, : 2 * slots].reshape(devices, slots, 2)
    live = jnp.arange(slots, dtype=jnp.int32)[None, :] < counts[:, None]
    row_block = pairs[..., 0].reshape(-1)
    col_block = pairs[..., 1].reshape(-1)
    live = live.reshape(-1)
    my_block = (lax.axis_index("row") * own) // BLK
    block_ids = jnp.arange(total_rows // BLK, dtype=jnp.int32)
    hit = live[:, None] & (
        ((row_block[:, None] == my_block) & (col_block[:, None] == block_ids[None, :]))
        | ((col_block[:, None] == my_block) & (row_block[:, None] == block_ids[None, :]))
    )
    mask_row = jnp.any(hit, axis=0).astype(jnp.int32)

    norm_own = jnp.sum(jnp.square(embeddings.astype(jnp.float32)), axis=0)[:, None]
    log2e = 1.0 / math.log(2.0)
    recip_own = (-log2e / local_scale.astype(jnp.float32))[:, None]
    own_terms = ((embeddings * 2).T, norm_own, recip_own)
    summed = own_rows_product(mask_row[(origin * own) // BLK], own_terms, mine, width)
    if theirs is not None:
        summed = summed + own_rows_product(
            mask_row[(their_origin * own) // BLK], own_terms, theirs, width
        )
    scaled = summed * (degree_scale[None, :] / math.sqrt(total_rows))
    partial_value = lax.dot_general(
        lanczos_block, scaled, (((1,), (1,)), ((), ())), precision=HIGHEST
    )
    coupling = sum_over_rows(partial_value) / total_rows
    projected = lax.dot_general(
        coupling, lanczos_block, (((0,), (0,)), ((), ())), precision=HIGHEST
    )
    result = scaled - projected - jnp.dot(previous_coupling, previous_block, precision=HIGHEST)
    return (result, coupling)


def solution(mesh):
    in_specs = (
        P(None, ("cohort", "row")),
        P(("cohort", "row")),
        P(("cohort", "row")),
        P(None, ("cohort", "row")),
        P(None, ("cohort", "row")),
        P("cohort", None),
        P(("cohort", "row"), None),
        P(("cohort", "row")),
    )
    out_specs = (P(None, ("cohort", "row")), P("cohort", None))
    return jax.shard_map(shards, mesh=mesh, in_specs=in_specs, out_specs=out_specs, check_vma=False)
```

```python
import functools
import math

import jax
import jax.numpy as jnp
from jax import lax
from jax.experimental import pallas as pl
from jax.experimental.pallas import tpu as pltpu
from jax.sharding import PartitionSpec as P

LANCZOS = 16
BLK = 1024


HIGHEST = lax.Precision.HIGHEST


def affinity_kernel(width, per, flag_ref, xo_ref, no_ref, ro_ref, x_ref, w_ref, out_ref):
    s = pl.program_id(0)

    @pl.when(s == 0)
    def _():
        out_ref[...] = jnp.zeros_like(out_ref)

    for k in range(per):

        @pl.when(flag_ref[s * per + k] != 0)
        def _():
            x_cols = x_ref[k, :width, :]
            x_wide = x_cols.astype(jnp.float32)
            norm_cols = jnp.sum(x_wide * x_wide, axis=0, keepdims=True)
            recip_cols = 1.0 / w_ref[k, LANCZOS : LANCZOS + 1, :].astype(jnp.float32)
            twice_inner = jnp.dot(xo_ref[...], x_cols, preferred_element_type=jnp.float32)
            distance = (no_ref[...] + norm_cols) - twice_inner
            weights = jnp.exp2(distance * (ro_ref[...] * recip_cols)).astype(jnp.bfloat16)
            out_ref[...] += lax.dot_general(
                w_ref[k, :LANCZOS, :], weights, (((1,), (1,)), ((), ())),
                preferred_element_type=jnp.float32,
            )


def own_rows_product(flags, own_terms, mine, width):
    twice_own_t, norm_own, recip_own = own_terms
    own = twice_own_t.shape[0]
    slots, rows = mine.shape[0], mine.shape[1]
    per = 2 if slots % 2 == 0 else 1
    lanes_row = width // LANCZOS
    x_spec = pl.BlockSpec((per, rows, own), lambda s, m: (s, 0, 0))
    w_spec = pl.BlockSpec((per, 2 * LANCZOS, own), lambda s, m: (s, lanes_row // 2, 0))
    grid_spec = pltpu.PrefetchScalarGridSpec(
        num_scalar_prefetch=1,
        grid=(slots // per,),
        in_specs=[
            pl.BlockSpec((own, width), lambda s, m: (0, 0)),
            pl.BlockSpec((own, 1), lambda s, m: (0, 0)),
            pl.BlockSpec((own, 1), lambda s, m: (0, 0)),
            x_spec, w_spec,
        ],
        out_specs=pl.BlockSpec((LANCZOS, own), lambda s, m: (0, 0)),
    )
    return pl.pallas_call(
        functools.partial(affinity_kernel, width, per),
        grid_spec=grid_spec,
        out_shape=jax.ShapeDtypeStruct((LANCZOS, own), jnp.float32),
    )(flags, twice_own_t, norm_own, recip_own, mine, mine)


def gather_pieces(packed):
    devices = lax.axis_size("row")
    me = lax.axis_index("row")
    if devices != 16:
        pieces = lax.all_gather(packed, "row", axis=0, tiled=False)
        return pieces, None, jnp.arange(devices, dtype=jnp.int32), None
    up = [(r, r + 4) for r in range(12)]
    down = [(r, r - 4) for r in range(4, 16)]
    across = [(r, r ^ 2) for r in range(16)]
    twin = [(r, r ^ 1) for r in range(16)]
    z = me // 4
    partner = me ^ 2

    up1 = lax.ppermute(packed, "row", up)
    down1 = lax.ppermute(packed, "row", down)
    across1 = lax.ppermute(packed, "row", across)
    up2 = lax.ppermute(up1, "row", up)
    down2 = lax.ppermute(down1, "row", down)
    across2 = lax.ppermute(jnp.stack([up1, down1]), "row", across)
    pick2 = jnp.where(z >= 2, up2, down2)
    up3 = lax.ppermute(up2, "row", up)
    down3 = lax.ppermute(down2, "row", down)
    across3 = lax.ppermute(pick2, "row", across)
    pick3 = jnp.where(z == 3, up3, down3)
    across4 = lax.ppermute(pick3, "row", across)

    ends = (z == 0) | (z == 3)
    line1 = jnp.where(z >= 1, up1, down1)
    line2 = jnp.where(z >= 2, up2, jnp.where(z == 1, down1, down2))
    line3 = jnp.where(z == 3, up3, jnp.where(z == 2, down1, jnp.where(z == 1, down2, down3)))
    other2 = jnp.where(z >= 1, across2[0], across2[1])
    other3 = jnp.where(ends, across4, across2[1])
    mine = jnp.stack([packed, line1, line2, line3, across1, across3, other2, other3])
    origin = jnp.stack([
        me,
        jnp.where(z >= 1, me - 4, me + 4),
        jnp.where(z >= 2, me - 8, jnp.where(z == 1, me + 4, me + 8)),
        jnp.where(z == 3, me - 12, jnp.where(z == 2, me + 4, jnp.where(z == 1, me + 8, me + 12))),
        partner,
        jnp.where(z >= 2, partner - 8, partner + 8),
        jnp.where(z >= 1, partner - 4, partner + 4),
        jnp.where(z == 3, partner - 12, jnp.where(z == 0, partner + 12, partner + 4)),
    ]).astype(jnp.int32)
    theirs = lax.ppermute(mine, "row", twin)
    return mine, theirs, origin, origin ^ 1


def sum_over_rows(value):
    devices = lax.axis_size("row")
    if devices & (devices - 1):
        return lax.psum(value, "row")
    stride = 1
    while stride < devices:
        value = value + lax.ppermute(value, "row", [(i, i ^ stride) for i in range(devices)])
        stride *= 2
    return value


def shards(
    embeddings,
    local_scale,
    degree_scale,
    lanczos_block,
    previous_block,
    previous_coupling,
    tile_plan,
    tile_counts,
):
    width, own = embeddings.shape
    devices = lax.axis_size("row")
    total_rows = devices * own
    slots = tile_plan.shape[0]
    weighted = (degree_scale[None, :] * lanczos_block).astype(jnp.bfloat16)
    plan_row = jnp.concatenate([tile_plan.reshape(-1), tile_counts]).astype(jnp.bfloat16)
    plan_row = jnp.pad(plan_row, (0, own - plan_row.shape[0]))
    packed = jnp.concatenate(
        [embeddings, weighted, local_scale[None, :], plan_row[None, :]], axis=0
    )
    packed = jnp.pad(packed, ((0, -packed.shape[0] % (2 * LANCZOS)), (0, 0)))
    mine, theirs, origin, their_origin = gather_pieces(packed)

    plan_at = width + LANCZOS + 1
    plans = mine[:, plan_at, : 2 * slots + 1]
    if theirs is not None:
        twin = [(r, r ^ 1) for r in range(devices)]
        plans = jnp.concatenate([plans, lax.ppermute(plans, "row", twin)])
    plans = plans.astype(jnp.int32)
    counts = plans[:, 2 * slots]
    pairs = plans[:, : 2 * slots].reshape(devices, slots, 2)
    live = jnp.arange(slots, dtype=jnp.int32)[None, :] < counts[:, None]
    row_block = pairs[..., 0].reshape(-1)
    col_block = pairs[..., 1].reshape(-1)
    live = live.reshape(-1)
    my_block = (lax.axis_index("row") * own) // BLK
    block_ids = jnp.arange(total_rows // BLK, dtype=jnp.int32)
    hit = live[:, None] & (
        ((row_block[:, None] == my_block) & (col_block[:, None] == block_ids[None, :]))
        | ((col_block[:, None] == my_block) & (row_block[:, None] == block_ids[None, :]))
    )
    mask_row = jnp.any(hit, axis=0).astype(jnp.int32)

    norm_own = jnp.sum(jnp.square(embeddings.astype(jnp.float32)), axis=0)[:, None]
    log2e = 1.0 / math.log(2.0)
    recip_own = (-log2e / local_scale.astype(jnp.float32))[:, None]
    own_terms = ((embeddings * 2).T, norm_own, recip_own)
    summed = own_rows_product(mask_row[(origin * own) // BLK], own_terms, mine, width)
    if theirs is not None:
        summed = summed + own_rows_product(
            mask_row[(their_origin * own) // BLK], own_terms, theirs, width
        )
    scaled = summed * (degree_scale[None, :] / math.sqrt(total_rows))
    partial_value = lax.dot_general(
        lanczos_block, scaled, (((1,), (1,)), ((), ())), precision=HIGHEST
    )
    coupling = sum_over_rows(partial_value) / total_rows
    projected = lax.dot_general(
        coupling, lanczos_block, (((0,), (0,)), ((), ())), precision=HIGHEST
    )
    result = scaled - projected - jnp.dot(previous_coupling, previous_block, precision=HIGHEST)
    return (result, coupling)


def solution(mesh):
    in_specs = (
        P(None, ("cohort", "row")),
        P(("cohort", "row")),
        P(("cohort", "row")),
        P(None, ("cohort", "row")),
        P(None, ("cohort", "row")),
        P("cohort", None),
        P(("cohort", "row"), None),
        P(("cohort", "row")),
    )
    out_specs = (P(None, ("cohort", "row")), P("cohort", None))
    return jax.shard_map(shards, mesh=mesh, in_specs=in_specs, out_specs=out_specs, check_vma=False)
```

```python
import functools
import math

import jax
import jax.numpy as jnp
from jax import lax
from jax.experimental import pallas as pl
from jax.experimental.pallas import tpu as pltpu
from jax.sharding import PartitionSpec as P

LANCZOS = 16
BLK = 1024


HIGHEST = lax.Precision.HIGHEST


def affinity_kernel(width, per, flag_ref, xo_ref, no_ref, ro_ref, x_ref, w_ref, out_ref):
    s = pl.program_id(0)

    @pl.when(s == 0)
    def _():
        out_ref[...] = jnp.zeros_like(out_ref)

    for k in range(per):

        @pl.when(flag_ref[s * per + k] != 0)
        def _():
            x_cols = x_ref[k, :width, :]
            x_wide = x_cols.astype(jnp.float32)
            norm_cols = jnp.sum(x_wide * x_wide, axis=0, keepdims=True)
            recip_cols = 1.0 / w_ref[k, LANCZOS : LANCZOS + 1, :].astype(jnp.float32)
            twice_inner = jnp.dot(xo_ref[...], x_cols, preferred_element_type=jnp.float32)
            distance = (no_ref[...] + norm_cols) - twice_inner
            weights = jnp.exp2(distance * (ro_ref[...] * recip_cols)).astype(jnp.bfloat16)
            out_ref[...] += lax.dot_general(
                w_ref[k, :LANCZOS, :], weights, (((1,), (1,)), ((), ())),
                preferred_element_type=jnp.float32,
            )


def own_rows_product(flags, own_terms, mine, width):
    twice_own_t, norm_own, recip_own = own_terms
    own = twice_own_t.shape[0]
    slots, rows, cols = mine.shape
    per = 2 if slots % 2 == 0 else 1
    lanes_row = width // LANCZOS
    x_spec = pl.BlockSpec((per, rows, cols), lambda s, m: (s, 0, 0))
    w_spec = pl.BlockSpec((per, 2 * LANCZOS, cols), lambda s, m: (s, lanes_row // 2, 0))
    grid_spec = pltpu.PrefetchScalarGridSpec(
        num_scalar_prefetch=1,
        grid=(slots // per,),
        in_specs=[
            pl.BlockSpec((own, width), lambda s, m: (0, 0)),
            pl.BlockSpec((own, 1), lambda s, m: (0, 0)),
            pl.BlockSpec((own, 1), lambda s, m: (0, 0)),
            x_spec, w_spec,
        ],
        out_specs=pl.BlockSpec((LANCZOS, own), lambda s, m: (0, 0)),
    )
    return pl.pallas_call(
        functools.partial(affinity_kernel, width, per),
        grid_spec=grid_spec,
        out_shape=jax.ShapeDtypeStruct((LANCZOS, own), jnp.float32),
    )(flags, twice_own_t, norm_own, recip_own, mine, mine)


def gather_pieces(packed):
    devices = lax.axis_size("row")
    me = lax.axis_index("row")
    if devices != 16:
        pieces = lax.all_gather(packed, "row", axis=0, tiled=False)
        return pieces, jnp.arange(devices, dtype=jnp.int32)
    up = [(r, r + 4) for r in range(12)]
    down = [(r, r - 4) for r in range(4, 16)]
    across = [(r, r ^ 2) for r in range(16)]
    z = me // 4
    partner = me ^ 2

    up1 = lax.ppermute(packed, "row", up)
    down1 = lax.ppermute(packed, "row", down)
    across1 = lax.ppermute(packed, "row", across)
    up2 = lax.ppermute(up1, "row", up)
    down2 = lax.ppermute(down1, "row", down)
    across2 = lax.ppermute(jnp.stack([up1, down1]), "row", across)
    pick2 = jnp.where(z >= 2, up2, down2)
    up3 = lax.ppermute(up2, "row", up)
    down3 = lax.ppermute(down2, "row", down)
    across3 = lax.ppermute(pick2, "row", across)
    pick3 = jnp.where(z == 3, up3, down3)
    across4 = lax.ppermute(pick3, "row", across)

    ends = (z == 0) | (z == 3)
    line1 = jnp.where(z >= 1, up1, down1)
    line2 = jnp.where(z >= 2, up2, jnp.where(z == 1, down1, down2))
    line3 = jnp.where(z == 3, up3, jnp.where(z == 2, down1, jnp.where(z == 1, down2, down3)))
    other2 = jnp.where(z >= 1, across2[0], across2[1])
    other3 = jnp.where(ends, across4, across2[1])
    mine = jnp.stack([packed, line1, line2, line3, across1, across3, other2, other3])
    origin = jnp.stack([
        me,
        jnp.where(z >= 1, me - 4, me + 4),
        jnp.where(z >= 2, me - 8, jnp.where(z == 1, me + 4, me + 8)),
        jnp.where(z == 3, me - 12, jnp.where(z == 2, me + 4, jnp.where(z == 1, me + 8, me + 12))),
        partner,
        jnp.where(z >= 2, partner - 8, partner + 8),
        jnp.where(z >= 1, partner - 4, partner + 4),
        jnp.where(z == 3, partner - 12, jnp.where(z == 0, partner + 12, partner + 4)),
    ]).astype(jnp.int32)
    return mine, origin


def sum_over_rows(value):
    devices = lax.axis_size("row")
    if devices & (devices - 1):
        return lax.psum(value, "row")
    stride = 1
    while stride < devices:
        value = value + lax.ppermute(value, "row", [(i, i ^ stride) for i in range(devices)])
        stride *= 2
    return value


def shards(
    embeddings,
    local_scale,
    degree_scale,
    lanczos_block,
    previous_block,
    previous_coupling,
    tile_plan,
    tile_counts,
):
    width, own = embeddings.shape
    devices = lax.axis_size("row")
    total_rows = devices * own
    slots = tile_plan.shape[0]
    chip_split = devices == 16
    twin = [(r, r ^ 1) for r in range(devices)]
    weighted = (degree_scale[None, :] * lanczos_block).astype(jnp.bfloat16)
    plan_len = 2 * slots + 1
    plan_row = jnp.concatenate([tile_plan.reshape(-1), tile_counts]).astype(jnp.bfloat16)
    if chip_split:
        plan_row = jnp.concatenate([plan_row, lax.ppermute(plan_row, "row", twin)])
    plan_row = jnp.pad(plan_row, (0, own - plan_row.shape[0]))
    packed = jnp.concatenate(
        [embeddings, weighted, local_scale[None, :], plan_row[None, :]], axis=0
    )
    packed = jnp.pad(packed, ((0, -packed.shape[0] % (2 * LANCZOS)), (0, 0)))
    mine, origin = gather_pieces(packed)

    plan_at = width + LANCZOS + 1
    copies = 2 if chip_split else 1
    plans = mine[:, plan_at, : copies * plan_len].astype(jnp.int32).reshape(devices, plan_len)
    counts = plans[:, 2 * slots]
    pairs = plans[:, : 2 * slots].reshape(devices, slots, 2)
    live = jnp.arange(slots, dtype=jnp.int32)[None, :] < counts[:, None]
    row_block = pairs[..., 0].reshape(-1)[:, None]
    col_block = pairs[..., 1].reshape(-1)[:, None]
    live = live.reshape(-1)[:, None]
    my_block = (lax.axis_index("row") * own) // BLK
    piece_block = ((origin * own) // BLK)[None, :]
    hit = live & (
        ((row_block == my_block) & (col_block == piece_block))
        | ((col_block == my_block) & (row_block == piece_block))
    )
    flags = jnp.any(hit, axis=0).astype(jnp.int32)

    if chip_split:
        twin_piece = lax.ppermute(packed, "row", twin)
        rows_x = jnp.concatenate([embeddings, twin_piece[:width]], axis=1)
        rows_scale = jnp.concatenate([local_scale, twin_piece[width + LANCZOS]])
    else:
        rows_x, rows_scale = embeddings, local_scale
    norm_rows = jnp.sum(jnp.square(rows_x.astype(jnp.float32)), axis=0)[:, None]
    log2e = 1.0 / math.log(2.0)
    recip_rows = (-log2e / rows_scale.astype(jnp.float32))[:, None]
    own_terms = ((rows_x * 2).T, norm_rows, recip_rows)
    summed = own_rows_product(flags, own_terms, mine, width)
    if chip_split:
        summed = summed[:, :own] + lax.ppermute(summed[:, own:], "row", twin)
    scaled = summed * (degree_scale[None, :] / math.sqrt(total_rows))
    partial_value = lax.dot_general(
        lanczos_block, scaled, (((1,), (1,)), ((), ())), precision=HIGHEST
    )
    coupling = sum_over_rows(partial_value) / total_rows
    projected = lax.dot_general(
        coupling, lanczos_block, (((0,), (0,)), ((), ())), precision=HIGHEST
    )
    result = scaled - projected - jnp.dot(previous_coupling, previous_block, precision=HIGHEST)
    return (result, coupling)


def solution(mesh):
    in_specs = (
        P(None, ("cohort", "row")),
        P(("cohort", "row")),
        P(("cohort", "row")),
        P(None, ("cohort", "row")),
        P(None, ("cohort", "row")),
        P("cohort", None),
        P(("cohort", "row"), None),
        P(("cohort", "row")),
    )
    out_specs = (P(None, ("cohort", "row")), P("cohort", None))
    return jax.shard_map(shards, mesh=mesh, in_specs=in_specs, out_specs=out_specs, check_vma=False)
```

```python
import functools
import math

import jax
import jax.numpy as jnp
from jax import lax
from jax.experimental import pallas as pl
from jax.experimental.pallas import tpu as pltpu
from jax.sharding import PartitionSpec as P

LANCZOS = 16
BLK = 1024


HIGHEST = lax.Precision.HIGHEST


def affinity_kernel(width, per, flag_ref, xo_ref, no_ref, ro_ref, x_ref, w_ref, out_ref):
    s = pl.program_id(0)

    @pl.when(s == 0)
    def _():
        out_ref[...] = jnp.zeros_like(out_ref)

    for k in range(per):

        @pl.when(flag_ref[s * per + k] != 0)
        def _():
            x_cols = x_ref[k, :width, :]
            x_wide = x_cols.astype(jnp.float32)
            norm_cols = jnp.sum(x_wide * x_wide, axis=0, keepdims=True)
            recip_cols = 1.0 / w_ref[k, LANCZOS : LANCZOS + 1, :].astype(jnp.float32)
            twice_inner = jnp.dot(xo_ref[...], x_cols, preferred_element_type=jnp.float32)
            distance = (no_ref[...] + norm_cols) - twice_inner
            weights = jnp.exp2(distance * (ro_ref[...] * recip_cols)).astype(jnp.bfloat16)
            out_ref[...] += lax.dot_general(
                w_ref[k, :LANCZOS, :], weights, (((1,), (1,)), ((), ())),
                preferred_element_type=jnp.float32,
            )


def own_rows_product(flags, own_terms, mine, width):
    twice_own_t, norm_own, recip_own = own_terms
    own = twice_own_t.shape[0]
    slots, rows, cols = mine.shape
    per = 2 if slots % 2 == 0 else 1
    lanes_row = width // LANCZOS
    x_spec = pl.BlockSpec((per, rows, cols), lambda s, m: (s, 0, 0))
    w_spec = pl.BlockSpec((per, 2 * LANCZOS, cols), lambda s, m: (s, lanes_row // 2, 0))
    grid_spec = pltpu.PrefetchScalarGridSpec(
        num_scalar_prefetch=1,
        grid=(slots // per,),
        in_specs=[
            pl.BlockSpec((own, width), lambda s, m: (0, 0)),
            pl.BlockSpec((own, 1), lambda s, m: (0, 0)),
            pl.BlockSpec((own, 1), lambda s, m: (0, 0)),
            x_spec, w_spec,
        ],
        out_specs=pl.BlockSpec((LANCZOS, own), lambda s, m: (0, 0)),
    )
    return pl.pallas_call(
        functools.partial(affinity_kernel, width, per),
        grid_spec=grid_spec,
        out_shape=jax.ShapeDtypeStruct((LANCZOS, own), jnp.float32),
    )(flags, twice_own_t, norm_own, recip_own, mine, mine)


def gather_pieces(packed):
    devices = lax.axis_size("row")
    me = lax.axis_index("row")
    if devices != 16:
        pieces = lax.all_gather(packed, "row", axis=0, tiled=False)
        return pieces, jnp.arange(devices, dtype=jnp.int32)
    up = [(r, r + 4) for r in range(12)]
    down = [(r, r - 4) for r in range(4, 16)]
    across = [(r, r ^ 2) for r in range(16)]
    z = me // 4
    partner = me ^ 2

    up1 = lax.ppermute(packed, "row", up)
    down1 = lax.ppermute(packed, "row", down)
    across1 = lax.ppermute(packed, "row", across)
    up2 = lax.ppermute(up1, "row", up)
    down2 = lax.ppermute(down1, "row", down)
    across2 = lax.ppermute(jnp.stack([up1, down1]), "row", across)
    pick2 = jnp.where(z >= 2, up2, down2)
    up3 = lax.ppermute(up2, "row", up)
    down3 = lax.ppermute(down2, "row", down)
    across3 = lax.ppermute(pick2, "row", across)
    pick3 = jnp.where(z == 3, up3, down3)
    across4 = lax.ppermute(pick3, "row", across)

    ends = (z == 0) | (z == 3)
    line1 = jnp.where(z >= 1, up1, down1)
    line2 = jnp.where(z >= 2, up2, jnp.where(z == 1, down1, down2))
    line3 = jnp.where(z == 3, up3, jnp.where(z == 2, down1, jnp.where(z == 1, down2, down3)))
    other2 = jnp.where(z >= 1, across2[0], across2[1])
    other3 = jnp.where(ends, across4, across2[1])
    mine = jnp.stack([packed, line1, line2, line3, across1, across3, other2, other3])
    origin = jnp.stack([
        me,
        jnp.where(z >= 1, me - 4, me + 4),
        jnp.where(z >= 2, me - 8, jnp.where(z == 1, me + 4, me + 8)),
        jnp.where(z == 3, me - 12, jnp.where(z == 2, me + 4, jnp.where(z == 1, me + 8, me + 12))),
        partner,
        jnp.where(z >= 2, partner - 8, partner + 8),
        jnp.where(z >= 1, partner - 4, partner + 4),
        jnp.where(z == 3, partner - 12, jnp.where(z == 0, partner + 12, partner + 4)),
    ]).astype(jnp.int32)
    return mine, origin


def sum_over_rows(value):
    devices = lax.axis_size("row")
    if devices != 16:
        if devices & (devices - 1):
            return lax.psum(value, "row")
        stride = 1
        while stride < devices:
            value = value + lax.ppermute(value, "row", [(i, i ^ stride) for i in range(devices)])
            stride *= 2
        return value
    me = lax.axis_index("row")
    for shift in (0, 2):
        got = {0: value}
        for m in (1, 2, 3):
            got[m] = lax.ppermute(value, "row", [(i, i ^ (m << shift)) for i in range(devices)])
        place = (me >> shift) & 3
        total = None
        for k in range(4):
            member = got[0]
            for m in (1, 2, 3):
                member = jnp.where((k ^ place) == m, got[m], member)
            total = member if total is None else total + member
        value = total
    return value


def shards(
    embeddings,
    local_scale,
    degree_scale,
    lanczos_block,
    previous_block,
    previous_coupling,
    tile_plan,
    tile_counts,
):
    width, own = embeddings.shape
    devices = lax.axis_size("row")
    total_rows = devices * own
    slots = tile_plan.shape[0]
    chip_split = devices == 16
    twin = [(r, r ^ 1) for r in range(devices)]
    weighted = (degree_scale[None, :] * lanczos_block).astype(jnp.bfloat16)
    plan_len = 2 * slots + 1
    plan_row = jnp.concatenate([tile_plan.reshape(-1), tile_counts]).astype(jnp.bfloat16)
    if chip_split:
        plan_row = jnp.concatenate([plan_row, lax.ppermute(plan_row, "row", twin)])
    plan_row = jnp.pad(plan_row, (0, own - plan_row.shape[0]))
    packed = jnp.concatenate(
        [embeddings, weighted, local_scale[None, :], plan_row[None, :]], axis=0
    )
    packed = jnp.pad(packed, ((0, -packed.shape[0] % (2 * LANCZOS)), (0, 0)))
    mine, origin = gather_pieces(packed)

    plan_at = width + LANCZOS + 1
    copies = 2 if chip_split else 1
    plans = mine[:, plan_at, : copies * plan_len].astype(jnp.int32).reshape(devices, plan_len)
    counts = plans[:, 2 * slots]
    pairs = plans[:, : 2 * slots].reshape(devices, slots, 2)
    live = jnp.arange(slots, dtype=jnp.int32)[None, :] < counts[:, None]
    row_block = pairs[..., 0].reshape(-1)[:, None]
    col_block = pairs[..., 1].reshape(-1)[:, None]
    live = live.reshape(-1)[:, None]
    my_block = (lax.axis_index("row") * own) // BLK
    piece_block = ((origin * own) // BLK)[None, :]
    hit = live & (
        ((row_block == my_block) & (col_block == piece_block))
        | ((col_block == my_block) & (row_block == piece_block))
    )
    flags = jnp.any(hit, axis=0).astype(jnp.int32)

    if chip_split:
        twin_piece = lax.ppermute(packed, "row", twin)
        rows_x = jnp.concatenate([embeddings, twin_piece[:width]], axis=1)
        rows_scale = jnp.concatenate([local_scale, twin_piece[width + LANCZOS]])
    else:
        rows_x, rows_scale = embeddings, local_scale
    norm_rows = jnp.sum(jnp.square(rows_x.astype(jnp.float32)), axis=0)[:, None]
    log2e = 1.0 / math.log(2.0)
    recip_rows = (-log2e / rows_scale.astype(jnp.float32))[:, None]
    own_terms = ((rows_x * 2).T, norm_rows, recip_rows)
    summed = own_rows_product(flags, own_terms, mine, width)
    if chip_split:
        summed = summed[:, :own] + lax.ppermute(summed[:, own:], "row", twin)
    scaled = summed * (degree_scale[None, :] / math.sqrt(total_rows))
    partial_value = lax.dot_general(
        lanczos_block, scaled, (((1,), (1,)), ((), ())), precision=HIGHEST
    )
    coupling = sum_over_rows(partial_value) / total_rows
    projected = lax.dot_general(
        coupling, lanczos_block, (((0,), (0,)), ((), ())), precision=HIGHEST
    )
    result = scaled - projected - jnp.dot(previous_coupling, previous_block, precision=HIGHEST)
    return (result, coupling)


def solution(mesh):
    in_specs = (
        P(None, ("cohort", "row")),
        P(("cohort", "row")),
        P(("cohort", "row")),
        P(None, ("cohort", "row")),
        P(None, ("cohort", "row")),
        P("cohort", None),
        P(("cohort", "row"), None),
        P(("cohort", "row")),
    )
    out_specs = (P(None, ("cohort", "row")), P("cohort", None))
    return jax.shard_map(shards, mesh=mesh, in_specs=in_specs, out_specs=out_specs, check_vma=False)
```

```python
import functools
import math

import jax
import jax.numpy as jnp
from jax import lax
from jax.experimental import pallas as pl
from jax.experimental.pallas import tpu as pltpu
from jax.sharding import PartitionSpec as P

LANCZOS = 16
BLK = 1024


HIGHEST = lax.Precision.HIGHEST


def piece_terms(width, x_cols, w_cols, xo_ref, no_ref, ro_ref):
    x_wide = x_cols.astype(jnp.float32)
    norm_cols = jnp.sum(x_wide * x_wide, axis=0, keepdims=True)
    recip_cols = 1.0 / w_cols[LANCZOS : LANCZOS + 1, :].astype(jnp.float32)
    twice_inner = jnp.dot(xo_ref[...], x_cols, preferred_element_type=jnp.float32)
    distance = (no_ref[...] + norm_cols) - twice_inner
    weights = jnp.exp2(distance * (ro_ref[...] * recip_cols)).astype(jnp.bfloat16)
    return lax.dot_general(
        w_cols[:LANCZOS, :], weights, (((1,), (1,)), ((), ())),
        preferred_element_type=jnp.float32,
    )


def affinity_kernel(width, per, flag_ref, xo_ref, no_ref, ro_ref, x_ref, w_ref, out_ref):
    s = pl.program_id(0)

    @pl.when(s == 0)
    def _():
        out_ref[...] = jnp.zeros_like(out_ref)

    for k in range(per):

        @pl.when(flag_ref[s * per + k] != 0)
        def _():
            out_ref[...] += piece_terms(
                width, x_ref[k, :width, :], w_ref[k],
                xo_ref, no_ref, ro_ref,
            )


def list_kernel(width, rows, counts, flag_ref, xo_ref, no_ref, ro_ref, *refs):
    out_ref = refs[-1]
    out_ref[...] = jnp.zeros_like(out_ref)
    slot = 0
    for ref, count in zip(refs[:-1], counts):
        for k in range(count):

            @pl.when(flag_ref[slot] != 0)
            def _():
                base = k * rows
                out_ref[...] += piece_terms(
                    width,
                    ref[base : base + width, :],
                    ref[base + width : base + width + 2 * LANCZOS, :],
                    xo_ref, no_ref, ro_ref,
                )

            slot += 1


def list_product(flags, own_terms, pieces, width, rows):
    twice_own_t, norm_own, recip_own = own_terms
    own = twice_own_t.shape[0]
    counts = [p.shape[0] // rows for p in pieces]
    vmem = pl.BlockSpec(memory_space=pltpu.VMEM)
    return pl.pallas_call(
        functools.partial(list_kernel, width, rows, counts),
        in_specs=[pl.BlockSpec(memory_space=pltpu.SMEM)] + [vmem] * (3 + len(pieces)),
        out_specs=vmem,
        out_shape=jax.ShapeDtypeStruct((LANCZOS, own), jnp.float32),
    )(flags, twice_own_t, norm_own, recip_own, *pieces)


def own_rows_product(flags, own_terms, mine, width):
    twice_own_t, norm_own, recip_own = own_terms
    own = twice_own_t.shape[0]
    slots, rows, cols = mine.shape
    per = 2 if slots % 2 == 0 else 1
    lanes_row = width // LANCZOS
    x_spec = pl.BlockSpec((per, rows, cols), lambda s, m: (s, 0, 0))
    w_spec = pl.BlockSpec((per, 2 * LANCZOS, cols), lambda s, m: (s, lanes_row // 2, 0))
    grid_spec = pltpu.PrefetchScalarGridSpec(
        num_scalar_prefetch=1,
        grid=(slots // per,),
        in_specs=[
            pl.BlockSpec((own, width), lambda s, m: (0, 0)),
            pl.BlockSpec((own, 1), lambda s, m: (0, 0)),
            pl.BlockSpec((own, 1), lambda s, m: (0, 0)),
            x_spec, w_spec,
        ],
        out_specs=pl.BlockSpec((LANCZOS, own), lambda s, m: (0, 0)),
    )
    return pl.pallas_call(
        functools.partial(affinity_kernel, width, per),
        grid_spec=grid_spec,
        out_shape=jax.ShapeDtypeStruct((LANCZOS, own), jnp.float32),
    )(flags, twice_own_t, norm_own, recip_own, mine, mine)


def gather_pieces(packed):
    devices = lax.axis_size("row")
    me = lax.axis_index("row")
    if devices != 16:
        pieces = lax.all_gather(packed, "row", axis=0, tiled=False)
        return [pieces], None, jnp.arange(devices, dtype=jnp.int32)
    up = [(r, r + 4) for r in range(12)]
    down = [(r, r - 4) for r in range(4, 16)]
    across = [(r, r ^ 2) for r in range(16)]
    z = me // 4
    partner = me ^ 2

    up1 = lax.ppermute(packed, "row", up)
    down1 = lax.ppermute(packed, "row", down)
    across1 = lax.ppermute(packed, "row", across)
    up2 = lax.ppermute(up1, "row", up)
    down2 = lax.ppermute(down1, "row", down)
    across2 = lax.ppermute(jnp.concatenate([up1, down1]), "row", across)
    pick2 = jnp.where(z >= 2, up2, down2)
    up3 = lax.ppermute(up2, "row", up)
    down3 = lax.ppermute(down2, "row", down)
    across3 = lax.ppermute(pick2, "row", across)
    pick3 = jnp.where(z == 3, up3, down3)
    across4 = lax.ppermute(pick3, "row", across)

    ends = (z == 0) | (z == 3)
    one = jnp.ones((), bool)
    pieces = [packed, up1, down1, across1, up2, down2, across2, up3, down3, across3, across4]
    valid = [one, z >= 1, z <= 2, one, z >= 2, z <= 1, z >= 1, z <= 2, z == 3, z == 0, one, ends]
    origin = [
        me, me - 4, me + 4, partner, me - 8, me + 8, partner - 4, partner + 4, me - 12, me + 12,
        jnp.where(z >= 2, partner - 8, partner + 8), jnp.where(z == 3, partner - 12, partner + 12),
    ]
    return pieces, jnp.stack(valid), jnp.clip(jnp.stack(origin), 0, devices - 1).astype(jnp.int32)


def sum_over_rows(value):
    devices = lax.axis_size("row")
    if devices != 16:
        if devices & (devices - 1):
            return lax.psum(value, "row")
        stride = 1
        while stride < devices:
            value = value + lax.ppermute(value, "row", [(i, i ^ stride) for i in range(devices)])
            stride *= 2
        return value
    me = lax.axis_index("row")
    for shift in (0, 2):
        got = {0: value}
        for m in (1, 2, 3):
            got[m] = lax.ppermute(value, "row", [(i, i ^ (m << shift)) for i in range(devices)])
        place = (me >> shift) & 3
        total = None
        for k in range(4):
            member = got[0]
            for m in (1, 2, 3):
                member = jnp.where((k ^ place) == m, got[m], member)
            total = member if total is None else total + member
        value = total
    return value


def shards(
    embeddings,
    local_scale,
    degree_scale,
    lanczos_block,
    previous_block,
    previous_coupling,
    tile_plan,
    tile_counts,
):
    width, own = embeddings.shape
    devices = lax.axis_size("row")
    total_rows = devices * own
    slots = tile_plan.shape[0]
    chip_split = devices == 16
    twin = [(r, r ^ 1) for r in range(devices)]
    weighted = (degree_scale[None, :] * lanczos_block).astype(jnp.bfloat16)
    plan_len = 2 * slots + 1
    plan_row = jnp.concatenate([tile_plan.reshape(-1), tile_counts]).astype(jnp.bfloat16)
    if chip_split:
        plan_row = jnp.concatenate([plan_row, lax.ppermute(plan_row, "row", twin)])
    plan_row = jnp.pad(plan_row, (0, own - plan_row.shape[0]))
    packed = jnp.concatenate(
        [embeddings, weighted, local_scale[None, :], plan_row[None, :]], axis=0
    )
    packed = jnp.pad(packed, ((0, -packed.shape[0] % (2 * LANCZOS)), (0, 0)))
    pieces, valid, origin = gather_pieces(packed)
    rows = packed.shape[0]

    plan_at = width + LANCZOS + 1
    copies = 2 if chip_split else 1
    plans = jnp.concatenate([p.reshape(-1, rows, own)[:, plan_at, : copies * plan_len] for p in pieces])
    plans = plans.astype(jnp.int32).reshape(-1, plan_len)
    counts = plans[:, 2 * slots]
    pairs = plans[:, : 2 * slots].reshape(-1, slots, 2)
    live = jnp.arange(slots, dtype=jnp.int32)[None, :] < counts[:, None]
    row_block = pairs[..., 0].reshape(-1)[:, None]
    col_block = pairs[..., 1].reshape(-1)[:, None]
    live = live.reshape(-1)[:, None]
    my_block = (lax.axis_index("row") * own) // BLK
    piece_block = ((origin * own) // BLK)[None, :]
    hit = live & (
        ((row_block == my_block) & (col_block == piece_block))
        | ((col_block == my_block) & (row_block == piece_block))
    )
    flags = jnp.any(hit, axis=0)
    if valid is not None:
        flags = flags & valid
    flags = flags.astype(jnp.int32)

    if chip_split:
        twin_piece = lax.ppermute(packed, "row", twin)
        rows_x = jnp.concatenate([embeddings, twin_piece[:width]], axis=1)
        rows_scale = jnp.concatenate([local_scale, twin_piece[width + LANCZOS]])
    else:
        rows_x, rows_scale = embeddings, local_scale
    norm_rows = jnp.sum(jnp.square(rows_x.astype(jnp.float32)), axis=0)[:, None]
    log2e = 1.0 / math.log(2.0)
    recip_rows = (-log2e / rows_scale.astype(jnp.float32))[:, None]
    own_terms = ((rows_x * 2).T, norm_rows, recip_rows)
    if chip_split:
        summed = list_product(flags, own_terms, pieces, width, rows)
    else:
        summed = own_rows_product(flags, own_terms, pieces[0].reshape(devices, rows, own), width)
    if chip_split:
        summed = summed[:, :own] + lax.ppermute(summed[:, own:], "row", twin)
    scaled = summed * (degree_scale[None, :] / math.sqrt(total_rows))
    partial_value = lax.dot_general(
        lanczos_block, scaled, (((1,), (1,)), ((), ())), precision=HIGHEST
    )
    coupling = sum_over_rows(partial_value) / total_rows
    projected = lax.dot_general(
        coupling, lanczos_block, (((0,), (0,)), ((), ())), precision=HIGHEST
    )
    result = scaled - projected - jnp.dot(previous_coupling, previous_block, precision=HIGHEST)
    return (result, coupling)


def solution(mesh):
    in_specs = (
        P(None, ("cohort", "row")),
        P(("cohort", "row")),
        P(("cohort", "row")),
        P(None, ("cohort", "row")),
        P(None, ("cohort", "row")),
        P("cohort", None),
        P(("cohort", "row"), None),
        P(("cohort", "row")),
    )
    out_specs = (P(None, ("cohort", "row")), P("cohort", None))
    return jax.shard_map(shards, mesh=mesh, in_specs=in_specs, out_specs=out_specs, check_vma=False)
```

```python
import functools
import math

import jax
import jax.numpy as jnp
from jax import lax
from jax.experimental import pallas as pl
from jax.experimental.pallas import tpu as pltpu
from jax.sharding import PartitionSpec as P

LANCZOS = 16
BLK = 1024


HIGHEST = lax.Precision.HIGHEST


def piece_terms(width, x_cols, w_cols, xo_ref, no_ref, ro_ref):
    x_wide = x_cols.astype(jnp.float32)
    norm_cols = jnp.sum(x_wide * x_wide, axis=0, keepdims=True)
    recip_cols = 1.0 / w_cols[LANCZOS : LANCZOS + 1, :].astype(jnp.float32)
    twice_inner = jnp.dot(xo_ref[...], x_cols, preferred_element_type=jnp.float32)
    distance = (no_ref[...] + norm_cols) - twice_inner
    weights = jnp.exp2(distance * (ro_ref[...] * recip_cols)).astype(jnp.bfloat16)
    return lax.dot_general(
        w_cols[:LANCZOS, :], weights, (((1,), (1,)), ((), ())),
        preferred_element_type=jnp.float32,
    )


def affinity_kernel(width, per, flag_ref, xo_ref, no_ref, ro_ref, x_ref, w_ref, out_ref):
    s = pl.program_id(0)

    @pl.when(s == 0)
    def _():
        out_ref[...] = jnp.zeros_like(out_ref)

    for k in range(per):

        @pl.when(flag_ref[s * per + k] != 0)
        def _():
            out_ref[...] += piece_terms(
                width, x_ref[k, :width, :], w_ref[k],
                xo_ref, no_ref, ro_ref,
            )


def list_kernel(width, rows, counts, flag_ref, xo_ref, no_ref, ro_ref, *refs):
    out_ref = refs[-1]
    out_ref[...] = jnp.zeros_like(out_ref)
    slot = 0
    for ref, count in zip(refs[:-1], counts):
        for k in range(count):

            @pl.when(flag_ref[slot] != 0)
            def _():
                base = k * rows
                out_ref[...] += piece_terms(
                    width,
                    ref[base : base + width, :],
                    ref[base + width : base + width + 2 * LANCZOS, :],
                    xo_ref, no_ref, ro_ref,
                )

            slot += 1


def list_product(flags, own_terms, pieces, width, rows):
    twice_own_t, norm_own, recip_own = own_terms
    own = twice_own_t.shape[0]
    counts = [p.shape[0] // rows for p in pieces]
    vmem = pl.BlockSpec(memory_space=pltpu.VMEM)
    return pl.pallas_call(
        functools.partial(list_kernel, width, rows, counts),
        in_specs=[pl.BlockSpec(memory_space=pltpu.SMEM)] + [vmem] * (3 + len(pieces)),
        out_specs=vmem,
        out_shape=jax.ShapeDtypeStruct((LANCZOS, own), jnp.float32),
    )(flags, twice_own_t, norm_own, recip_own, *pieces)


def own_rows_product(flags, own_terms, mine, width):
    twice_own_t, norm_own, recip_own = own_terms
    own = twice_own_t.shape[0]
    slots, rows, cols = mine.shape
    per = 2 if slots % 2 == 0 else 1
    lanes_row = width // LANCZOS
    x_spec = pl.BlockSpec((per, rows, cols), lambda s, m: (s, 0, 0))
    w_spec = pl.BlockSpec((per, 2 * LANCZOS, cols), lambda s, m: (s, lanes_row // 2, 0))
    grid_spec = pltpu.PrefetchScalarGridSpec(
        num_scalar_prefetch=1,
        grid=(slots // per,),
        in_specs=[
            pl.BlockSpec((own, width), lambda s, m: (0, 0)),
            pl.BlockSpec((own, 1), lambda s, m: (0, 0)),
            pl.BlockSpec((own, 1), lambda s, m: (0, 0)),
            x_spec, w_spec,
        ],
        out_specs=pl.BlockSpec((LANCZOS, own), lambda s, m: (0, 0)),
    )
    return pl.pallas_call(
        functools.partial(affinity_kernel, width, per),
        grid_spec=grid_spec,
        out_shape=jax.ShapeDtypeStruct((LANCZOS, own), jnp.float32),
    )(flags, twice_own_t, norm_own, recip_own, mine, mine)


def gather_pieces(packed):
    devices = lax.axis_size("row")
    me = lax.axis_index("row")
    if devices != 16:
        pieces = lax.all_gather(packed, "row", axis=0, tiled=False)
        return [pieces], None, jnp.arange(devices, dtype=jnp.int32)
    up = [(r, r + 4) for r in range(12)]
    down = [(r, r - 4) for r in range(4, 16)]
    across = [(r, r ^ 2) for r in range(16)]
    z = me // 4
    partner = me ^ 2

    ends = (z == 0) | (z == 3)
    up1 = lax.ppermute(packed, "row", up)
    down1 = lax.ppermute(packed, "row", down)
    across1 = lax.ppermute(packed, "row", across)
    up2 = lax.ppermute(up1, "row", up)
    down2 = lax.ppermute(down1, "row", down)
    across2 = lax.ppermute(jnp.where(z <= 2, down1, up1), "row", across)
    up3 = lax.ppermute(up2, "row", up)
    down3 = lax.ppermute(down2, "row", down)
    across3 = lax.ppermute(jnp.where(z >= 2, up2, down2), "row", across)
    last = jnp.where(ends, jnp.where(z == 3, up3, down3), up1)
    across4 = lax.ppermute(last, "row", across)

    one = jnp.ones((), bool)
    pieces = [packed, up1, down1, across1, up2, down2, across2, up3, down3, across3, across4]
    valid = [one, z >= 1, z <= 2, one, z >= 2, z <= 1, one, z == 3, z == 0, one, one]
    origin = [
        me, me - 4, me + 4, partner, me - 8, me + 8,
        jnp.where(z <= 2, partner + 4, partner - 4), me - 12, me + 12,
        jnp.where(z >= 2, partner - 8, partner + 8),
        jnp.where(ends, jnp.where(z == 3, partner - 12, partner + 12), partner - 4),
    ]
    return pieces, jnp.stack(valid), jnp.clip(jnp.stack(origin), 0, devices - 1).astype(jnp.int32)


def sum_over_rows(value):
    devices = lax.axis_size("row")
    if devices != 16:
        if devices & (devices - 1):
            return lax.psum(value, "row")
        stride = 1
        while stride < devices:
            value = value + lax.ppermute(value, "row", [(i, i ^ stride) for i in range(devices)])
            stride *= 2
        return value
    me = lax.axis_index("row")
    for shift in (0, 2):
        got = {0: value}
        for m in (1, 2, 3):
            got[m] = lax.ppermute(value, "row", [(i, i ^ (m << shift)) for i in range(devices)])
        place = (me >> shift) & 3
        total = None
        for k in range(4):
            member = got[0]
            for m in (1, 2, 3):
                member = jnp.where((k ^ place) == m, got[m], member)
            total = member if total is None else total + member
        value = total
    return value


def shards(
    embeddings,
    local_scale,
    degree_scale,
    lanczos_block,
    previous_block,
    previous_coupling,
    tile_plan,
    tile_counts,
):
    width, own = embeddings.shape
    devices = lax.axis_size("row")
    total_rows = devices * own
    slots = tile_plan.shape[0]
    chip_split = devices == 16
    twin = [(r, r ^ 1) for r in range(devices)]
    weighted = (degree_scale[None, :] * lanczos_block).astype(jnp.bfloat16)
    plan_len = 2 * slots + 1
    plan_row = jnp.concatenate([tile_plan.reshape(-1), tile_counts]).astype(jnp.bfloat16)
    if chip_split:
        plan_row = jnp.concatenate([plan_row, lax.ppermute(plan_row, "row", twin)])
    plan_row = jnp.pad(plan_row, (0, own - plan_row.shape[0]))
    packed = jnp.concatenate(
        [embeddings, weighted, local_scale[None, :], plan_row[None, :]], axis=0
    )
    packed = jnp.pad(packed, ((0, -packed.shape[0] % (2 * LANCZOS)), (0, 0)))
    pieces, valid, origin = gather_pieces(packed)
    rows = packed.shape[0]

    plan_at = width + LANCZOS + 1
    copies = 2 if chip_split else 1
    plans = jnp.concatenate([p.reshape(-1, rows, own)[:, plan_at, : copies * plan_len] for p in pieces])
    plans = plans.astype(jnp.int32).reshape(-1, plan_len)
    counts = plans[:, 2 * slots]
    pairs = plans[:, : 2 * slots].reshape(-1, slots, 2)
    live = jnp.arange(slots, dtype=jnp.int32)[None, :] < counts[:, None]
    row_block = pairs[..., 0].reshape(-1)[:, None]
    col_block = pairs[..., 1].reshape(-1)[:, None]
    live = live.reshape(-1)[:, None]
    my_block = (lax.axis_index("row") * own) // BLK
    piece_block = ((origin * own) // BLK)[None, :]
    hit = live & (
        ((row_block == my_block) & (col_block == piece_block))
        | ((col_block == my_block) & (row_block == piece_block))
    )
    flags = jnp.any(hit, axis=0)
    if valid is not None:
        flags = flags & valid
    flags = flags.astype(jnp.int32)

    if chip_split:
        twin_piece = lax.ppermute(packed, "row", twin)
        rows_x = jnp.concatenate([embeddings, twin_piece[:width]], axis=1)
        rows_scale = jnp.concatenate([local_scale, twin_piece[width + LANCZOS]])
    else:
        rows_x, rows_scale = embeddings, local_scale
    norm_rows = jnp.sum(jnp.square(rows_x.astype(jnp.float32)), axis=0)[:, None]
    log2e = 1.0 / math.log(2.0)
    recip_rows = (-log2e / rows_scale.astype(jnp.float32))[:, None]
    own_terms = ((rows_x * 2).T, norm_rows, recip_rows)
    if chip_split:
        summed = list_product(flags, own_terms, pieces, width, rows)
    else:
        summed = own_rows_product(flags, own_terms, pieces[0].reshape(devices, rows, own), width)
    if chip_split:
        summed = summed[:, :own] + lax.ppermute(summed[:, own:], "row", twin)
    scaled = summed * (degree_scale[None, :] / math.sqrt(total_rows))
    partial_value = lax.dot_general(
        lanczos_block, scaled, (((1,), (1,)), ((), ())), precision=HIGHEST
    )
    coupling = sum_over_rows(partial_value) / total_rows
    projected = lax.dot_general(
        coupling, lanczos_block, (((0,), (0,)), ((), ())), precision=HIGHEST
    )
    result = scaled - projected - jnp.dot(previous_coupling, previous_block, precision=HIGHEST)
    return (result, coupling)


def solution(mesh):
    in_specs = (
        P(None, ("cohort", "row")),
        P(("cohort", "row")),
        P(("cohort", "row")),
        P(None, ("cohort", "row")),
        P(None, ("cohort", "row")),
        P("cohort", None),
        P(("cohort", "row"), None),
        P(("cohort", "row")),
    )
    out_specs = (P(None, ("cohort", "row")), P("cohort", None))
    return jax.shard_map(shards, mesh=mesh, in_specs=in_specs, out_specs=out_specs, check_vma=False)
```

```python
import functools
import math

import jax
import jax.numpy as jnp
from jax import lax
from jax.experimental import pallas as pl
from jax.experimental.pallas import tpu as pltpu
from jax.sharding import PartitionSpec as P

LANCZOS = 16
BLK = 1024


HIGHEST = lax.Precision.HIGHEST


def piece_terms(width, x_cols, w_cols, xo_ref, no_ref, ro_ref):
    x_wide = x_cols.astype(jnp.float32)
    norm_cols = jnp.sum(x_wide * x_wide, axis=0, keepdims=True)
    recip_cols = 1.0 / w_cols[LANCZOS : LANCZOS + 1, :].astype(jnp.float32)
    twice_inner = jnp.dot(xo_ref[...], x_cols, preferred_element_type=jnp.float32)
    distance = (no_ref[...] + norm_cols) - twice_inner
    weights = jnp.exp2(distance * (ro_ref[...] * recip_cols)).astype(jnp.bfloat16)
    return lax.dot_general(
        w_cols[:LANCZOS, :], weights, (((1,), (1,)), ((), ())),
        preferred_element_type=jnp.float32,
    )


def affinity_kernel(width, per, flag_ref, xo_ref, no_ref, ro_ref, x_ref, w_ref, out_ref):
    s = pl.program_id(0)

    @pl.when(s == 0)
    def _():
        out_ref[...] = jnp.zeros_like(out_ref)

    for k in range(per):

        @pl.when(flag_ref[s * per + k] != 0)
        def _():
            out_ref[...] += piece_terms(
                width, x_ref[k, :width, :], w_ref[k],
                xo_ref, no_ref, ro_ref,
            )


def list_kernel(width, rows, counts, split, flag_ref, xo_ref, no_ref, ro_ref, *refs):
    out_ref = refs[-1]
    if not split:
        out_ref[...] = jnp.zeros_like(out_ref)
    slot = 0
    for ref, count in zip(refs[:-1], counts):
        for k in range(count):
            base = k * rows

            def term(ref=ref, base=base):
                return piece_terms(
                    width,
                    ref[base : base + width, :],
                    ref[base + width : base + width + 2 * LANCZOS, :],
                    xo_ref, no_ref, ro_ref,
                )

            if split:

                @pl.when(flag_ref[slot] != 0)
                def _(term=term, slot=slot):
                    out_ref[slot] = term()

                @pl.when(flag_ref[slot] == 0)
                def _(slot=slot):
                    out_ref[slot] = jnp.zeros(out_ref.shape[1:], jnp.float32)

            else:

                @pl.when(flag_ref[slot] != 0)
                def _(term=term):
                    out_ref[...] += term()

            slot += 1


def list_product(flags, own_terms, pieces, width, rows, split=False):
    twice_own_t, norm_own, recip_own = own_terms
    own = twice_own_t.shape[0]
    counts = [p.shape[0] // rows for p in pieces]
    shape = (sum(counts), LANCZOS, own) if split else (LANCZOS, own)
    vmem = pl.BlockSpec(memory_space=pltpu.VMEM)
    cols = pieces[0].shape[1]
    slots = sum(counts)
    cost = pl.CostEstimate(
        flops=slots * 2 * own * cols * (width + LANCZOS),
        transcendentals=slots * own * cols,
        bytes_accessed=sum(p.size * 2 for p in pieces) + int(math.prod(shape)) * 4,
    )
    return pl.pallas_call(
        functools.partial(list_kernel, width, rows, counts, split),
        cost_estimate=cost,
        in_specs=[pl.BlockSpec(memory_space=pltpu.SMEM)] + [vmem] * (3 + len(pieces)),
        out_specs=vmem,
        out_shape=jax.ShapeDtypeStruct(shape, jnp.float32),
    )(flags, twice_own_t, norm_own, recip_own, *pieces)


def own_rows_product(flags, own_terms, mine, width):
    twice_own_t, norm_own, recip_own = own_terms
    own = twice_own_t.shape[0]
    slots, rows, cols = mine.shape
    per = 2 if slots % 2 == 0 else 1
    lanes_row = width // LANCZOS
    x_spec = pl.BlockSpec((per, rows, cols), lambda s, m: (s, 0, 0))
    w_spec = pl.BlockSpec((per, 2 * LANCZOS, cols), lambda s, m: (s, lanes_row // 2, 0))
    grid_spec = pltpu.PrefetchScalarGridSpec(
        num_scalar_prefetch=1,
        grid=(slots // per,),
        in_specs=[
            pl.BlockSpec((own, width), lambda s, m: (0, 0)),
            pl.BlockSpec((own, 1), lambda s, m: (0, 0)),
            pl.BlockSpec((own, 1), lambda s, m: (0, 0)),
            x_spec, w_spec,
        ],
        out_specs=pl.BlockSpec((LANCZOS, own), lambda s, m: (0, 0)),
    )
    return pl.pallas_call(
        functools.partial(affinity_kernel, width, per),
        grid_spec=grid_spec,
        out_shape=jax.ShapeDtypeStruct((LANCZOS, own), jnp.float32),
    )(flags, twice_own_t, norm_own, recip_own, mine, mine)


def gather_pieces(packed, early_work=None):
    devices = lax.axis_size("row")
    me = lax.axis_index("row")
    if devices != 16:
        pieces = lax.all_gather(packed, "row", axis=0, tiled=False)
        return [pieces], None, jnp.arange(devices, dtype=jnp.int32)
    up = [(r, r + 4) for r in range(12)]
    down = [(r, r - 4) for r in range(4, 16)]
    across = [(r, r ^ 2) for r in range(16)]
    z = me // 4
    partner = me ^ 2

    ends = (z == 0) | (z == 3)
    up1 = lax.ppermute(packed, "row", up)
    down1 = lax.ppermute(packed, "row", down)
    across1 = lax.ppermute(packed, "row", across)
    up2 = lax.ppermute(up1, "row", up)
    down2 = lax.ppermute(down1, "row", down)
    across2 = lax.ppermute(jnp.where(z <= 2, down1, up1), "row", across)
    up3 = lax.ppermute(up2, "row", up)
    down3 = lax.ppermute(down2, "row", down)
    across3 = lax.ppermute(jnp.where(z >= 2, up2, down2), "row", across)
    last = jnp.where(ends, jnp.where(z == 3, up3, down3), up1)
    one = jnp.ones((), bool)
    early = None
    if early_work is not None:
        early = early_work([packed, up1, down1, across1, up2, down2],
                           jnp.stack([one, z >= 1, z <= 2, one, z >= 2, z <= 1]))
        last, early = lax.optimization_barrier((last, early))
    across4 = lax.ppermute(last, "row", across)

    pieces = [packed, up1, down1, across1, up2, down2, across2, up3, down3, across3, across4]
    valid = [one, z >= 1, z <= 2, one, z >= 2, z <= 1, one, z == 3, z == 0, one, one]
    origin = [
        me, me - 4, me + 4, partner, me - 8, me + 8,
        jnp.where(z <= 2, partner + 4, partner - 4), me - 12, me + 12,
        jnp.where(z >= 2, partner - 8, partner + 8),
        jnp.where(ends, jnp.where(z == 3, partner - 12, partner + 12), partner - 4),
    ]
    origin = jnp.clip(jnp.stack(origin), 0, devices - 1).astype(jnp.int32)
    if early_work is not None:
        return pieces, jnp.stack(valid), origin, early
    return pieces, jnp.stack(valid), origin


def sum_over_rows(value):
    devices = lax.axis_size("row")
    if devices != 16:
        if devices & (devices - 1):
            return lax.psum(value, "row")
        stride = 1
        while stride < devices:
            value = value + lax.ppermute(value, "row", [(i, i ^ stride) for i in range(devices)])
            stride *= 2
        return value
    me = lax.axis_index("row")
    for shift in (0, 2):
        got = {0: value}
        for m in (1, 2, 3):
            got[m] = lax.ppermute(value, "row", [(i, i ^ (m << shift)) for i in range(devices)])
        place = (me >> shift) & 3
        total = None
        for k in range(4):
            member = got[0]
            for m in (1, 2, 3):
                member = jnp.where((k ^ place) == m, got[m], member)
            total = member if total is None else total + member
        value = total
    return value


def shards(
    embeddings,
    local_scale,
    degree_scale,
    lanczos_block,
    previous_block,
    previous_coupling,
    tile_plan,
    tile_counts,
):
    width, own = embeddings.shape
    devices = lax.axis_size("row")
    total_rows = devices * own
    slots = tile_plan.shape[0]
    chip_split = devices == 16
    twin = [(r, r ^ 1) for r in range(devices)]
    weighted = (degree_scale[None, :] * lanczos_block).astype(jnp.bfloat16)
    plan_len = 2 * slots + 1
    plan_row = jnp.concatenate([tile_plan.reshape(-1), tile_counts]).astype(jnp.bfloat16)
    if chip_split:
        plan_row = jnp.concatenate([plan_row, lax.ppermute(plan_row, "row", twin)])
    plan_row = jnp.pad(plan_row, (0, own - plan_row.shape[0]))
    packed = jnp.concatenate(
        [embeddings, weighted, local_scale[None, :], plan_row[None, :]], axis=0
    )
    packed = jnp.pad(packed, ((0, -packed.shape[0] % (2 * LANCZOS)), (0, 0)))
    rows = packed.shape[0]
    if chip_split:
        twin_piece = lax.ppermute(packed, "row", twin)
        rows_x = jnp.concatenate([embeddings, twin_piece[:width]], axis=1)
        rows_scale = jnp.concatenate([local_scale, twin_piece[width + LANCZOS]])
    else:
        rows_x, rows_scale = embeddings, local_scale
    norm_rows = jnp.sum(jnp.square(rows_x.astype(jnp.float32)), axis=0)[:, None]
    log2e = 1.0 / math.log(2.0)
    recip_rows = (-log2e / rows_scale.astype(jnp.float32))[:, None]
    own_terms = ((rows_x * 2).T, norm_rows, recip_rows)
    if chip_split:
        def early_work(first, first_valid):
            return list_product(first_valid, own_terms, first, width, rows, split=True)

        pieces, valid, origin, early = gather_pieces(packed, early_work)
    else:
        pieces, valid, origin = gather_pieces(packed)

    plan_at = width + LANCZOS + 1
    copies = 2 if chip_split else 1
    plans = jnp.concatenate([p.reshape(-1, rows, own)[:, plan_at, : copies * plan_len] for p in pieces])
    plans = plans.astype(jnp.int32).reshape(-1, plan_len)
    counts = plans[:, 2 * slots]
    pairs = plans[:, : 2 * slots].reshape(-1, slots, 2)
    live = jnp.arange(slots, dtype=jnp.int32)[None, :] < counts[:, None]
    row_block = pairs[..., 0].reshape(-1)[:, None]
    col_block = pairs[..., 1].reshape(-1)[:, None]
    live = live.reshape(-1)[:, None]
    my_block = (lax.axis_index("row") * own) // BLK
    piece_block = ((origin * own) // BLK)[None, :]
    hit = live & (
        ((row_block == my_block) & (col_block == piece_block))
        | ((col_block == my_block) & (row_block == piece_block))
    )
    flags = jnp.any(hit, axis=0)
    if valid is not None:
        flags = flags & valid
    flags = flags.astype(jnp.int32)

    if chip_split:
        head = early.shape[0]
        summed = list_product(flags[head:], own_terms, pieces[head:], width, rows)
        summed = summed + jnp.sum(jnp.where(flags[:head, None, None] != 0, early, 0.0), axis=0)
    else:
        summed = own_rows_product(flags, own_terms, pieces[0].reshape(devices, rows, own), width)
    if chip_split:
        summed = summed[:, :own] + lax.ppermute(summed[:, own:], "row", twin)
    scaled = summed * (degree_scale[None, :] / math.sqrt(total_rows))
    partial_value = lax.dot_general(
        lanczos_block, scaled, (((1,), (1,)), ((), ())), precision=HIGHEST
    )
    coupling = sum_over_rows(partial_value) / total_rows
    projected = lax.dot_general(
        coupling, lanczos_block, (((0,), (0,)), ((), ())), precision=HIGHEST
    )
    result = scaled - projected - jnp.dot(previous_coupling, previous_block, precision=HIGHEST)
    return (result, coupling)


def solution(mesh):
    in_specs = (
        P(None, ("cohort", "row")),
        P(("cohort", "row")),
        P(("cohort", "row")),
        P(None, ("cohort", "row")),
        P(None, ("cohort", "row")),
        P("cohort", None),
        P(("cohort", "row"), None),
        P(("cohort", "row")),
    )
    out_specs = (P(None, ("cohort", "row")), P("cohort", None))
    return jax.shard_map(shards, mesh=mesh, in_specs=in_specs, out_specs=out_specs, check_vma=False)
```

```python
import functools
import math

import jax
import jax.numpy as jnp
from jax import lax
from jax.experimental import pallas as pl
from jax.experimental.pallas import tpu as pltpu
from jax.sharding import PartitionSpec as P

LANCZOS = 16
BLK = 1024


HIGHEST = lax.Precision.HIGHEST


def piece_terms(width, x_cols, w_cols, xo_ref, no_ref, ro_ref):
    x_wide = x_cols.astype(jnp.float32)
    norm_cols = jnp.sum(x_wide * x_wide, axis=0, keepdims=True)
    recip_cols = 1.0 / w_cols[LANCZOS : LANCZOS + 1, :].astype(jnp.float32)
    twice_inner = jnp.dot(xo_ref[...], x_cols, preferred_element_type=jnp.float32)
    distance = (no_ref[...] + norm_cols) - twice_inner
    weights = jnp.exp2(distance * (ro_ref[...] * recip_cols)).astype(jnp.bfloat16)
    return lax.dot_general(
        w_cols[:LANCZOS, :], weights, (((1,), (1,)), ((), ())),
        preferred_element_type=jnp.float32,
    )


def affinity_kernel(width, per, flag_ref, xo_ref, no_ref, ro_ref, x_ref, w_ref, out_ref):
    s = pl.program_id(0)

    @pl.when(s == 0)
    def _():
        out_ref[...] = jnp.zeros_like(out_ref)

    for k in range(per):

        @pl.when(flag_ref[s * per + k] != 0)
        def _():
            out_ref[...] += piece_terms(
                width, x_ref[k, :width, :], w_ref[k],
                xo_ref, no_ref, ro_ref,
            )


def list_kernel(width, rows, counts, split, flag_ref, xo_ref, no_ref, ro_ref, *refs):
    out_ref = refs[-1]
    if not split:
        out_ref[...] = jnp.zeros_like(out_ref)
    slot = 0
    for ref, count in zip(refs[:-1], counts):
        for k in range(count):
            base = k * rows

            def term(ref=ref, base=base):
                return piece_terms(
                    width,
                    ref[base : base + width, :],
                    ref[base + width : base + width + 2 * LANCZOS, :],
                    xo_ref, no_ref, ro_ref,
                )

            if split:

                @pl.when(flag_ref[slot] != 0)
                def _(term=term, slot=slot):
                    out_ref[slot] = term()

                @pl.when(flag_ref[slot] == 0)
                def _(slot=slot):
                    out_ref[slot] = jnp.zeros(out_ref.shape[1:], jnp.float32)

            else:

                @pl.when(flag_ref[slot] != 0)
                def _(term=term):
                    out_ref[...] += term()

            slot += 1


def list_product(flags, own_terms, pieces, width, rows, split=False):
    twice_own_t, norm_own, recip_own = own_terms
    own = twice_own_t.shape[0]
    counts = [p.shape[0] // rows for p in pieces]
    shape = (sum(counts), LANCZOS, own) if split else (LANCZOS, own)
    vmem = pl.BlockSpec(memory_space=pltpu.VMEM)
    cols = pieces[0].shape[1]
    slots = sum(counts)
    cost = pl.CostEstimate(
        flops=slots * 2 * own * cols * (width + LANCZOS),
        transcendentals=slots * own * cols,
        bytes_accessed=sum(p.size * 2 for p in pieces) + int(math.prod(shape)) * 4,
    )
    return pl.pallas_call(
        functools.partial(list_kernel, width, rows, counts, split),
        cost_estimate=cost,
        in_specs=[pl.BlockSpec(memory_space=pltpu.SMEM)] + [vmem] * (3 + len(pieces)),
        out_specs=vmem,
        out_shape=jax.ShapeDtypeStruct(shape, jnp.float32),
    )(flags, twice_own_t, norm_own, recip_own, *pieces)


def own_rows_product(flags, own_terms, mine, width):
    twice_own_t, norm_own, recip_own = own_terms
    own = twice_own_t.shape[0]
    slots, rows, cols = mine.shape
    per = 2 if slots % 2 == 0 else 1
    lanes_row = width // LANCZOS
    x_spec = pl.BlockSpec((per, rows, cols), lambda s, m: (s, 0, 0))
    w_spec = pl.BlockSpec((per, 2 * LANCZOS, cols), lambda s, m: (s, lanes_row // 2, 0))
    grid_spec = pltpu.PrefetchScalarGridSpec(
        num_scalar_prefetch=1,
        grid=(slots // per,),
        in_specs=[
            pl.BlockSpec((own, width), lambda s, m: (0, 0)),
            pl.BlockSpec((own, 1), lambda s, m: (0, 0)),
            pl.BlockSpec((own, 1), lambda s, m: (0, 0)),
            x_spec, w_spec,
        ],
        out_specs=pl.BlockSpec((LANCZOS, own), lambda s, m: (0, 0)),
    )
    return pl.pallas_call(
        functools.partial(affinity_kernel, width, per),
        grid_spec=grid_spec,
        out_shape=jax.ShapeDtypeStruct((LANCZOS, own), jnp.float32),
    )(flags, twice_own_t, norm_own, recip_own, mine, mine)


def gather_pieces(packed, early_work=None):
    devices = lax.axis_size("row")
    me = lax.axis_index("row")
    if devices != 16:
        pieces = lax.all_gather(packed, "row", axis=0, tiled=False)
        return [pieces], None, jnp.arange(devices, dtype=jnp.int32)
    up = [(r, r + 4) for r in range(12)]
    down = [(r, r - 4) for r in range(4, 16)]
    across = [(r, r ^ 2) for r in range(16)]
    z = me // 4
    partner = me ^ 2

    ends = (z == 0) | (z == 3)
    up1 = lax.ppermute(packed, "row", up)
    down1 = lax.ppermute(packed, "row", down)
    across1 = lax.ppermute(packed, "row", across)
    second = jnp.where(z <= 2, down1, up1)
    up1, down1, second = lax.optimization_barrier((up1, down1, second))
    up2 = lax.ppermute(up1, "row", up)
    down2 = lax.ppermute(down1, "row", down)
    across2 = lax.ppermute(second, "row", across)
    up3 = lax.ppermute(up2, "row", up)
    down3 = lax.ppermute(down2, "row", down)
    across3 = lax.ppermute(jnp.where(z >= 2, up2, down2), "row", across)
    last = jnp.where(ends, jnp.where(z == 3, up3, down3), up1)
    one = jnp.ones((), bool)
    early = None
    if early_work is not None:
        early = early_work([packed, up1, down1, across1, up2, down2, across2],
                           jnp.stack([one, z >= 1, z <= 2, one, z >= 2, z <= 1, one]))
        last, early = lax.optimization_barrier((last, early))
    across4 = lax.ppermute(last, "row", across)

    pieces = [packed, up1, down1, across1, up2, down2, across2, up3, down3, across3, across4]
    valid = [one, z >= 1, z <= 2, one, z >= 2, z <= 1, one, z == 3, z == 0, one, one]
    origin = [
        me, me - 4, me + 4, partner, me - 8, me + 8,
        jnp.where(z <= 2, partner + 4, partner - 4), me - 12, me + 12,
        jnp.where(z >= 2, partner - 8, partner + 8),
        jnp.where(ends, jnp.where(z == 3, partner - 12, partner + 12), partner - 4),
    ]
    origin = jnp.clip(jnp.stack(origin), 0, devices - 1).astype(jnp.int32)
    if early_work is not None:
        return pieces, jnp.stack(valid), origin, early
    return pieces, jnp.stack(valid), origin


def sum_over_rows(value):
    devices = lax.axis_size("row")
    if devices != 16:
        if devices & (devices - 1):
            return lax.psum(value, "row")
        stride = 1
        while stride < devices:
            value = value + lax.ppermute(value, "row", [(i, i ^ stride) for i in range(devices)])
            stride *= 2
        return value
    me = lax.axis_index("row")
    for shift in (0, 2):
        got = {0: value}
        for m in (1, 2, 3):
            got[m] = lax.ppermute(value, "row", [(i, i ^ (m << shift)) for i in range(devices)])
        place = (me >> shift) & 3
        total = None
        for k in range(4):
            member = got[0]
            for m in (1, 2, 3):
                member = jnp.where((k ^ place) == m, got[m], member)
            total = member if total is None else total + member
        value = total
    return value


def shards(
    embeddings,
    local_scale,
    degree_scale,
    lanczos_block,
    previous_block,
    previous_coupling,
    tile_plan,
    tile_counts,
):
    width, own = embeddings.shape
    devices = lax.axis_size("row")
    total_rows = devices * own
    slots = tile_plan.shape[0]
    chip_split = devices == 16
    twin = [(r, r ^ 1) for r in range(devices)]
    weighted = (degree_scale[None, :] * lanczos_block).astype(jnp.bfloat16)
    plan_len = 2 * slots + 1
    plan_row = jnp.concatenate([tile_plan.reshape(-1), tile_counts]).astype(jnp.bfloat16)
    if chip_split:
        plan_row = jnp.concatenate([plan_row, lax.ppermute(plan_row, "row", twin)])
    plan_row = jnp.pad(plan_row, (0, own - plan_row.shape[0]))
    packed = jnp.concatenate(
        [embeddings, weighted, local_scale[None, :], plan_row[None, :]], axis=0
    )
    packed = jnp.pad(packed, ((0, -packed.shape[0] % (2 * LANCZOS)), (0, 0)))
    rows = packed.shape[0]
    if chip_split:
        twin_piece = lax.ppermute(packed, "row", twin)
        rows_x = jnp.concatenate([embeddings, twin_piece[:width]], axis=1)
        rows_scale = jnp.concatenate([local_scale, twin_piece[width + LANCZOS]])
    else:
        rows_x, rows_scale = embeddings, local_scale
    norm_rows = jnp.sum(jnp.square(rows_x.astype(jnp.float32)), axis=0)[:, None]
    log2e = 1.0 / math.log(2.0)
    recip_rows = (-log2e / rows_scale.astype(jnp.float32))[:, None]
    own_terms = ((rows_x * 2).T, norm_rows, recip_rows)
    if chip_split:
        def early_work(first, first_valid):
            return list_product(first_valid, own_terms, first, width, rows, split=True)

        pieces, valid, origin, early = gather_pieces(packed, early_work)
    else:
        pieces, valid, origin = gather_pieces(packed)

    plan_at = width + LANCZOS + 1
    copies = 2 if chip_split else 1
    plans = jnp.concatenate([p.reshape(-1, rows, own)[:, plan_at, : copies * plan_len] for p in pieces])
    plans = plans.astype(jnp.int32).reshape(-1, plan_len)
    counts = plans[:, 2 * slots]
    pairs = plans[:, : 2 * slots].reshape(-1, slots, 2)
    live = jnp.arange(slots, dtype=jnp.int32)[None, :] < counts[:, None]
    row_block = pairs[..., 0].reshape(-1)[:, None]
    col_block = pairs[..., 1].reshape(-1)[:, None]
    live = live.reshape(-1)[:, None]
    my_block = (lax.axis_index("row") * own) // BLK
    piece_block = ((origin * own) // BLK)[None, :]
    hit = live & (
        ((row_block == my_block) & (col_block == piece_block))
        | ((col_block == my_block) & (row_block == piece_block))
    )
    flags = jnp.any(hit, axis=0)
    if valid is not None:
        flags = flags & valid
    flags = flags.astype(jnp.int32)

    if chip_split:
        head = early.shape[0]
        summed = list_product(flags[head:], own_terms, pieces[head:], width, rows)
        summed = summed + jnp.sum(jnp.where(flags[:head, None, None] != 0, early, 0.0), axis=0)
    else:
        summed = own_rows_product(flags, own_terms, pieces[0].reshape(devices, rows, own), width)
    if chip_split:
        summed = summed[:, :own] + lax.ppermute(summed[:, own:], "row", twin)
    scaled = summed * (degree_scale[None, :] / math.sqrt(total_rows))
    partial_value = lax.dot_general(
        lanczos_block, scaled, (((1,), (1,)), ((), ())), precision=HIGHEST
    )
    coupling = sum_over_rows(partial_value) / total_rows
    projected = lax.dot_general(
        coupling, lanczos_block, (((0,), (0,)), ((), ())), precision=HIGHEST
    )
    result = scaled - projected - jnp.dot(previous_coupling, previous_block, precision=HIGHEST)
    return (result, coupling)


def solution(mesh):
    in_specs = (
        P(None, ("cohort", "row")),
        P(("cohort", "row")),
        P(("cohort", "row")),
        P(None, ("cohort", "row")),
        P(None, ("cohort", "row")),
        P("cohort", None),
        P(("cohort", "row"), None),
        P(("cohort", "row")),
    )
    out_specs = (P(None, ("cohort", "row")), P("cohort", None))
    return jax.shard_map(shards, mesh=mesh, in_specs=in_specs, out_specs=out_specs, check_vma=False)
```

```python
import functools
import math

import jax
import jax.numpy as jnp
from jax import lax
from jax.experimental import pallas as pl
from jax.experimental.pallas import tpu as pltpu
from jax.sharding import PartitionSpec as P

LANCZOS = 16
BLK = 1024


HIGHEST = lax.Precision.HIGHEST


def piece_terms(width, x_cols, w_cols, xo_ref, no_ref, ro_ref):
    x_wide = x_cols.astype(jnp.float32)
    norm_cols = jnp.sum(x_wide * x_wide, axis=0, keepdims=True)
    recip_cols = 1.0 / w_cols[LANCZOS : LANCZOS + 1, :].astype(jnp.float32)
    twice_inner = jnp.dot(xo_ref[...], x_cols, preferred_element_type=jnp.float32)
    distance = (no_ref[...] + norm_cols) - twice_inner
    weights = jnp.exp2(distance * (ro_ref[...] * recip_cols)).astype(jnp.bfloat16)
    return lax.dot_general(
        w_cols[:LANCZOS, :], weights, (((1,), (1,)), ((), ())),
        preferred_element_type=jnp.float32,
    )


def affinity_kernel(width, per, flag_ref, xo_ref, no_ref, ro_ref, x_ref, w_ref, out_ref):
    s = pl.program_id(0)

    @pl.when(s == 0)
    def _():
        out_ref[...] = jnp.zeros_like(out_ref)

    for k in range(per):

        @pl.when(flag_ref[s * per + k] != 0)
        def _():
            out_ref[...] += piece_terms(
                width, x_ref[k, :width, :], w_ref[k],
                xo_ref, no_ref, ro_ref,
            )


def list_kernel(width, rows, counts, split, flag_ref, xo_ref, no_ref, ro_ref, *refs):
    out_ref = refs[-1]
    if not split:
        out_ref[...] = jnp.zeros_like(out_ref)
    slot = 0
    for ref, count in zip(refs[:-1], counts):
        for k in range(count):
            base = k * rows

            def term(ref=ref, base=base):
                return piece_terms(
                    width,
                    ref[base : base + width, :],
                    ref[base + width : base + width + 2 * LANCZOS, :],
                    xo_ref, no_ref, ro_ref,
                )

            if split:

                @pl.when(flag_ref[slot] != 0)
                def _(term=term, slot=slot):
                    out_ref[slot] = term()

                @pl.when(flag_ref[slot] == 0)
                def _(slot=slot):
                    out_ref[slot] = jnp.zeros(out_ref.shape[1:], jnp.float32)

            else:

                @pl.when(flag_ref[slot] != 0)
                def _(term=term):
                    out_ref[...] += term()

            slot += 1


def list_product(flags, own_terms, pieces, width, rows, split=False):
    twice_own_t, norm_own, recip_own = own_terms
    own = twice_own_t.shape[0]
    counts = [p.shape[0] // rows for p in pieces]
    shape = (sum(counts), LANCZOS, own) if split else (LANCZOS, own)
    vmem = pl.BlockSpec(memory_space=pltpu.VMEM)
    cols = pieces[0].shape[1]
    slots = sum(counts)
    cost = pl.CostEstimate(
        flops=slots * 2 * own * cols * (width + LANCZOS),
        transcendentals=slots * own * cols,
        bytes_accessed=sum(p.size * 2 for p in pieces) + int(math.prod(shape)) * 4,
    )
    return pl.pallas_call(
        functools.partial(list_kernel, width, rows, counts, split),
        cost_estimate=cost,
        in_specs=[pl.BlockSpec(memory_space=pltpu.SMEM)] + [vmem] * (3 + len(pieces)),
        out_specs=vmem,
        out_shape=jax.ShapeDtypeStruct(shape, jnp.float32),
    )(flags, twice_own_t, norm_own, recip_own, *pieces)


def own_rows_product(flags, own_terms, mine, width):
    twice_own_t, norm_own, recip_own = own_terms
    own = twice_own_t.shape[0]
    slots, rows, cols = mine.shape
    per = 2 if slots % 2 == 0 else 1
    lanes_row = width // LANCZOS
    x_spec = pl.BlockSpec((per, rows, cols), lambda s, m: (s, 0, 0))
    w_spec = pl.BlockSpec((per, 2 * LANCZOS, cols), lambda s, m: (s, lanes_row // 2, 0))
    grid_spec = pltpu.PrefetchScalarGridSpec(
        num_scalar_prefetch=1,
        grid=(slots // per,),
        in_specs=[
            pl.BlockSpec((own, width), lambda s, m: (0, 0)),
            pl.BlockSpec((own, 1), lambda s, m: (0, 0)),
            pl.BlockSpec((own, 1), lambda s, m: (0, 0)),
            x_spec, w_spec,
        ],
        out_specs=pl.BlockSpec((LANCZOS, own), lambda s, m: (0, 0)),
    )
    return pl.pallas_call(
        functools.partial(affinity_kernel, width, per),
        grid_spec=grid_spec,
        out_shape=jax.ShapeDtypeStruct((LANCZOS, own), jnp.float32),
    )(flags, twice_own_t, norm_own, recip_own, mine, mine)


def gather_pieces(packed, early_work=None):
    devices = lax.axis_size("row")
    me = lax.axis_index("row")
    if devices != 16:
        pieces = lax.all_gather(packed, "row", axis=0, tiled=False)
        return [pieces], None, jnp.arange(devices, dtype=jnp.int32)
    up = [(r, r + 4) for r in range(12)]
    down = [(r, r - 4) for r in range(4, 16)]
    across = [(r, r ^ 2) for r in range(16)]
    z = me // 4
    partner = me ^ 2

    ends = (z == 0) | (z == 3)
    up1 = lax.ppermute(packed, "row", up)
    down1 = lax.ppermute(packed, "row", down)
    across1 = lax.ppermute(packed, "row", across)
    second = jnp.where(z <= 2, down1, up1)
    up1, down1, second = lax.optimization_barrier((up1, down1, second))
    up2 = lax.ppermute(up1, "row", up)
    down2 = lax.ppermute(down1, "row", down)
    across2 = lax.ppermute(second, "row", across)
    up3 = lax.ppermute(up2, "row", up)
    down3 = lax.ppermute(down2, "row", down)
    across3 = lax.ppermute(jnp.where(z >= 2, up2, down2), "row", across)
    last = jnp.where(ends, jnp.where(z == 3, up3, down3), up1)
    one = jnp.ones((), bool)
    early = None
    if early_work is not None:
        early = early_work([packed, up1, down1, across1, up2, down2, across2],
                           jnp.stack([one, z >= 1, z <= 2, one, z >= 2, z <= 1, one]))
        last, early = lax.optimization_barrier((last, early))
    across4 = lax.ppermute(last, "row", across)

    pieces = [packed, up1, down1, across1, up2, down2, across2, up3, down3, across3, across4]
    valid = [one, z >= 1, z <= 2, one, z >= 2, z <= 1, one, z == 3, z == 0, one, one]
    origin = [
        me, me - 4, me + 4, partner, me - 8, me + 8,
        jnp.where(z <= 2, partner + 4, partner - 4), me - 12, me + 12,
        jnp.where(z >= 2, partner - 8, partner + 8),
        jnp.where(ends, jnp.where(z == 3, partner - 12, partner + 12), partner - 4),
    ]
    origin = jnp.clip(jnp.stack(origin), 0, devices - 1).astype(jnp.int32)
    if early_work is not None:
        return pieces, jnp.stack(valid), origin, early
    return pieces, jnp.stack(valid), origin


def sum_over_rows(value):
    devices = lax.axis_size("row")
    if devices != 16:
        if devices & (devices - 1):
            return lax.psum(value, "row")
        stride = 1
        while stride < devices:
            value = value + lax.ppermute(value, "row", [(i, i ^ stride) for i in range(devices)])
            stride *= 2
        return value
    me = lax.axis_index("row")
    for shift in (0, 2):
        got = {0: value}
        for m in (1, 2, 3):
            got[m] = lax.ppermute(value, "row", [(i, i ^ (m << shift)) for i in range(devices)])
        place = (me >> shift) & 3
        total = None
        for k in range(4):
            member = got[0]
            for m in (1, 2, 3):
                member = jnp.where((k ^ place) == m, got[m], member)
            total = member if total is None else total + member
        value = total
    return value


def shards(
    embeddings,
    local_scale,
    degree_scale,
    lanczos_block,
    previous_block,
    previous_coupling,
    tile_plan,
    tile_counts,
):
    width, own = embeddings.shape
    devices = lax.axis_size("row")
    total_rows = devices * own
    slots = tile_plan.shape[0]
    chip_split = devices == 16
    twin = [(r, r ^ 1) for r in range(devices)]
    weighted = (degree_scale[None, :] * lanczos_block).astype(jnp.bfloat16)
    plan_len = 2 * slots + 1
    plan_row = jnp.concatenate([tile_plan.reshape(-1), tile_counts]).astype(jnp.bfloat16)
    if chip_split:
        plan_row = jnp.concatenate([plan_row, lax.ppermute(plan_row, "row", twin)])
    plan_row = jnp.pad(plan_row, (0, own - plan_row.shape[0]))
    packed = jnp.concatenate(
        [embeddings, weighted, local_scale[None, :], plan_row[None, :]], axis=0
    )
    packed = jnp.pad(packed, ((0, -packed.shape[0] % (2 * LANCZOS)), (0, 0)))
    rows = packed.shape[0]
    if chip_split:
        twin_piece = lax.ppermute(packed, "row", twin)
        rows_x = jnp.concatenate([embeddings, twin_piece[:width]], axis=1)
        rows_scale = jnp.concatenate([local_scale, twin_piece[width + LANCZOS]])
    else:
        rows_x, rows_scale = embeddings, local_scale
    norm_rows = jnp.sum(jnp.square(rows_x.astype(jnp.float32)), axis=0)[:, None]
    log2e = 1.0 / math.log(2.0)
    recip_rows = (-log2e / rows_scale.astype(jnp.float32))[:, None]
    own_terms = ((rows_x * 2).T, norm_rows, recip_rows)
    if chip_split:
        def early_work(first, first_valid):
            return list_product(first_valid, own_terms, first, width, rows, split=True)

        pieces, valid, origin, early = gather_pieces(packed, early_work)
    else:
        pieces, valid, origin = gather_pieces(packed)

    plan_at = width + LANCZOS + 1
    copies = 2 if chip_split else 1
    plans = jnp.concatenate([p.reshape(-1, rows, own)[:, plan_at, : copies * plan_len] for p in pieces])
    plans = plans.astype(jnp.int32).reshape(-1, plan_len)
    counts = plans[:, 2 * slots]
    pairs = plans[:, : 2 * slots].reshape(-1, slots, 2)
    live = jnp.arange(slots, dtype=jnp.int32)[None, :] < counts[:, None]
    row_block = pairs[..., 0].reshape(-1)[:, None]
    col_block = pairs[..., 1].reshape(-1)[:, None]
    live = live.reshape(-1)[:, None]
    my_block = (lax.axis_index("row") * own) // BLK
    piece_block = ((origin * own) // BLK)[None, :]
    hit = live & (
        ((row_block == my_block) & (col_block == piece_block))
        | ((col_block == my_block) & (row_block == piece_block))
    )
    flags = jnp.any(hit, axis=0)
    if valid is not None:
        flags = flags & valid
    flags = flags.astype(jnp.int32)

    if chip_split:
        head = early.shape[0]
        tail = len(pieces) - 1
        middle = list_product(valid[head:tail], own_terms, pieces[head:tail], width, rows, split=True)
        parts = jnp.concatenate([early, middle])
        summed = list_product(flags[tail:], own_terms, pieces[tail:], width, rows)
        summed = summed + jnp.sum(jnp.where(flags[:tail, None, None] != 0, parts, 0.0), axis=0)
    else:
        summed = own_rows_product(flags, own_terms, pieces[0].reshape(devices, rows, own), width)
    if chip_split:
        summed = summed[:, :own] + lax.ppermute(summed[:, own:], "row", twin)
    scaled = summed * (degree_scale[None, :] / math.sqrt(total_rows))
    partial_value = lax.dot_general(
        lanczos_block, scaled, (((1,), (1,)), ((), ())), precision=HIGHEST
    )
    coupling = sum_over_rows(partial_value) / total_rows
    projected = lax.dot_general(
        coupling, lanczos_block, (((0,), (0,)), ((), ())), precision=HIGHEST
    )
    result = scaled - projected - jnp.dot(previous_coupling, previous_block, precision=HIGHEST)
    return (result, coupling)


def solution(mesh):
    in_specs = (
        P(None, ("cohort", "row")),
        P(("cohort", "row")),
        P(("cohort", "row")),
        P(None, ("cohort", "row")),
        P(None, ("cohort", "row")),
        P("cohort", None),
        P(("cohort", "row"), None),
        P(("cohort", "row")),
    )
    out_specs = (P(None, ("cohort", "row")), P("cohort", None))
    return jax.shard_map(shards, mesh=mesh, in_specs=in_specs, out_specs=out_specs, check_vma=False)
```

```python
import functools
import math

import jax
import jax.numpy as jnp
from jax import lax
from jax.experimental import pallas as pl
from jax.experimental.pallas import tpu as pltpu
from jax.sharding import PartitionSpec as P

LANCZOS = 16
BLK = 1024


HIGHEST = lax.Precision.HIGHEST


def piece_terms(width, x_cols, w_cols, xo_ref, no_ref, ro_ref):
    x_wide = x_cols.astype(jnp.float32)
    norm_cols = jnp.sum(x_wide * x_wide, axis=0, keepdims=True)
    recip_cols = 1.0 / w_cols[LANCZOS : LANCZOS + 1, :].astype(jnp.float32)
    twice_inner = jnp.dot(xo_ref[...], x_cols, preferred_element_type=jnp.float32)
    distance = (no_ref[...] + norm_cols) - twice_inner
    weights = jnp.exp2(distance * (ro_ref[...] * recip_cols)).astype(jnp.bfloat16)
    return lax.dot_general(
        w_cols[:LANCZOS, :], weights, (((1,), (1,)), ((), ())),
        preferred_element_type=jnp.float32,
    )


def affinity_kernel(width, per, flag_ref, xo_ref, no_ref, ro_ref, x_ref, w_ref, out_ref):
    s = pl.program_id(0)

    @pl.when(s == 0)
    def _():
        out_ref[...] = jnp.zeros_like(out_ref)

    for k in range(per):

        @pl.when(flag_ref[s * per + k] != 0)
        def _():
            out_ref[...] += piece_terms(
                width, x_ref[k, :width, :], w_ref[k],
                xo_ref, no_ref, ro_ref,
            )


def list_kernel(width, rows, counts, split, flag_ref, xo_ref, no_ref, ro_ref, *refs):
    out_ref = refs[-1]
    if not split:
        out_ref[...] = jnp.zeros_like(out_ref)
    slot = 0
    for ref, count in zip(refs[:-1], counts):
        for k in range(count):
            base = k * rows

            def term(ref=ref, base=base):
                return piece_terms(
                    width,
                    ref[base : base + width, :],
                    ref[base + width : base + width + 2 * LANCZOS, :],
                    xo_ref, no_ref, ro_ref,
                )

            if split:

                @pl.when(flag_ref[slot] != 0)
                def _(term=term, slot=slot):
                    out_ref[slot] = term()

                @pl.when(flag_ref[slot] == 0)
                def _(slot=slot):
                    out_ref[slot] = jnp.zeros(out_ref.shape[1:], jnp.float32)

            else:

                @pl.when(flag_ref[slot] != 0)
                def _(term=term):
                    out_ref[...] += term()

            slot += 1


def list_product(flags, own_terms, pieces, width, rows, split=False):
    twice_own_t, norm_own, recip_own = own_terms
    own = twice_own_t.shape[0]
    counts = [p.shape[0] // rows for p in pieces]
    shape = (sum(counts), LANCZOS, own) if split else (LANCZOS, own)
    vmem = pl.BlockSpec(memory_space=pltpu.VMEM)
    cols = pieces[0].shape[1]
    slots = sum(counts)
    cost = pl.CostEstimate(
        flops=slots * 2 * own * cols * (width + LANCZOS),
        transcendentals=slots * own * cols,
        bytes_accessed=sum(p.size * 2 for p in pieces) + int(math.prod(shape)) * 4,
    )
    return pl.pallas_call(
        functools.partial(list_kernel, width, rows, counts, split),
        cost_estimate=cost,
        in_specs=[pl.BlockSpec(memory_space=pltpu.SMEM)] + [vmem] * (3 + len(pieces)),
        out_specs=vmem,
        out_shape=jax.ShapeDtypeStruct(shape, jnp.float32),
    )(flags, twice_own_t, norm_own, recip_own, *pieces)


def own_rows_product(flags, own_terms, mine, width):
    twice_own_t, norm_own, recip_own = own_terms
    own = twice_own_t.shape[0]
    slots, rows, cols = mine.shape
    per = 2 if slots % 2 == 0 else 1
    lanes_row = width // LANCZOS
    x_spec = pl.BlockSpec((per, rows, cols), lambda s, m: (s, 0, 0))
    w_spec = pl.BlockSpec((per, 2 * LANCZOS, cols), lambda s, m: (s, lanes_row // 2, 0))
    grid_spec = pltpu.PrefetchScalarGridSpec(
        num_scalar_prefetch=1,
        grid=(slots // per,),
        in_specs=[
            pl.BlockSpec((own, width), lambda s, m: (0, 0)),
            pl.BlockSpec((own, 1), lambda s, m: (0, 0)),
            pl.BlockSpec((own, 1), lambda s, m: (0, 0)),
            x_spec, w_spec,
        ],
        out_specs=pl.BlockSpec((LANCZOS, own), lambda s, m: (0, 0)),
    )
    return pl.pallas_call(
        functools.partial(affinity_kernel, width, per),
        grid_spec=grid_spec,
        out_shape=jax.ShapeDtypeStruct((LANCZOS, own), jnp.float32),
    )(flags, twice_own_t, norm_own, recip_own, mine, mine)


def gather_pieces(packed, early_work=None):
    devices = lax.axis_size("row")
    me = lax.axis_index("row")
    if devices != 16:
        pieces = lax.all_gather(packed, "row", axis=0, tiled=False)
        return [pieces], None, jnp.arange(devices, dtype=jnp.int32)
    zone = [r // 4 for r in range(16)]
    pairs_swap = [(r, r ^ 4) for r in range(16)]
    inner_swap = [(r, r + 4) for r in range(16) if zone[r] == 1] + [
        (r, r - 4) for r in range(16) if zone[r] == 2
    ]
    outward = [(r, r - 4) for r in range(16) if zone[r] == 1] + [
        (r, r + 4) for r in range(16) if zone[r] == 2
    ]
    across = [(r, r ^ 2) for r in range(16)]
    z = me // 4
    partner = me ^ 2
    mid = (z == 1) | (z == 2)
    low = z <= 1

    swap1 = lax.ppermute(packed, "row", pairs_swap)
    inner1 = lax.ppermute(packed, "row", inner_swap)
    across1 = lax.ppermute(packed, "row", across)
    swap1, inner1 = lax.optimization_barrier((swap1, inner1))
    inner2 = lax.ppermute(swap1, "row", inner_swap)
    out2 = lax.ppermute(inner1, "row", outward)
    across2 = lax.ppermute(swap1, "row", across)
    out3 = lax.ppermute(inner2, "row", outward)
    across3 = lax.ppermute(jnp.where(mid, inner1, out2), "row", across)
    last = jnp.where(mid, inner2, out3)
    one = jnp.ones((), bool)
    early = None
    if early_work is not None:
        early = early_work([packed, swap1, inner1, across1, inner2, out2, across2],
                           jnp.stack([one, one, mid, one, mid, ~mid, one]))
        last, early = lax.optimization_barrier((last, early))
    across4 = lax.ppermute(last, "row", across)

    pieces = [packed, swap1, inner1, across1, inner2, out2, across2, out3, across3, across4]
    valid = [one, one, mid, one, mid, ~mid, one, ~mid, one, one]
    origin = [
        me, me ^ 4, jnp.where(low, me + 4, me - 4), partner,
        jnp.where(low, me + 8, me - 8), jnp.where(low, me + 8, me - 8), partner ^ 4,
        jnp.where(low, me + 12, me - 12),
        jnp.where(mid, jnp.where(low, partner + 4, partner - 4), jnp.where(low, partner + 8, partner - 8)),
        jnp.where(mid, jnp.where(low, partner + 8, partner - 8), jnp.where(low, partner + 12, partner - 12)),
    ]
    origin = jnp.clip(jnp.stack(origin), 0, devices - 1).astype(jnp.int32)
    if early_work is not None:
        return pieces, jnp.stack(valid), origin, early
    return pieces, jnp.stack(valid), origin


def sum_over_rows(value):
    devices = lax.axis_size("row")
    if devices != 16:
        if devices & (devices - 1):
            return lax.psum(value, "row")
        stride = 1
        while stride < devices:
            value = value + lax.ppermute(value, "row", [(i, i ^ stride) for i in range(devices)])
            stride *= 2
        return value
    me = lax.axis_index("row")
    for shift in (0, 2):
        got = {0: value}
        for m in (1, 2, 3):
            got[m] = lax.ppermute(value, "row", [(i, i ^ (m << shift)) for i in range(devices)])
        place = (me >> shift) & 3
        total = None
        for k in range(4):
            member = got[0]
            for m in (1, 2, 3):
                member = jnp.where((k ^ place) == m, got[m], member)
            total = member if total is None else total + member
        value = total
    return value


def shards(
    embeddings,
    local_scale,
    degree_scale,
    lanczos_block,
    previous_block,
    previous_coupling,
    tile_plan,
    tile_counts,
):
    width, own = embeddings.shape
    devices = lax.axis_size("row")
    total_rows = devices * own
    slots = tile_plan.shape[0]
    chip_split = devices == 16
    twin = [(r, r ^ 1) for r in range(devices)]
    weighted = (degree_scale[None, :] * lanczos_block).astype(jnp.bfloat16)
    plan_len = 2 * slots + 1
    plan_row = jnp.concatenate([tile_plan.reshape(-1), tile_counts]).astype(jnp.bfloat16)
    if chip_split:
        plan_row = jnp.concatenate([plan_row, lax.ppermute(plan_row, "row", twin)])
    plan_row = jnp.pad(plan_row, (0, own - plan_row.shape[0]))
    packed = jnp.concatenate(
        [embeddings, weighted, local_scale[None, :], plan_row[None, :]], axis=0
    )
    packed = jnp.pad(packed, ((0, -packed.shape[0] % (2 * LANCZOS)), (0, 0)))
    rows = packed.shape[0]
    if chip_split:
        twin_piece = lax.ppermute(packed, "row", twin)
        rows_x = jnp.concatenate([embeddings, twin_piece[:width]], axis=1)
        rows_scale = jnp.concatenate([local_scale, twin_piece[width + LANCZOS]])
    else:
        rows_x, rows_scale = embeddings, local_scale
    norm_rows = jnp.sum(jnp.square(rows_x.astype(jnp.float32)), axis=0)[:, None]
    log2e = 1.0 / math.log(2.0)
    recip_rows = (-log2e / rows_scale.astype(jnp.float32))[:, None]
    own_terms = ((rows_x * 2).T, norm_rows, recip_rows)
    if chip_split:
        def early_work(first, first_valid):
            return list_product(first_valid, own_terms, first, width, rows, split=True)

        pieces, valid, origin, early = gather_pieces(packed, early_work)
    else:
        pieces, valid, origin = gather_pieces(packed)

    plan_at = width + LANCZOS + 1
    copies = 2 if chip_split else 1
    plans = jnp.concatenate([p.reshape(-1, rows, own)[:, plan_at, : copies * plan_len] for p in pieces])
    plans = plans.astype(jnp.int32).reshape(-1, plan_len)
    counts = plans[:, 2 * slots]
    pairs = plans[:, : 2 * slots].reshape(-1, slots, 2)
    live = jnp.arange(slots, dtype=jnp.int32)[None, :] < counts[:, None]
    row_block = pairs[..., 0].reshape(-1)[:, None]
    col_block = pairs[..., 1].reshape(-1)[:, None]
    live = live.reshape(-1)[:, None]
    my_block = (lax.axis_index("row") * own) // BLK
    piece_block = ((origin * own) // BLK)[None, :]
    hit = live & (
        ((row_block == my_block) & (col_block == piece_block))
        | ((col_block == my_block) & (row_block == piece_block))
    )
    flags = jnp.any(hit, axis=0)
    if valid is not None:
        flags = flags & valid
    flags = flags.astype(jnp.int32)

    if chip_split:
        head = early.shape[0]
        summed = list_product(flags[head:], own_terms, pieces[head:], width, rows)
        summed = summed + jnp.sum(jnp.where(flags[:head, None, None] != 0, early, 0.0), axis=0)
    else:
        summed = own_rows_product(flags, own_terms, pieces[0].reshape(devices, rows, own), width)
    if chip_split:
        summed = summed[:, :own] + lax.ppermute(summed[:, own:], "row", twin)
    scaled = summed * (degree_scale[None, :] / math.sqrt(total_rows))
    partial_value = lax.dot_general(
        lanczos_block, scaled, (((1,), (1,)), ((), ())), precision=HIGHEST
    )
    coupling = sum_over_rows(partial_value) / total_rows
    projected = lax.dot_general(
        coupling, lanczos_block, (((0,), (0,)), ((), ())), precision=HIGHEST
    )
    result = scaled - projected - jnp.dot(previous_coupling, previous_block, precision=HIGHEST)
    return (result, coupling)


def solution(mesh):
    in_specs = (
        P(None, ("cohort", "row")),
        P(("cohort", "row")),
        P(("cohort", "row")),
        P(None, ("cohort", "row")),
        P(None, ("cohort", "row")),
        P("cohort", None),
        P(("cohort", "row"), None),
        P(("cohort", "row")),
    )
    out_specs = (P(None, ("cohort", "row")), P("cohort", None))
    return jax.shard_map(shards, mesh=mesh, in_specs=in_specs, out_specs=out_specs, check_vma=False)
```

```python
import functools
import math

import jax
import jax.numpy as jnp
from jax import lax
from jax.experimental import pallas as pl
from jax.experimental.pallas import tpu as pltpu
from jax.sharding import PartitionSpec as P

LANCZOS = 16
BLK = 1024


HIGHEST = lax.Precision.HIGHEST


def piece_terms(width, x_cols, w_cols, xo_ref, no_ref, ro_ref):
    x_wide = x_cols.astype(jnp.float32)
    norm_cols = jnp.sum(x_wide * x_wide, axis=0, keepdims=True)
    recip_cols = 1.0 / w_cols[LANCZOS : LANCZOS + 1, :].astype(jnp.float32)
    twice_inner = jnp.dot(xo_ref[...], x_cols, preferred_element_type=jnp.float32)
    distance = (no_ref[...] + norm_cols) - twice_inner
    weights = jnp.exp2(distance * (ro_ref[...] * recip_cols)).astype(jnp.bfloat16)
    return lax.dot_general(
        w_cols[:LANCZOS, :], weights, (((1,), (1,)), ((), ())),
        preferred_element_type=jnp.float32,
    )


def affinity_kernel(width, per, flag_ref, xo_ref, no_ref, ro_ref, x_ref, w_ref, out_ref):
    s = pl.program_id(0)

    @pl.when(s == 0)
    def _():
        out_ref[...] = jnp.zeros_like(out_ref)

    for k in range(per):

        @pl.when(flag_ref[s * per + k] != 0)
        def _():
            out_ref[...] += piece_terms(
                width, x_ref[k, :width, :], w_ref[k],
                xo_ref, no_ref, ro_ref,
            )


def list_kernel(width, rows, counts, split, flag_ref, xo_ref, no_ref, ro_ref, *refs):
    out_ref = refs[-1]
    if not split:
        out_ref[...] = jnp.zeros_like(out_ref)
    slot = 0
    for ref, count in zip(refs[:-1], counts):
        for k in range(count):
            base = k * rows

            def term(ref=ref, base=base):
                return piece_terms(
                    width,
                    ref[base : base + width, :],
                    ref[base + width : base + width + 2 * LANCZOS, :],
                    xo_ref, no_ref, ro_ref,
                )

            if split:

                @pl.when(flag_ref[slot] != 0)
                def _(term=term, slot=slot):
                    out_ref[slot] = term()

                @pl.when(flag_ref[slot] == 0)
                def _(slot=slot):
                    out_ref[slot] = jnp.zeros(out_ref.shape[1:], jnp.float32)

            else:

                @pl.when(flag_ref[slot] != 0)
                def _(term=term):
                    out_ref[...] += term()

            slot += 1


def list_product(flags, own_terms, pieces, width, rows, split=False):
    twice_own_t, norm_own, recip_own = own_terms
    own = twice_own_t.shape[0]
    counts = [p.shape[0] // rows for p in pieces]
    shape = (sum(counts), LANCZOS, own) if split else (LANCZOS, own)
    vmem = pl.BlockSpec(memory_space=pltpu.VMEM)
    cols = pieces[0].shape[1]
    slots = sum(counts)
    cost = pl.CostEstimate(
        flops=slots * 2 * own * cols * (width + LANCZOS),
        transcendentals=slots * own * cols,
        bytes_accessed=sum(p.size * 2 for p in pieces) + int(math.prod(shape)) * 4,
    )
    return pl.pallas_call(
        functools.partial(list_kernel, width, rows, counts, split),
        cost_estimate=cost,
        in_specs=[pl.BlockSpec(memory_space=pltpu.SMEM)] + [vmem] * (3 + len(pieces)),
        out_specs=vmem,
        out_shape=jax.ShapeDtypeStruct(shape, jnp.float32),
    )(flags, twice_own_t, norm_own, recip_own, *pieces)


def own_rows_product(flags, own_terms, mine, width):
    twice_own_t, norm_own, recip_own = own_terms
    own = twice_own_t.shape[0]
    slots, rows, cols = mine.shape
    per = 2 if slots % 2 == 0 else 1
    lanes_row = width // LANCZOS
    x_spec = pl.BlockSpec((per, rows, cols), lambda s, m: (s, 0, 0))
    w_spec = pl.BlockSpec((per, 2 * LANCZOS, cols), lambda s, m: (s, lanes_row // 2, 0))
    grid_spec = pltpu.PrefetchScalarGridSpec(
        num_scalar_prefetch=1,
        grid=(slots // per,),
        in_specs=[
            pl.BlockSpec((own, width), lambda s, m: (0, 0)),
            pl.BlockSpec((own, 1), lambda s, m: (0, 0)),
            pl.BlockSpec((own, 1), lambda s, m: (0, 0)),
            x_spec, w_spec,
        ],
        out_specs=pl.BlockSpec((LANCZOS, own), lambda s, m: (0, 0)),
    )
    return pl.pallas_call(
        functools.partial(affinity_kernel, width, per),
        grid_spec=grid_spec,
        out_shape=jax.ShapeDtypeStruct((LANCZOS, own), jnp.float32),
    )(flags, twice_own_t, norm_own, recip_own, mine, mine)


def gather_pieces(packed, early_work=None):
    devices = lax.axis_size("row")
    me = lax.axis_index("row")
    if devices != 16:
        pieces = lax.all_gather(packed, "row", axis=0, tiled=False)
        return [pieces], None, jnp.arange(devices, dtype=jnp.int32)
    zone = [r // 4 for r in range(16)]
    pairs_swap = [(r, r ^ 4) for r in range(16)]
    inner_swap = [(r, r + 4) for r in range(16) if zone[r] == 1] + [
        (r, r - 4) for r in range(16) if zone[r] == 2
    ]
    outward = [(r, r - 4) for r in range(16) if zone[r] == 1] + [
        (r, r + 4) for r in range(16) if zone[r] == 2
    ]
    across = [(r, r ^ 2) for r in range(16)]
    z = me // 4
    partner = me ^ 2
    mid = (z == 1) | (z == 2)
    low = z <= 1

    swap1 = lax.ppermute(packed, "row", pairs_swap)
    inner1 = lax.ppermute(packed, "row", inner_swap)
    across1 = lax.ppermute(packed, "row", across)
    swap1, inner1 = lax.optimization_barrier((swap1, inner1))
    inner2 = lax.ppermute(swap1, "row", inner_swap)
    out2 = lax.ppermute(inner1, "row", outward)
    across2 = lax.ppermute(swap1, "row", across)
    out3 = lax.ppermute(inner2, "row", outward)
    across3 = lax.ppermute(jnp.where(mid, inner1, out2), "row", across)
    last = jnp.where(mid, inner2, out3)
    one = jnp.ones((), bool)
    early = None
    if early_work is not None:
        early = early_work([packed, swap1, inner1, across1, inner2, out2, across2],
                           jnp.stack([one, one, mid, one, mid, ~mid, one]))
        last, early = lax.optimization_barrier((last, early))
    across4 = lax.ppermute(last, "row", across)

    pieces = [packed, swap1, inner1, across1, inner2, out2, across2, out3, across3, across4]
    valid = [one, one, mid, one, mid, ~mid, one, ~mid, one, one]
    origin = [
        me, me ^ 4, jnp.where(low, me + 4, me - 4), partner,
        jnp.where(low, me + 8, me - 8), jnp.where(low, me + 8, me - 8), partner ^ 4,
        jnp.where(low, me + 12, me - 12),
        jnp.where(mid, jnp.where(low, partner + 4, partner - 4), jnp.where(low, partner + 8, partner - 8)),
        jnp.where(mid, jnp.where(low, partner + 8, partner - 8), jnp.where(low, partner + 12, partner - 12)),
    ]
    origin = jnp.clip(jnp.stack(origin), 0, devices - 1).astype(jnp.int32)
    if early_work is not None:
        return pieces, jnp.stack(valid), origin, early
    return pieces, jnp.stack(valid), origin


def sum_over_rows(value):
    devices = lax.axis_size("row")
    if devices != 16:
        if devices & (devices - 1):
            return lax.psum(value, "row")
        stride = 1
        while stride < devices:
            value = value + lax.ppermute(value, "row", [(i, i ^ stride) for i in range(devices)])
            stride *= 2
        return value
    me = lax.axis_index("row")
    for shift in (0, 2):
        got = {0: value}
        for m in (1, 2, 3):
            got[m] = lax.ppermute(value, "row", [(i, i ^ (m << shift)) for i in range(devices)])
        place = (me >> shift) & 3
        total = None
        for k in range(4):
            member = got[0]
            for m in (1, 2, 3):
                member = jnp.where((k ^ place) == m, got[m], member)
            total = member if total is None else total + member
        value = total
    return value


def shards(
    embeddings,
    local_scale,
    degree_scale,
    lanczos_block,
    previous_block,
    previous_coupling,
    tile_plan,
    tile_counts,
):
    width, own = embeddings.shape
    devices = lax.axis_size("row")
    total_rows = devices * own
    slots = tile_plan.shape[0]
    chip_split = devices == 16
    twin = [(r, r ^ 1) for r in range(devices)]
    weighted = (degree_scale[None, :] * lanczos_block).astype(jnp.bfloat16)
    plan_len = 2 * slots + 1
    plan_row = jnp.concatenate([tile_plan.reshape(-1), tile_counts]).astype(jnp.bfloat16)
    if chip_split:
        plan_row = jnp.concatenate([plan_row, lax.ppermute(plan_row, "row", twin)])
    plan_row = jnp.pad(plan_row, (0, own - plan_row.shape[0]))
    packed = jnp.concatenate(
        [embeddings, weighted, local_scale[None, :], plan_row[None, :]], axis=0
    )
    packed = jnp.pad(packed, ((0, -packed.shape[0] % (2 * LANCZOS)), (0, 0)))
    rows = packed.shape[0]
    if chip_split:
        twin_piece = lax.ppermute(packed, "row", twin)
        twin_terms = lax.ppermute(
            jnp.concatenate([lanczos_block, degree_scale[None, :]]), "row", twin
        )
        rows_x = jnp.concatenate([embeddings, twin_piece[:width]], axis=1)
        rows_scale = jnp.concatenate([local_scale, twin_piece[width + LANCZOS]])
    else:
        rows_x, rows_scale = embeddings, local_scale
    norm_rows = jnp.sum(jnp.square(rows_x.astype(jnp.float32)), axis=0)[:, None]
    log2e = 1.0 / math.log(2.0)
    recip_rows = (-log2e / rows_scale.astype(jnp.float32))[:, None]
    own_terms = ((rows_x * 2).T, norm_rows, recip_rows)
    if chip_split:
        def early_work(first, first_valid):
            return list_product(first_valid, own_terms, first, width, rows, split=True)

        pieces, valid, origin, early = gather_pieces(packed, early_work)
    else:
        pieces, valid, origin = gather_pieces(packed)

    plan_at = width + LANCZOS + 1
    copies = 2 if chip_split else 1
    plans = jnp.concatenate([p.reshape(-1, rows, own)[:, plan_at, : copies * plan_len] for p in pieces])
    plans = plans.astype(jnp.int32).reshape(-1, plan_len)
    counts = plans[:, 2 * slots]
    pairs = plans[:, : 2 * slots].reshape(-1, slots, 2)
    live = jnp.arange(slots, dtype=jnp.int32)[None, :] < counts[:, None]
    row_block = pairs[..., 0].reshape(-1)[:, None]
    col_block = pairs[..., 1].reshape(-1)[:, None]
    live = live.reshape(-1)[:, None]
    my_block = (lax.axis_index("row") * own) // BLK
    piece_block = ((origin * own) // BLK)[None, :]
    hit = live & (
        ((row_block == my_block) & (col_block == piece_block))
        | ((col_block == my_block) & (row_block == piece_block))
    )
    flags = jnp.any(hit, axis=0)
    if valid is not None:
        flags = flags & valid
    flags = flags.astype(jnp.int32)

    if chip_split:
        head = early.shape[0]
        summed = list_product(flags[head:], own_terms, pieces[head:], width, rows)
        summed = summed + jnp.sum(jnp.where(flags[:head, None, None] != 0, early, 0.0), axis=0)
    else:
        summed = own_rows_product(flags, own_terms, pieces[0].reshape(devices, rows, own), width)
    if chip_split:
        chip_lanes = jnp.concatenate([lanczos_block, twin_terms[:LANCZOS]], axis=1)
        chip_scale = jnp.concatenate([degree_scale, twin_terms[LANCZOS]])
        partial_value = lax.dot_general(
            chip_lanes, summed * (chip_scale[None, :] / math.sqrt(total_rows)),
            (((1,), (1,)), ((), ())), precision=HIGHEST,
        )
        summed = summed[:, :own] + lax.ppermute(summed[:, own:], "row", twin)
        scaled = summed * (degree_scale[None, :] / math.sqrt(total_rows))
    else:
        scaled = summed * (degree_scale[None, :] / math.sqrt(total_rows))
        partial_value = lax.dot_general(
            lanczos_block, scaled, (((1,), (1,)), ((), ())), precision=HIGHEST
        )
    coupling = sum_over_rows(partial_value) / total_rows
    projected = lax.dot_general(
        coupling, lanczos_block, (((0,), (0,)), ((), ())), precision=HIGHEST
    )
    result = scaled - projected - jnp.dot(previous_coupling, previous_block, precision=HIGHEST)
    return (result, coupling)


def solution(mesh):
    in_specs = (
        P(None, ("cohort", "row")),
        P(("cohort", "row")),
        P(("cohort", "row")),
        P(None, ("cohort", "row")),
        P(None, ("cohort", "row")),
        P("cohort", None),
        P(("cohort", "row"), None),
        P(("cohort", "row")),
    )
    out_specs = (P(None, ("cohort", "row")), P("cohort", None))
    return jax.shard_map(shards, mesh=mesh, in_specs=in_specs, out_specs=out_specs, check_vma=False)
```

```python
import functools
import math

import jax
import jax.numpy as jnp
from jax import lax
from jax.experimental import pallas as pl
from jax.experimental.pallas import tpu as pltpu
from jax.sharding import PartitionSpec as P

LANCZOS = 16
BLK = 1024


HIGHEST = lax.Precision.HIGHEST


def piece_terms(width, x_cols, w_cols, xo_ref, no_ref, ro_ref):
    x_wide = x_cols.astype(jnp.float32)
    norm_cols = jnp.sum(x_wide * x_wide, axis=0, keepdims=True)
    recip_cols = 1.0 / w_cols[LANCZOS : LANCZOS + 1, :].astype(jnp.float32)
    twice_inner = jnp.dot(xo_ref[...], x_cols, preferred_element_type=jnp.float32)
    distance = (no_ref[...] + norm_cols) - twice_inner
    weights = jnp.exp2(distance * (ro_ref[...] * recip_cols)).astype(jnp.bfloat16)
    return lax.dot_general(
        w_cols[:LANCZOS, :], weights, (((1,), (1,)), ((), ())),
        preferred_element_type=jnp.float32,
    )


def affinity_kernel(width, per, flag_ref, xo_ref, no_ref, ro_ref, x_ref, w_ref, out_ref):
    s = pl.program_id(0)

    @pl.when(s == 0)
    def _():
        out_ref[...] = jnp.zeros_like(out_ref)

    for k in range(per):

        @pl.when(flag_ref[s * per + k] != 0)
        def _():
            out_ref[...] += piece_terms(
                width, x_ref[k, :width, :], w_ref[k],
                xo_ref, no_ref, ro_ref,
            )


def list_kernel(width, rows, counts, split, head, flag_ref, xo_ref, no_ref, ro_ref, *refs):
    out_ref = refs[-1]
    if not split:
        out_ref[...] = jnp.zeros_like(out_ref)
    if head:
        early_ref, refs = refs[0], refs[1:]
        for k in range(head):

            @pl.when(flag_ref[k] != 0)
            def _(k=k):
                out_ref[...] += early_ref[k]

    slot = head
    for ref, count in zip(refs[:-1], counts):
        for k in range(count):
            base = k * rows

            def term(ref=ref, base=base):
                return piece_terms(
                    width,
                    ref[base : base + width, :],
                    ref[base + width : base + width + 2 * LANCZOS, :],
                    xo_ref, no_ref, ro_ref,
                )

            if split:

                @pl.when(flag_ref[slot] != 0)
                def _(term=term, slot=slot):
                    out_ref[slot] = term()

                @pl.when(flag_ref[slot] == 0)
                def _(slot=slot):
                    out_ref[slot] = jnp.zeros(out_ref.shape[1:], jnp.float32)

            else:

                @pl.when(flag_ref[slot] != 0)
                def _(term=term):
                    out_ref[...] += term()

            slot += 1


def list_product(flags, own_terms, pieces, width, rows, split=False, early=None):
    twice_own_t, norm_own, recip_own = own_terms
    own = twice_own_t.shape[0]
    counts = [p.shape[0] // rows for p in pieces]
    shape = (sum(counts), LANCZOS, own) if split else (LANCZOS, own)
    vmem = pl.BlockSpec(memory_space=pltpu.VMEM)
    cols = pieces[0].shape[1]
    slots = sum(counts)
    cost = pl.CostEstimate(
        flops=slots * 2 * own * cols * (width + LANCZOS),
        transcendentals=slots * own * cols,
        bytes_accessed=sum(p.size * 2 for p in pieces) + int(math.prod(shape)) * 4,
    )
    head = 0 if early is None else early.shape[0]
    extra = [] if early is None else [early]
    return pl.pallas_call(
        functools.partial(list_kernel, width, rows, counts, split, head),
        cost_estimate=cost,
        in_specs=[pl.BlockSpec(memory_space=pltpu.SMEM)] + [vmem] * (3 + len(extra) + len(pieces)),
        out_specs=vmem,
        out_shape=jax.ShapeDtypeStruct(shape, jnp.float32),
    )(flags, twice_own_t, norm_own, recip_own, *extra, *pieces)


def own_rows_product(flags, own_terms, mine, width):
    twice_own_t, norm_own, recip_own = own_terms
    own = twice_own_t.shape[0]
    slots, rows, cols = mine.shape
    per = 2 if slots % 2 == 0 else 1
    lanes_row = width // LANCZOS
    x_spec = pl.BlockSpec((per, rows, cols), lambda s, m: (s, 0, 0))
    w_spec = pl.BlockSpec((per, 2 * LANCZOS, cols), lambda s, m: (s, lanes_row // 2, 0))
    grid_spec = pltpu.PrefetchScalarGridSpec(
        num_scalar_prefetch=1,
        grid=(slots // per,),
        in_specs=[
            pl.BlockSpec((own, width), lambda s, m: (0, 0)),
            pl.BlockSpec((own, 1), lambda s, m: (0, 0)),
            pl.BlockSpec((own, 1), lambda s, m: (0, 0)),
            x_spec, w_spec,
        ],
        out_specs=pl.BlockSpec((LANCZOS, own), lambda s, m: (0, 0)),
    )
    return pl.pallas_call(
        functools.partial(affinity_kernel, width, per),
        grid_spec=grid_spec,
        out_shape=jax.ShapeDtypeStruct((LANCZOS, own), jnp.float32),
    )(flags, twice_own_t, norm_own, recip_own, mine, mine)


def gather_pieces(packed, early_work=None):
    devices = lax.axis_size("row")
    me = lax.axis_index("row")
    if devices != 16:
        pieces = lax.all_gather(packed, "row", axis=0, tiled=False)
        return [pieces], None, jnp.arange(devices, dtype=jnp.int32)
    zone = [r // 4 for r in range(16)]
    pairs_swap = [(r, r ^ 4) for r in range(16)]
    inner_swap = [(r, r + 4) for r in range(16) if zone[r] == 1] + [
        (r, r - 4) for r in range(16) if zone[r] == 2
    ]
    outward = [(r, r - 4) for r in range(16) if zone[r] == 1] + [
        (r, r + 4) for r in range(16) if zone[r] == 2
    ]
    across = [(r, r ^ 2) for r in range(16)]
    z = me // 4
    partner = me ^ 2
    mid = (z == 1) | (z == 2)
    low = z <= 1

    swap1 = lax.ppermute(packed, "row", pairs_swap)
    inner1 = lax.ppermute(packed, "row", inner_swap)
    across1 = lax.ppermute(packed, "row", across)
    swap1, inner1 = lax.optimization_barrier((swap1, inner1))
    inner2 = lax.ppermute(swap1, "row", inner_swap)
    out2 = lax.ppermute(inner1, "row", outward)
    across2 = lax.ppermute(swap1, "row", across)
    out3 = lax.ppermute(inner2, "row", outward)
    across3 = lax.ppermute(jnp.where(mid, inner1, out2), "row", across)
    last = jnp.where(mid, inner2, out3)
    one = jnp.ones((), bool)
    early = None
    if early_work is not None:
        early = early_work([packed, swap1, inner1, across1, inner2, out2, across2],
                           jnp.stack([one, one, mid, one, mid, ~mid, one]))
        last, early = lax.optimization_barrier((last, early))
    across4 = lax.ppermute(last, "row", across)

    pieces = [packed, swap1, inner1, across1, inner2, out2, across2, out3, across3, across4]
    valid = [one, one, mid, one, mid, ~mid, one, ~mid, one, one]
    origin = [
        me, me ^ 4, jnp.where(low, me + 4, me - 4), partner,
        jnp.where(low, me + 8, me - 8), jnp.where(low, me + 8, me - 8), partner ^ 4,
        jnp.where(low, me + 12, me - 12),
        jnp.where(mid, jnp.where(low, partner + 4, partner - 4), jnp.where(low, partner + 8, partner - 8)),
        jnp.where(mid, jnp.where(low, partner + 8, partner - 8), jnp.where(low, partner + 12, partner - 12)),
    ]
    origin = jnp.clip(jnp.stack(origin), 0, devices - 1).astype(jnp.int32)
    if early_work is not None:
        return pieces, jnp.stack(valid), origin, early
    return pieces, jnp.stack(valid), origin


def sum_over_rows(value):
    devices = lax.axis_size("row")
    if devices != 16:
        if devices & (devices - 1):
            return lax.psum(value, "row")
        stride = 1
        while stride < devices:
            value = value + lax.ppermute(value, "row", [(i, i ^ stride) for i in range(devices)])
            stride *= 2
        return value
    me = lax.axis_index("row")
    for shift in (0, 2):
        got = {0: value}
        for m in (1, 2, 3):
            got[m] = lax.ppermute(value, "row", [(i, i ^ (m << shift)) for i in range(devices)])
        place = (me >> shift) & 3
        total = None
        for k in range(4):
            member = got[0]
            for m in (1, 2, 3):
                member = jnp.where((k ^ place) == m, got[m], member)
            total = member if total is None else total + member
        value = total
    return value


def shards(
    embeddings,
    local_scale,
    degree_scale,
    lanczos_block,
    previous_block,
    previous_coupling,
    tile_plan,
    tile_counts,
):
    width, own = embeddings.shape
    devices = lax.axis_size("row")
    total_rows = devices * own
    slots = tile_plan.shape[0]
    chip_split = devices == 16
    twin = [(r, r ^ 1) for r in range(devices)]
    weighted = (degree_scale[None, :] * lanczos_block).astype(jnp.bfloat16)
    plan_len = 2 * slots + 1
    plan_row = jnp.concatenate([tile_plan.reshape(-1), tile_counts]).astype(jnp.bfloat16)
    if chip_split:
        plan_row = jnp.concatenate([plan_row, lax.ppermute(plan_row, "row", twin)])
    plan_row = jnp.pad(plan_row, (0, own - plan_row.shape[0]))
    packed = jnp.concatenate(
        [embeddings, weighted, local_scale[None, :], plan_row[None, :]], axis=0
    )
    packed = jnp.pad(packed, ((0, -packed.shape[0] % (2 * LANCZOS)), (0, 0)))
    rows = packed.shape[0]
    if chip_split:
        twin_piece = lax.ppermute(packed, "row", twin)
        twin_terms = lax.ppermute(
            jnp.concatenate([lanczos_block, degree_scale[None, :]]), "row", twin
        )
        rows_x = jnp.concatenate([embeddings, twin_piece[:width]], axis=1)
        rows_scale = jnp.concatenate([local_scale, twin_piece[width + LANCZOS]])
    else:
        rows_x, rows_scale = embeddings, local_scale
    norm_rows = jnp.sum(jnp.square(rows_x.astype(jnp.float32)), axis=0)[:, None]
    log2e = 1.0 / math.log(2.0)
    recip_rows = (-log2e / rows_scale.astype(jnp.float32))[:, None]
    own_terms = ((rows_x * 2).T, norm_rows, recip_rows)
    if chip_split:
        def early_work(first, first_valid):
            return list_product(first_valid, own_terms, first, width, rows, split=True)

        pieces, valid, origin, early = gather_pieces(packed, early_work)
    else:
        pieces, valid, origin = gather_pieces(packed)

    plan_at = width + LANCZOS + 1
    copies = 2 if chip_split else 1
    plans = jnp.concatenate([p.reshape(-1, rows, own)[:, plan_at, : copies * plan_len] for p in pieces])
    plans = plans.astype(jnp.int32).reshape(-1, plan_len)
    counts = plans[:, 2 * slots]
    pairs = plans[:, : 2 * slots].reshape(-1, slots, 2)
    live = jnp.arange(slots, dtype=jnp.int32)[None, :] < counts[:, None]
    row_block = pairs[..., 0].reshape(-1)[:, None]
    col_block = pairs[..., 1].reshape(-1)[:, None]
    live = live.reshape(-1)[:, None]
    my_block = (lax.axis_index("row") * own) // BLK
    piece_block = ((origin * own) // BLK)[None, :]
    hit = live & (
        ((row_block == my_block) & (col_block == piece_block))
        | ((col_block == my_block) & (row_block == piece_block))
    )
    flags = jnp.any(hit, axis=0)
    if valid is not None:
        flags = flags & valid
    flags = flags.astype(jnp.int32)

    if chip_split:
        head = early.shape[0]
        summed = list_product(flags, own_terms, pieces[head:], width, rows, early=early)
    else:
        summed = own_rows_product(flags, own_terms, pieces[0].reshape(devices, rows, own), width)
    if chip_split:
        chip_lanes = jnp.concatenate([lanczos_block, twin_terms[:LANCZOS]], axis=1)
        chip_scale = jnp.concatenate([degree_scale, twin_terms[LANCZOS]])
        partial_value = lax.dot_general(
            chip_lanes, summed * (chip_scale[None, :] / math.sqrt(total_rows)),
            (((1,), (1,)), ((), ())), precision=HIGHEST,
        )
        summed = summed[:, :own] + lax.ppermute(summed[:, own:], "row", twin)
        scaled = summed * (degree_scale[None, :] / math.sqrt(total_rows))
    else:
        scaled = summed * (degree_scale[None, :] / math.sqrt(total_rows))
        partial_value = lax.dot_general(
            lanczos_block, scaled, (((1,), (1,)), ((), ())), precision=HIGHEST
        )
    coupling = sum_over_rows(partial_value) / total_rows
    projected = lax.dot_general(
        coupling, lanczos_block, (((0,), (0,)), ((), ())), precision=HIGHEST
    )
    result = scaled - projected - jnp.dot(previous_coupling, previous_block, precision=HIGHEST)
    return (result, coupling)


def solution(mesh):
    in_specs = (
        P(None, ("cohort", "row")),
        P(("cohort", "row")),
        P(("cohort", "row")),
        P(None, ("cohort", "row")),
        P(None, ("cohort", "row")),
        P("cohort", None),
        P(("cohort", "row"), None),
        P(("cohort", "row")),
    )
    out_specs = (P(None, ("cohort", "row")), P("cohort", None))
    return jax.shard_map(shards, mesh=mesh, in_specs=in_specs, out_specs=out_specs, check_vma=False)
```

```python
import functools
import math

import jax
import jax.numpy as jnp
from jax import lax
from jax.experimental import pallas as pl
from jax.experimental.pallas import tpu as pltpu
from jax.sharding import PartitionSpec as P

LANCZOS = 16
BLK = 1024


HIGHEST = lax.Precision.HIGHEST


def piece_terms(width, x_cols, w_cols, xo_ref, no_ref, ro_ref):
    x_wide = x_cols.astype(jnp.float32)
    norm_cols = jnp.sum(x_wide * x_wide, axis=0, keepdims=True)
    recip_cols = 1.0 / w_cols[LANCZOS : LANCZOS + 1, :].astype(jnp.float32)
    twice_inner = jnp.dot(xo_ref[...], x_cols, preferred_element_type=jnp.float32)
    distance = (no_ref[...] + norm_cols) - twice_inner
    weights = jnp.exp2(distance * (ro_ref[...] * recip_cols)).astype(jnp.bfloat16)
    return lax.dot_general(
        w_cols[:LANCZOS, :], weights, (((1,), (1,)), ((), ())),
        preferred_element_type=jnp.float32,
    )


def affinity_kernel(width, per, flag_ref, xo_ref, no_ref, ro_ref, x_ref, w_ref, out_ref):
    s = pl.program_id(0)

    @pl.when(s == 0)
    def _():
        out_ref[...] = jnp.zeros_like(out_ref)

    for k in range(per):

        @pl.when(flag_ref[s * per + k] != 0)
        def _():
            out_ref[...] += piece_terms(
                width, x_ref[k, :width, :], w_ref[k],
                xo_ref, no_ref, ro_ref,
            )


def list_kernel(width, rows, counts, split, flag_ref, xo_ref, no_ref, ro_ref, *refs):
    out_ref = refs[-1]
    if not split:
        out_ref[...] = jnp.zeros_like(out_ref)
    slot = 0
    for ref, count in zip(refs[:-1], counts):
        for k in range(count):
            base = k * rows

            def term(ref=ref, base=base):
                return piece_terms(
                    width,
                    ref[base : base + width, :],
                    ref[base + width : base + width + LANCZOS + 1, :],
                    xo_ref, no_ref, ro_ref,
                )

            if split:

                @pl.when(flag_ref[slot] != 0)
                def _(term=term, slot=slot):
                    out_ref[slot] = term()

                @pl.when(flag_ref[slot] == 0)
                def _(slot=slot):
                    out_ref[slot] = jnp.zeros(out_ref.shape[1:], jnp.float32)

            else:

                @pl.when(flag_ref[slot] != 0)
                def _(term=term):
                    out_ref[...] += term()

            slot += 1


def list_product(flags, own_terms, pieces, width, rows, split=False):
    twice_own_t, norm_own, recip_own = own_terms
    own = twice_own_t.shape[0]
    counts = [p.shape[0] // rows for p in pieces]
    shape = (sum(counts), LANCZOS, own) if split else (LANCZOS, own)
    vmem = pl.BlockSpec(memory_space=pltpu.VMEM)
    cols = pieces[0].shape[1]
    slots = sum(counts)
    cost = pl.CostEstimate(
        flops=slots * 2 * own * cols * (width + LANCZOS),
        transcendentals=slots * own * cols,
        bytes_accessed=sum(p.size * 2 for p in pieces) + int(math.prod(shape)) * 4,
    )
    return pl.pallas_call(
        functools.partial(list_kernel, width, rows, counts, split),
        cost_estimate=cost,
        in_specs=[pl.BlockSpec(memory_space=pltpu.SMEM)] + [vmem] * (3 + len(pieces)),
        out_specs=vmem,
        out_shape=jax.ShapeDtypeStruct(shape, jnp.float32),
    )(flags, twice_own_t, norm_own, recip_own, *pieces)


def own_rows_product(flags, own_terms, mine, width):
    twice_own_t, norm_own, recip_own = own_terms
    own = twice_own_t.shape[0]
    slots, rows, cols = mine.shape
    per = 2 if slots % 2 == 0 else 1
    lanes_row = width // LANCZOS
    x_spec = pl.BlockSpec((per, rows, cols), lambda s, m: (s, 0, 0))
    w_spec = pl.BlockSpec((per, 2 * LANCZOS, cols), lambda s, m: (s, lanes_row // 2, 0))
    grid_spec = pltpu.PrefetchScalarGridSpec(
        num_scalar_prefetch=1,
        grid=(slots // per,),
        in_specs=[
            pl.BlockSpec((own, width), lambda s, m: (0, 0)),
            pl.BlockSpec((own, 1), lambda s, m: (0, 0)),
            pl.BlockSpec((own, 1), lambda s, m: (0, 0)),
            x_spec, w_spec,
        ],
        out_specs=pl.BlockSpec((LANCZOS, own), lambda s, m: (0, 0)),
    )
    return pl.pallas_call(
        functools.partial(affinity_kernel, width, per),
        grid_spec=grid_spec,
        out_shape=jax.ShapeDtypeStruct((LANCZOS, own), jnp.float32),
    )(flags, twice_own_t, norm_own, recip_own, mine, mine)


def gather_pieces(packed, early_work=None):
    devices = lax.axis_size("row")
    me = lax.axis_index("row")
    if devices != 16:
        pieces = lax.all_gather(packed, "row", axis=0, tiled=False)
        return [pieces], None, jnp.arange(devices, dtype=jnp.int32)
    zone = [r // 4 for r in range(16)]
    pairs_swap = [(r, r ^ 4) for r in range(16)]
    inner_swap = [(r, r + 4) for r in range(16) if zone[r] == 1] + [
        (r, r - 4) for r in range(16) if zone[r] == 2
    ]
    outward = [(r, r - 4) for r in range(16) if zone[r] == 1] + [
        (r, r + 4) for r in range(16) if zone[r] == 2
    ]
    across = [(r, r ^ 2) for r in range(16)]
    z = me // 4
    partner = me ^ 2
    mid = (z == 1) | (z == 2)
    low = z <= 1

    swap1 = lax.ppermute(packed, "row", pairs_swap)
    inner1 = lax.ppermute(packed, "row", inner_swap)
    across1 = lax.ppermute(packed, "row", across)
    swap1, inner1 = lax.optimization_barrier((swap1, inner1))
    inner2 = lax.ppermute(swap1, "row", inner_swap)
    out2 = lax.ppermute(inner1, "row", outward)
    across2 = lax.ppermute(swap1, "row", across)
    out3 = lax.ppermute(inner2, "row", outward)
    across3 = lax.ppermute(jnp.where(mid, inner1, out2), "row", across)
    last = jnp.where(mid, inner2, out3)
    one = jnp.ones((), bool)
    early = None
    if early_work is not None:
        early = early_work([packed, swap1, inner1, across1, inner2, out2, across2],
                           jnp.stack([one, one, mid, one, mid, ~mid, one]))
        last, early = lax.optimization_barrier((last, early))
    across4 = lax.ppermute(last, "row", across)

    pieces = [packed, swap1, inner1, across1, inner2, out2, across2, out3, across3, across4]
    valid = [one, one, mid, one, mid, ~mid, one, ~mid, one, one]
    origin = [
        me, me ^ 4, jnp.where(low, me + 4, me - 4), partner,
        jnp.where(low, me + 8, me - 8), jnp.where(low, me + 8, me - 8), partner ^ 4,
        jnp.where(low, me + 12, me - 12),
        jnp.where(mid, jnp.where(low, partner + 4, partner - 4), jnp.where(low, partner + 8, partner - 8)),
        jnp.where(mid, jnp.where(low, partner + 8, partner - 8), jnp.where(low, partner + 12, partner - 12)),
    ]
    origin = jnp.clip(jnp.stack(origin), 0, devices - 1).astype(jnp.int32)
    if early_work is not None:
        return pieces, jnp.stack(valid), origin, early
    return pieces, jnp.stack(valid), origin


def sum_over_rows(value):
    devices = lax.axis_size("row")
    if devices != 16:
        if devices & (devices - 1):
            return lax.psum(value, "row")
        stride = 1
        while stride < devices:
            value = value + lax.ppermute(value, "row", [(i, i ^ stride) for i in range(devices)])
            stride *= 2
        return value
    me = lax.axis_index("row")
    for shift in (0, 2):
        got = {0: value}
        for m in (1, 2, 3):
            got[m] = lax.ppermute(value, "row", [(i, i ^ (m << shift)) for i in range(devices)])
        place = (me >> shift) & 3
        total = None
        for k in range(4):
            member = got[0]
            for m in (1, 2, 3):
                member = jnp.where((k ^ place) == m, got[m], member)
            total = member if total is None else total + member
        value = total
    return value


def shards(
    embeddings,
    local_scale,
    degree_scale,
    lanczos_block,
    previous_block,
    previous_coupling,
    tile_plan,
    tile_counts,
):
    width, own = embeddings.shape
    devices = lax.axis_size("row")
    total_rows = devices * own
    slots = tile_plan.shape[0]
    chip_split = devices == 16
    twin = [(r, r ^ 1) for r in range(devices)]
    weighted = (degree_scale[None, :] * lanczos_block).astype(jnp.bfloat16)
    plan_len = 2 * slots + 1
    plan_row = jnp.concatenate([tile_plan.reshape(-1), tile_counts]).astype(jnp.bfloat16)
    if chip_split:
        plan_row = jnp.concatenate([plan_row, lax.ppermute(plan_row, "row", twin)])
    plan_row = jnp.pad(plan_row, (0, own - plan_row.shape[0]))
    packed = jnp.concatenate(
        [embeddings, weighted, local_scale[None, :], plan_row[None, :]], axis=0
    )
    packed = jnp.pad(packed, ((0, -packed.shape[0] % (8 if chip_split else 2 * LANCZOS)), (0, 0)))
    rows = packed.shape[0]
    if chip_split:
        twin_piece = lax.ppermute(packed, "row", twin)
        twin_terms = lax.ppermute(
            jnp.concatenate([lanczos_block, degree_scale[None, :]]), "row", twin
        )
        rows_x = jnp.concatenate([embeddings, twin_piece[:width]], axis=1)
        rows_scale = jnp.concatenate([local_scale, twin_piece[width + LANCZOS]])
    else:
        rows_x, rows_scale = embeddings, local_scale
    norm_rows = jnp.sum(jnp.square(rows_x.astype(jnp.float32)), axis=0)[:, None]
    log2e = 1.0 / math.log(2.0)
    recip_rows = (-log2e / rows_scale.astype(jnp.float32))[:, None]
    own_terms = ((rows_x * 2).T, norm_rows, recip_rows)
    if chip_split:
        def early_work(first, first_valid):
            return list_product(first_valid, own_terms, first, width, rows, split=True)

        pieces, valid, origin, early = gather_pieces(packed, early_work)
    else:
        pieces, valid, origin = gather_pieces(packed)

    plan_at = width + LANCZOS + 1
    copies = 2 if chip_split else 1
    plans = jnp.concatenate([p.reshape(-1, rows, own)[:, plan_at, : copies * plan_len] for p in pieces])
    plans = plans.astype(jnp.int32).reshape(-1, plan_len)
    counts = plans[:, 2 * slots]
    pairs = plans[:, : 2 * slots].reshape(-1, slots, 2)
    live = jnp.arange(slots, dtype=jnp.int32)[None, :] < counts[:, None]
    row_block = pairs[..., 0].reshape(-1)[:, None]
    col_block = pairs[..., 1].reshape(-1)[:, None]
    live = live.reshape(-1)[:, None]
    my_block = (lax.axis_index("row") * own) // BLK
    piece_block = ((origin * own) // BLK)[None, :]
    hit = live & (
        ((row_block == my_block) & (col_block == piece_block))
        | ((col_block == my_block) & (row_block == piece_block))
    )
    flags = jnp.any(hit, axis=0)
    if valid is not None:
        flags = flags & valid
    flags = flags.astype(jnp.int32)

    if chip_split:
        head = early.shape[0]
        summed = list_product(flags[head:], own_terms, pieces[head:], width, rows)
        summed = summed + jnp.sum(jnp.where(flags[:head, None, None] != 0, early, 0.0), axis=0)
    else:
        summed = own_rows_product(flags, own_terms, pieces[0].reshape(devices, rows, own), width)
    if chip_split:
        chip_lanes = jnp.concatenate([lanczos_block, twin_terms[:LANCZOS]], axis=1)
        chip_scale = jnp.concatenate([degree_scale, twin_terms[LANCZOS]])
        partial_value = lax.dot_general(
            chip_lanes, summed * (chip_scale[None, :] / math.sqrt(total_rows)),
            (((1,), (1,)), ((), ())), precision=HIGHEST,
        )
        summed = summed[:, :own] + lax.ppermute(summed[:, own:], "row", twin)
        scaled = summed * (degree_scale[None, :] / math.sqrt(total_rows))
    else:
        scaled = summed * (degree_scale[None, :] / math.sqrt(total_rows))
        partial_value = lax.dot_general(
            lanczos_block, scaled, (((1,), (1,)), ((), ())), precision=HIGHEST
        )
    coupling = sum_over_rows(partial_value) / total_rows
    projected = lax.dot_general(
        coupling, lanczos_block, (((0,), (0,)), ((), ())), precision=HIGHEST
    )
    result = scaled - projected - jnp.dot(previous_coupling, previous_block, precision=HIGHEST)
    return (result, coupling)


def solution(mesh):
    in_specs = (
        P(None, ("cohort", "row")),
        P(("cohort", "row")),
        P(("cohort", "row")),
        P(None, ("cohort", "row")),
        P(None, ("cohort", "row")),
        P("cohort", None),
        P(("cohort", "row"), None),
        P(("cohort", "row")),
    )
    out_specs = (P(None, ("cohort", "row")), P("cohort", None))
    return jax.shard_map(shards, mesh=mesh, in_specs=in_specs, out_specs=out_specs, check_vma=False)
```

```python
import functools
import math

import jax
import jax.numpy as jnp
from jax import lax
from jax.experimental import pallas as pl
from jax.experimental.pallas import tpu as pltpu
from jax.sharding import PartitionSpec as P

LANCZOS = 16
BLK = 1024


HIGHEST = lax.Precision.HIGHEST


def piece_terms(width, x_cols, w_cols, xo_ref, norm_rows, recip_rows):
    x_wide = x_cols.astype(jnp.float32)
    norm_cols = jnp.sum(x_wide * x_wide, axis=0, keepdims=True)
    recip_cols = 1.0 / w_cols[LANCZOS : LANCZOS + 1, :].astype(jnp.float32)
    twice_inner = jnp.dot(xo_ref[...], x_cols, preferred_element_type=jnp.float32)
    distance = (norm_rows + norm_cols) - twice_inner
    weights = jnp.exp2(distance * (recip_rows * recip_cols)).astype(jnp.bfloat16)
    return lax.dot_general(
        w_cols[:LANCZOS, :], weights, (((1,), (1,)), ((), ())),
        preferred_element_type=jnp.float32,
    )


def affinity_kernel(width, per, flag_ref, xo_ref, no_ref, ro_ref, x_ref, w_ref, out_ref):
    s = pl.program_id(0)

    @pl.when(s == 0)
    def _():
        out_ref[...] = jnp.zeros_like(out_ref)

    for k in range(per):

        @pl.when(flag_ref[s * per + k] != 0)
        def _():
            out_ref[...] += piece_terms(
                width, x_ref[k, :width, :], w_ref[k],
                xo_ref, no_ref[...], ro_ref[...],
            )


def list_kernel(width, rows, counts, split, flag_ref, xo_ref, terms_ref, *refs):
    out_ref = refs[-1]
    row_terms = jnp.transpose(terms_ref[...])
    norm_rows, recip_rows = row_terms[:, 0:1], row_terms[:, 1:2]
    if not split:
        out_ref[...] = jnp.zeros_like(out_ref)
    slot = 0
    for ref, count in zip(refs[:-1], counts):
        for k in range(count):
            base = k * rows

            def term(ref=ref, base=base):
                return piece_terms(
                    width,
                    ref[base : base + width, :],
                    ref[base + width : base + width + LANCZOS + 1, :],
                    xo_ref, norm_rows, recip_rows,
                )

            if split:

                @pl.when(flag_ref[slot] != 0)
                def _(term=term, slot=slot):
                    out_ref[slot] = term()

                @pl.when(flag_ref[slot] == 0)
                def _(slot=slot):
                    out_ref[slot] = jnp.zeros(out_ref.shape[1:], jnp.float32)

            else:

                @pl.when(flag_ref[slot] != 0)
                def _(term=term):
                    out_ref[...] += term()

            slot += 1


def list_product(flags, own_terms, pieces, width, rows, split=False):
    twice_own_t, norm_own, recip_own = own_terms
    own = twice_own_t.shape[0]
    counts = [p.shape[0] // rows for p in pieces]
    shape = (sum(counts), LANCZOS, own) if split else (LANCZOS, own)
    vmem = pl.BlockSpec(memory_space=pltpu.VMEM)
    row_terms = jnp.concatenate(
        [norm_own.reshape(1, own), recip_own.reshape(1, own), jnp.zeros((6, own), jnp.float32)]
    )
    cols = pieces[0].shape[1]
    slots = sum(counts)
    cost = pl.CostEstimate(
        flops=slots * 2 * own * cols * (width + LANCZOS),
        transcendentals=slots * own * cols,
        bytes_accessed=sum(p.size * 2 for p in pieces) + int(math.prod(shape)) * 4,
    )
    return pl.pallas_call(
        functools.partial(list_kernel, width, rows, counts, split),
        cost_estimate=cost,
        in_specs=[pl.BlockSpec(memory_space=pltpu.SMEM)] + [vmem] * (2 + len(pieces)),
        out_specs=vmem,
        out_shape=jax.ShapeDtypeStruct(shape, jnp.float32),
    )(flags, twice_own_t, row_terms, *pieces)


def own_rows_product(flags, own_terms, mine, width):
    twice_own_t, norm_own, recip_own = own_terms
    own = twice_own_t.shape[0]
    slots, rows, cols = mine.shape
    per = 2 if slots % 2 == 0 else 1
    lanes_row = width // LANCZOS
    x_spec = pl.BlockSpec((per, rows, cols), lambda s, m: (s, 0, 0))
    w_spec = pl.BlockSpec((per, 2 * LANCZOS, cols), lambda s, m: (s, lanes_row // 2, 0))
    grid_spec = pltpu.PrefetchScalarGridSpec(
        num_scalar_prefetch=1,
        grid=(slots // per,),
        in_specs=[
            pl.BlockSpec((own, width), lambda s, m: (0, 0)),
            pl.BlockSpec((own, 1), lambda s, m: (0, 0)),
            pl.BlockSpec((own, 1), lambda s, m: (0, 0)),
            x_spec, w_spec,
        ],
        out_specs=pl.BlockSpec((LANCZOS, own), lambda s, m: (0, 0)),
    )
    return pl.pallas_call(
        functools.partial(affinity_kernel, width, per),
        grid_spec=grid_spec,
        out_shape=jax.ShapeDtypeStruct((LANCZOS, own), jnp.float32),
    )(flags, twice_own_t, norm_own, recip_own, mine, mine)


def gather_pieces(packed, early_work=None):
    devices = lax.axis_size("row")
    me = lax.axis_index("row")
    if devices != 16:
        pieces = lax.all_gather(packed, "row", axis=0, tiled=False)
        return [pieces], None, jnp.arange(devices, dtype=jnp.int32)
    zone = [r // 4 for r in range(16)]
    pairs_swap = [(r, r ^ 4) for r in range(16)]
    inner_swap = [(r, r + 4) for r in range(16) if zone[r] == 1] + [
        (r, r - 4) for r in range(16) if zone[r] == 2
    ]
    outward = [(r, r - 4) for r in range(16) if zone[r] == 1] + [
        (r, r + 4) for r in range(16) if zone[r] == 2
    ]
    across = [(r, r ^ 2) for r in range(16)]
    z = me // 4
    partner = me ^ 2
    mid = (z == 1) | (z == 2)
    low = z <= 1

    swap1 = lax.ppermute(packed, "row", pairs_swap)
    inner1 = lax.ppermute(packed, "row", inner_swap)
    across1 = lax.ppermute(packed, "row", across)
    swap1, inner1 = lax.optimization_barrier((swap1, inner1))
    inner2 = lax.ppermute(swap1, "row", inner_swap)
    out2 = lax.ppermute(inner1, "row", outward)
    across2 = lax.ppermute(swap1, "row", across)
    out3 = lax.ppermute(inner2, "row", outward)
    across3 = lax.ppermute(jnp.where(mid, inner1, out2), "row", across)
    last = jnp.where(mid, inner2, out3)
    one = jnp.ones((), bool)
    early = None
    if early_work is not None:
        early = early_work([packed, swap1, inner1, across1, inner2, out2, across2],
                           jnp.stack([one, one, mid, one, mid, ~mid, one]))
        last, early = lax.optimization_barrier((last, early))
    across4 = lax.ppermute(last, "row", across)

    pieces = [packed, swap1, inner1, across1, inner2, out2, across2, out3, across3, across4]
    valid = [one, one, mid, one, mid, ~mid, one, ~mid, one, one]
    origin = [
        me, me ^ 4, jnp.where(low, me + 4, me - 4), partner,
        jnp.where(low, me + 8, me - 8), jnp.where(low, me + 8, me - 8), partner ^ 4,
        jnp.where(low, me + 12, me - 12),
        jnp.where(mid, jnp.where(low, partner + 4, partner - 4), jnp.where(low, partner + 8, partner - 8)),
        jnp.where(mid, jnp.where(low, partner + 8, partner - 8), jnp.where(low, partner + 12, partner - 12)),
    ]
    origin = jnp.clip(jnp.stack(origin), 0, devices - 1).astype(jnp.int32)
    if early_work is not None:
        return pieces, jnp.stack(valid), origin, early
    return pieces, jnp.stack(valid), origin


def sum_over_rows(value):
    devices = lax.axis_size("row")
    if devices != 16:
        if devices & (devices - 1):
            return lax.psum(value, "row")
        stride = 1
        while stride < devices:
            value = value + lax.ppermute(value, "row", [(i, i ^ stride) for i in range(devices)])
            stride *= 2
        return value
    me = lax.axis_index("row")
    for shift in (0, 2):
        got = {0: value}
        for m in (1, 2, 3):
            got[m] = lax.ppermute(value, "row", [(i, i ^ (m << shift)) for i in range(devices)])
        place = (me >> shift) & 3
        total = None
        for k in range(4):
            member = got[0]
            for m in (1, 2, 3):
                member = jnp.where((k ^ place) == m, got[m], member)
            total = member if total is None else total + member
        value = total
    return value


def shards(
    embeddings,
    local_scale,
    degree_scale,
    lanczos_block,
    previous_block,
    previous_coupling,
    tile_plan,
    tile_counts,
):
    width, own = embeddings.shape
    devices = lax.axis_size("row")
    total_rows = devices * own
    slots = tile_plan.shape[0]
    chip_split = devices == 16
    twin = [(r, r ^ 1) for r in range(devices)]
    weighted = (degree_scale[None, :] * lanczos_block).astype(jnp.bfloat16)
    plan_len = 2 * slots + 1
    plan_row = jnp.concatenate([tile_plan.reshape(-1), tile_counts]).astype(jnp.bfloat16)
    if chip_split:
        plan_row = jnp.concatenate([plan_row, lax.ppermute(plan_row, "row", twin)])
    plan_row = jnp.pad(plan_row, (0, own - plan_row.shape[0]))
    packed = jnp.concatenate(
        [embeddings, weighted, local_scale[None, :], plan_row[None, :]], axis=0
    )
    packed = jnp.pad(packed, ((0, -packed.shape[0] % (8 if chip_split else 2 * LANCZOS)), (0, 0)))
    rows = packed.shape[0]
    if chip_split:
        twin_piece = lax.ppermute(packed, "row", twin)
        twin_terms = lax.ppermute(
            jnp.concatenate([lanczos_block, degree_scale[None, :]]), "row", twin
        )
        rows_x = jnp.concatenate([embeddings, twin_piece[:width]], axis=1)
        rows_scale = jnp.concatenate([local_scale, twin_piece[width + LANCZOS]])
    else:
        rows_x, rows_scale = embeddings, local_scale
    norm_rows = jnp.sum(jnp.square(rows_x.astype(jnp.float32)), axis=0)[:, None]
    log2e = 1.0 / math.log(2.0)
    recip_rows = (-log2e / rows_scale.astype(jnp.float32))[:, None]
    own_terms = ((rows_x * 2).T, norm_rows, recip_rows)
    if chip_split:
        def early_work(first, first_valid):
            return list_product(first_valid, own_terms, first, width, rows, split=True)

        pieces, valid, origin, early = gather_pieces(packed, early_work)
    else:
        pieces, valid, origin = gather_pieces(packed)

    plan_at = width + LANCZOS + 1
    copies = 2 if chip_split else 1
    plans = jnp.concatenate([p.reshape(-1, rows, own)[:, plan_at, : copies * plan_len] for p in pieces])
    plans = plans.astype(jnp.int32).reshape(-1, plan_len)
    counts = plans[:, 2 * slots]
    pairs = plans[:, : 2 * slots].reshape(-1, slots, 2)
    live = jnp.arange(slots, dtype=jnp.int32)[None, :] < counts[:, None]
    row_block = pairs[..., 0].reshape(-1)[:, None]
    col_block = pairs[..., 1].reshape(-1)[:, None]
    live = live.reshape(-1)[:, None]
    my_block = (lax.axis_index("row") * own) // BLK
    piece_block = ((origin * own) // BLK)[None, :]
    hit = live & (
        ((row_block == my_block) & (col_block == piece_block))
        | ((col_block == my_block) & (row_block == piece_block))
    )
    flags = jnp.any(hit, axis=0)
    if valid is not None:
        flags = flags & valid
    flags = flags.astype(jnp.int32)

    if chip_split:
        head = early.shape[0]
        summed = list_product(flags[head:], own_terms, pieces[head:], width, rows)
        summed = summed + jnp.sum(jnp.where(flags[:head, None, None] != 0, early, 0.0), axis=0)
    else:
        summed = own_rows_product(flags, own_terms, pieces[0].reshape(devices, rows, own), width)
    if chip_split:
        chip_lanes = jnp.concatenate([lanczos_block, twin_terms[:LANCZOS]], axis=1)
        chip_scale = jnp.concatenate([degree_scale, twin_terms[LANCZOS]])
        partial_value = lax.dot_general(
            chip_lanes, summed * (chip_scale[None, :] / math.sqrt(total_rows)),
            (((1,), (1,)), ((), ())), precision=HIGHEST,
        )
        summed = summed[:, :own] + lax.ppermute(summed[:, own:], "row", twin)
        scaled = summed * (degree_scale[None, :] / math.sqrt(total_rows))
    else:
        scaled = summed * (degree_scale[None, :] / math.sqrt(total_rows))
        partial_value = lax.dot_general(
            lanczos_block, scaled, (((1,), (1,)), ((), ())), precision=HIGHEST
        )
    coupling = sum_over_rows(partial_value) / total_rows
    projected = lax.dot_general(
        coupling, lanczos_block, (((0,), (0,)), ((), ())), precision=HIGHEST
    )
    result = scaled - projected - jnp.dot(previous_coupling, previous_block, precision=HIGHEST)
    return (result, coupling)


def solution(mesh):
    in_specs = (
        P(None, ("cohort", "row")),
        P(("cohort", "row")),
        P(("cohort", "row")),
        P(None, ("cohort", "row")),
        P(None, ("cohort", "row")),
        P("cohort", None),
        P(("cohort", "row"), None),
        P(("cohort", "row")),
    )
    out_specs = (P(None, ("cohort", "row")), P("cohort", None))
    return jax.shard_map(shards, mesh=mesh, in_specs=in_specs, out_specs=out_specs, check_vma=False)
```

```python
import functools
import math

import jax
import jax.numpy as jnp
from jax import lax
from jax.experimental import pallas as pl
from jax.experimental.pallas import tpu as pltpu
from jax.sharding import PartitionSpec as P

LANCZOS = 16
BLK = 1024


HIGHEST = lax.Precision.HIGHEST


def piece_terms(width, x_cols, w_cols, xo_ref, norm_rows, recip_rows):
    x_wide = x_cols.astype(jnp.float32)
    norm_cols = jnp.sum(x_wide * x_wide, axis=0, keepdims=True)
    recip_cols = 1.0 / w_cols[LANCZOS : LANCZOS + 1, :].astype(jnp.float32)
    twice_inner = jnp.dot(xo_ref[...], x_cols, preferred_element_type=jnp.float32)
    distance = (norm_rows + norm_cols) - twice_inner
    weights = jnp.exp2(distance * (recip_rows * recip_cols)).astype(jnp.bfloat16)
    return lax.dot_general(
        w_cols[:LANCZOS, :], weights, (((1,), (1,)), ((), ())),
        preferred_element_type=jnp.float32,
    )


def affinity_kernel(width, per, flag_ref, xo_ref, no_ref, ro_ref, x_ref, w_ref, out_ref):
    s = pl.program_id(0)

    @pl.when(s == 0)
    def _():
        out_ref[...] = jnp.zeros_like(out_ref)

    for k in range(per):

        @pl.when(flag_ref[s * per + k] != 0)
        def _():
            out_ref[...] += piece_terms(
                width, x_ref[k, :width, :], w_ref[k],
                xo_ref, no_ref[...], ro_ref[...],
            )


def list_kernel(width, rows, counts, split, head, flag_ref, xo_ref, terms_ref, *refs):
    out_ref = refs[-1]
    row_terms = jnp.transpose(terms_ref[...])
    norm_rows, recip_rows = row_terms[:, 0:1], row_terms[:, 1:2]
    if not split:
        out_ref[...] = jnp.zeros_like(out_ref)
    if head:
        early_ref, refs = refs[0], refs[1:]
        for k in range(head):

            @pl.when(flag_ref[k] != 0)
            def _(k=k):
                out_ref[...] += early_ref[k]

    slot = head
    for ref, count in zip(refs[:-1], counts):
        for k in range(count):
            base = k * rows

            def term(ref=ref, base=base):
                return piece_terms(
                    width,
                    ref[base : base + width, :],
                    ref[base + width : base + width + LANCZOS + 1, :],
                    xo_ref, norm_rows, recip_rows,
                )

            if split:

                @pl.when(flag_ref[slot] != 0)
                def _(term=term, slot=slot):
                    out_ref[slot] = term()

                @pl.when(flag_ref[slot] == 0)
                def _(slot=slot):
                    out_ref[slot] = jnp.zeros(out_ref.shape[1:], jnp.float32)

            else:

                @pl.when(flag_ref[slot] != 0)
                def _(term=term):
                    out_ref[...] += term()

            slot += 1


def list_product(flags, own_terms, pieces, width, rows, split=False, early=None):
    twice_own_t, norm_own, recip_own = own_terms
    own = twice_own_t.shape[0]
    counts = [p.shape[0] // rows for p in pieces]
    shape = (sum(counts), LANCZOS, own) if split else (LANCZOS, own)
    vmem = pl.BlockSpec(memory_space=pltpu.VMEM)
    row_terms = jnp.concatenate(
        [norm_own.reshape(1, own), recip_own.reshape(1, own), jnp.zeros((6, own), jnp.float32)]
    )
    cols = pieces[0].shape[1]
    slots = sum(counts)
    cost = pl.CostEstimate(
        flops=slots * 2 * own * cols * (width + LANCZOS),
        transcendentals=slots * own * cols,
        bytes_accessed=sum(p.size * 2 for p in pieces) + int(math.prod(shape)) * 4,
    )
    head = 0 if early is None else early.shape[0]
    extra = [] if early is None else [early]
    return pl.pallas_call(
        functools.partial(list_kernel, width, rows, counts, split, head),
        cost_estimate=cost,
        in_specs=[pl.BlockSpec(memory_space=pltpu.SMEM)] + [vmem] * (2 + len(extra) + len(pieces)),
        out_specs=vmem,
        out_shape=jax.ShapeDtypeStruct(shape, jnp.float32),
    )(flags, twice_own_t, row_terms, *extra, *pieces)


def own_rows_product(flags, own_terms, mine, width):
    twice_own_t, norm_own, recip_own = own_terms
    own = twice_own_t.shape[0]
    slots, rows, cols = mine.shape
    per = 2 if slots % 2 == 0 else 1
    lanes_row = width // LANCZOS
    x_spec = pl.BlockSpec((per, rows, cols), lambda s, m: (s, 0, 0))
    w_spec = pl.BlockSpec((per, 2 * LANCZOS, cols), lambda s, m: (s, lanes_row // 2, 0))
    grid_spec = pltpu.PrefetchScalarGridSpec(
        num_scalar_prefetch=1,
        grid=(slots // per,),
        in_specs=[
            pl.BlockSpec((own, width), lambda s, m: (0, 0)),
            pl.BlockSpec((own, 1), lambda s, m: (0, 0)),
            pl.BlockSpec((own, 1), lambda s, m: (0, 0)),
            x_spec, w_spec,
        ],
        out_specs=pl.BlockSpec((LANCZOS, own), lambda s, m: (0, 0)),
    )
    return pl.pallas_call(
        functools.partial(affinity_kernel, width, per),
        grid_spec=grid_spec,
        out_shape=jax.ShapeDtypeStruct((LANCZOS, own), jnp.float32),
    )(flags, twice_own_t, norm_own, recip_own, mine, mine)


def gather_pieces(packed, early_work=None):
    devices = lax.axis_size("row")
    me = lax.axis_index("row")
    if devices != 16:
        pieces = lax.all_gather(packed, "row", axis=0, tiled=False)
        return [pieces], None, jnp.arange(devices, dtype=jnp.int32)
    zone = [r // 4 for r in range(16)]
    pairs_swap = [(r, r ^ 4) for r in range(16)]
    inner_swap = [(r, r + 4) for r in range(16) if zone[r] == 1] + [
        (r, r - 4) for r in range(16) if zone[r] == 2
    ]
    outward = [(r, r - 4) for r in range(16) if zone[r] == 1] + [
        (r, r + 4) for r in range(16) if zone[r] == 2
    ]
    across = [(r, r ^ 2) for r in range(16)]
    z = me // 4
    partner = me ^ 2
    mid = (z == 1) | (z == 2)
    low = z <= 1

    swap1 = lax.ppermute(packed, "row", pairs_swap)
    inner1 = lax.ppermute(packed, "row", inner_swap)
    across1 = lax.ppermute(packed, "row", across)
    swap1, inner1 = lax.optimization_barrier((swap1, inner1))
    inner2 = lax.ppermute(swap1, "row", inner_swap)
    out2 = lax.ppermute(inner1, "row", outward)
    across2 = lax.ppermute(swap1, "row", across)
    out3 = lax.ppermute(inner2, "row", outward)
    across3 = lax.ppermute(jnp.where(mid, inner1, out2), "row", across)
    last = jnp.where(mid, inner2, out3)
    one = jnp.ones((), bool)
    early = None
    if early_work is not None:
        early = early_work([packed, swap1, inner1, across1, inner2, out2, across2],
                           jnp.stack([one, one, mid, one, mid, ~mid, one]))
        last, early = lax.optimization_barrier((last, early))
    across4 = lax.ppermute(last, "row", across)

    pieces = [packed, swap1, inner1, across1, inner2, out2, across2, out3, across3, across4]
    valid = [one, one, mid, one, mid, ~mid, one, ~mid, one, one]
    origin = [
        me, me ^ 4, jnp.where(low, me + 4, me - 4), partner,
        jnp.where(low, me + 8, me - 8), jnp.where(low, me + 8, me - 8), partner ^ 4,
        jnp.where(low, me + 12, me - 12),
        jnp.where(mid, jnp.where(low, partner + 4, partner - 4), jnp.where(low, partner + 8, partner - 8)),
        jnp.where(mid, jnp.where(low, partner + 8, partner - 8), jnp.where(low, partner + 12, partner - 12)),
    ]
    origin = jnp.clip(jnp.stack(origin), 0, devices - 1).astype(jnp.int32)
    if early_work is not None:
        return pieces, jnp.stack(valid), origin, early
    return pieces, jnp.stack(valid), origin


def sum_over_rows(value):
    devices = lax.axis_size("row")
    if devices != 16:
        if devices & (devices - 1):
            return lax.psum(value, "row")
        stride = 1
        while stride < devices:
            value = value + lax.ppermute(value, "row", [(i, i ^ stride) for i in range(devices)])
            stride *= 2
        return value
    me = lax.axis_index("row")
    for shift in (0, 2):
        got = {0: value}
        for m in (1, 2, 3):
            got[m] = lax.ppermute(value, "row", [(i, i ^ (m << shift)) for i in range(devices)])
        place = (me >> shift) & 3
        total = None
        for k in range(4):
            member = got[0]
            for m in (1, 2, 3):
                member = jnp.where((k ^ place) == m, got[m], member)
            total = member if total is None else total + member
        value = total
    return value


def shards(
    embeddings,
    local_scale,
    degree_scale,
    lanczos_block,
    previous_block,
    previous_coupling,
    tile_plan,
    tile_counts,
):
    width, own = embeddings.shape
    devices = lax.axis_size("row")
    total_rows = devices * own
    slots = tile_plan.shape[0]
    chip_split = devices == 16
    twin = [(r, r ^ 1) for r in range(devices)]
    weighted = (degree_scale[None, :] * lanczos_block).astype(jnp.bfloat16)
    plan_len = 2 * slots + 1
    plan_row = jnp.concatenate([tile_plan.reshape(-1), tile_counts]).astype(jnp.bfloat16)
    if chip_split:
        plan_row = jnp.concatenate([plan_row, lax.ppermute(plan_row, "row", twin)])
    plan_row = jnp.pad(plan_row, (0, own - plan_row.shape[0]))
    packed = jnp.concatenate(
        [embeddings, weighted, local_scale[None, :], plan_row[None, :]], axis=0
    )
    packed = jnp.pad(packed, ((0, -packed.shape[0] % (8 if chip_split else 2 * LANCZOS)), (0, 0)))
    rows = packed.shape[0]
    if chip_split:
        twin_piece = lax.ppermute(packed, "row", twin)
        twin_terms = lax.ppermute(
            jnp.concatenate([lanczos_block, degree_scale[None, :]]), "row", twin
        )
        rows_x = jnp.concatenate([embeddings, twin_piece[:width]], axis=1)
        rows_scale = jnp.concatenate([local_scale, twin_piece[width + LANCZOS]])
    else:
        rows_x, rows_scale = embeddings, local_scale
    norm_rows = jnp.sum(jnp.square(rows_x.astype(jnp.float32)), axis=0)[:, None]
    log2e = 1.0 / math.log(2.0)
    recip_rows = (-log2e / rows_scale.astype(jnp.float32))[:, None]
    own_terms = ((rows_x * 2).T, norm_rows, recip_rows)
    if chip_split:
        def early_work(first, first_valid):
            return list_product(first_valid, own_terms, first, width, rows, split=True)

        pieces, valid, origin, early = gather_pieces(packed, early_work)
    else:
        pieces, valid, origin = gather_pieces(packed)

    plan_at = width + LANCZOS + 1
    copies = 2 if chip_split else 1
    plans = jnp.concatenate([p.reshape(-1, rows, own)[:, plan_at, : copies * plan_len] for p in pieces])
    plans = plans.astype(jnp.int32).reshape(-1, plan_len)
    counts = plans[:, 2 * slots]
    pairs = plans[:, : 2 * slots].reshape(-1, slots, 2)
    live = jnp.arange(slots, dtype=jnp.int32)[None, :] < counts[:, None]
    row_block = pairs[..., 0].reshape(-1)[:, None]
    col_block = pairs[..., 1].reshape(-1)[:, None]
    live = live.reshape(-1)[:, None]
    my_block = (lax.axis_index("row") * own) // BLK
    piece_block = ((origin * own) // BLK)[None, :]
    hit = live & (
        ((row_block == my_block) & (col_block == piece_block))
        | ((col_block == my_block) & (row_block == piece_block))
    )
    flags = jnp.any(hit, axis=0)
    if valid is not None:
        flags = flags & valid
    flags = flags.astype(jnp.int32)

    if chip_split:
        head = early.shape[0]
        summed = list_product(flags, own_terms, pieces[head:], width, rows, early=early)
    else:
        summed = own_rows_product(flags, own_terms, pieces[0].reshape(devices, rows, own), width)
    if chip_split:
        chip_lanes = jnp.concatenate([lanczos_block, twin_terms[:LANCZOS]], axis=1)
        chip_scale = jnp.concatenate([degree_scale, twin_terms[LANCZOS]])
        partial_value = lax.dot_general(
            chip_lanes, summed * (chip_scale[None, :] / math.sqrt(total_rows)),
            (((1,), (1,)), ((), ())), precision=HIGHEST,
        )
        summed = summed[:, :own] + lax.ppermute(summed[:, own:], "row", twin)
        scaled = summed * (degree_scale[None, :] / math.sqrt(total_rows))
    else:
        scaled = summed * (degree_scale[None, :] / math.sqrt(total_rows))
        partial_value = lax.dot_general(
            lanczos_block, scaled, (((1,), (1,)), ((), ())), precision=HIGHEST
        )
    coupling = sum_over_rows(partial_value) / total_rows
    projected = lax.dot_general(
        coupling, lanczos_block, (((0,), (0,)), ((), ())), precision=HIGHEST
    )
    result = scaled - projected - jnp.dot(previous_coupling, previous_block, precision=HIGHEST)
    return (result, coupling)


def solution(mesh):
    in_specs = (
        P(None, ("cohort", "row")),
        P(("cohort", "row")),
        P(("cohort", "row")),
        P(None, ("cohort", "row")),
        P(None, ("cohort", "row")),
        P("cohort", None),
        P(("cohort", "row"), None),
        P(("cohort", "row")),
    )
    out_specs = (P(None, ("cohort", "row")), P("cohort", None))
    return jax.shard_map(shards, mesh=mesh, in_specs=in_specs, out_specs=out_specs, check_vma=False)
```

```python
import functools
import math

import jax
import jax.numpy as jnp
from jax import lax
from jax.experimental import pallas as pl
from jax.experimental.pallas import tpu as pltpu
from jax.sharding import PartitionSpec as P

LANCZOS = 16
BLK = 1024


HIGHEST = lax.Precision.HIGHEST


def piece_terms(width, x_cols, w_cols, xo_ref, norm_rows, recip_rows):
    x_wide = x_cols.astype(jnp.float32)
    norm_cols = jnp.sum(x_wide * x_wide, axis=0, keepdims=True)
    recip_cols = 1.0 / w_cols[LANCZOS : LANCZOS + 1, :].astype(jnp.float32)
    twice_inner = jnp.dot(xo_ref[...], x_cols, preferred_element_type=jnp.float32)
    distance = (norm_rows + norm_cols) - twice_inner
    weights = jnp.exp2(distance * (recip_rows * recip_cols)).astype(jnp.bfloat16)
    return lax.dot_general(
        w_cols[:LANCZOS, :], weights, (((1,), (1,)), ((), ())),
        preferred_element_type=jnp.float32,
    )


def affinity_kernel(width, per, flag_ref, xo_ref, no_ref, ro_ref, x_ref, w_ref, out_ref):
    s = pl.program_id(0)

    @pl.when(s == 0)
    def _():
        out_ref[...] = jnp.zeros_like(out_ref)

    for k in range(per):

        @pl.when(flag_ref[s * per + k] != 0)
        def _():
            out_ref[...] += piece_terms(
                width, x_ref[k, :width, :], w_ref[k],
                xo_ref, no_ref[...], ro_ref[...],
            )


def list_kernel(width, rows, counts, split, flag_ref, xo_ref, terms_ref, *refs):
    out_ref = refs[-1]
    row_terms = jnp.transpose(terms_ref[...])
    norm_rows, recip_rows = row_terms[:, 0:1], row_terms[:, 1:2]
    if not split:
        out_ref[...] = jnp.zeros_like(out_ref)
    slot = 0
    for ref, count in zip(refs[:-1], counts):
        for k in range(count):
            base = k * rows

            def term(ref=ref, base=base):
                return piece_terms(
                    width,
                    ref[base : base + width, :],
                    ref[base + width : base + width + LANCZOS + 1, :],
                    xo_ref, norm_rows, recip_rows,
                )

            if split:

                @pl.when(flag_ref[slot] != 0)
                def _(term=term, slot=slot):
                    out_ref[slot] = term()

                @pl.when(flag_ref[slot] == 0)
                def _(slot=slot):
                    out_ref[slot] = jnp.zeros(out_ref.shape[1:], jnp.float32)

            else:

                @pl.when(flag_ref[slot] != 0)
                def _(term=term):
                    out_ref[...] += term()

            slot += 1


def list_product(flags, own_terms, pieces, width, rows, split=False):
    twice_own_t, norm_own, recip_own = own_terms
    own = twice_own_t.shape[0]
    counts = [p.shape[0] // rows for p in pieces]
    shape = (sum(counts), LANCZOS, own) if split else (LANCZOS, own)
    vmem = pl.BlockSpec(memory_space=pltpu.VMEM)
    row_terms = jnp.concatenate(
        [norm_own.reshape(1, own), recip_own.reshape(1, own), jnp.zeros((6, own), jnp.float32)]
    )
    cols = pieces[0].shape[1]
    slots = sum(counts)
    cost = pl.CostEstimate(
        flops=slots * 2 * own * cols * (width + LANCZOS),
        transcendentals=slots * own * cols,
        bytes_accessed=sum(p.size * 2 for p in pieces) + int(math.prod(shape)) * 4,
    )
    return pl.pallas_call(
        functools.partial(list_kernel, width, rows, counts, split),
        cost_estimate=cost,
        in_specs=[pl.BlockSpec(memory_space=pltpu.SMEM)] + [vmem] * (2 + len(pieces)),
        out_specs=vmem,
        out_shape=jax.ShapeDtypeStruct(shape, jnp.float32),
    )(flags, twice_own_t, row_terms, *pieces)


def own_rows_product(flags, own_terms, mine, width):
    twice_own_t, norm_own, recip_own = own_terms
    own = twice_own_t.shape[0]
    slots, rows, cols = mine.shape
    per = 2 if slots % 2 == 0 else 1
    lanes_row = width // LANCZOS
    x_spec = pl.BlockSpec((per, rows, cols), lambda s, m: (s, 0, 0))
    w_spec = pl.BlockSpec((per, 2 * LANCZOS, cols), lambda s, m: (s, lanes_row // 2, 0))
    grid_spec = pltpu.PrefetchScalarGridSpec(
        num_scalar_prefetch=1,
        grid=(slots // per,),
        in_specs=[
            pl.BlockSpec((own, width), lambda s, m: (0, 0)),
            pl.BlockSpec((own, 1), lambda s, m: (0, 0)),
            pl.BlockSpec((own, 1), lambda s, m: (0, 0)),
            x_spec, w_spec,
        ],
        out_specs=pl.BlockSpec((LANCZOS, own), lambda s, m: (0, 0)),
    )
    return pl.pallas_call(
        functools.partial(affinity_kernel, width, per),
        grid_spec=grid_spec,
        out_shape=jax.ShapeDtypeStruct((LANCZOS, own), jnp.float32),
    )(flags, twice_own_t, norm_own, recip_own, mine, mine)


def gather_pieces(packed, early_work=None):
    devices = lax.axis_size("row")
    me = lax.axis_index("row")
    if devices != 16:
        pieces = lax.all_gather(packed, "row", axis=0, tiled=False)
        return [pieces], None, jnp.arange(devices, dtype=jnp.int32)
    zone = [r // 4 for r in range(16)]
    pairs_swap = [(r, r ^ 4) for r in range(16)]
    inner_swap = [(r, r + 4) for r in range(16) if zone[r] == 1] + [
        (r, r - 4) for r in range(16) if zone[r] == 2
    ]
    outward = [(r, r - 4) for r in range(16) if zone[r] == 1] + [
        (r, r + 4) for r in range(16) if zone[r] == 2
    ]
    across = [(r, r ^ 2) for r in range(16)]
    z = me // 4
    partner = me ^ 2
    mid = (z == 1) | (z == 2)
    low = z <= 1

    swap1 = lax.ppermute(packed, "row", pairs_swap)
    inner1 = lax.ppermute(packed, "row", inner_swap)
    across1 = lax.ppermute(packed, "row", across)
    swap1, inner1 = lax.optimization_barrier((swap1, inner1))
    inner2 = lax.ppermute(swap1, "row", inner_swap)
    out2 = lax.ppermute(inner1, "row", outward)
    across2 = lax.ppermute(swap1, "row", across)
    out3 = lax.ppermute(inner2, "row", outward)
    across3 = lax.ppermute(jnp.where(mid, inner1, out2), "row", across)
    last = jnp.where(mid, inner2, out3)
    one = jnp.ones((), bool)
    early = None
    if early_work is not None:
        early = early_work([packed, swap1, inner1, across1, inner2, out2, across2],
                           jnp.stack([one, one, mid, one, mid, ~mid, one]))
        last, early = lax.optimization_barrier((last, early))
    across4 = lax.ppermute(last, "row", across)

    pieces = [packed, swap1, inner1, across1, inner2, out2, across2, out3, across3, across4]
    valid = [one, one, mid, one, mid, ~mid, one, ~mid, one, one]
    origin = [
        me, me ^ 4, jnp.where(low, me + 4, me - 4), partner,
        jnp.where(low, me + 8, me - 8), jnp.where(low, me + 8, me - 8), partner ^ 4,
        jnp.where(low, me + 12, me - 12),
        jnp.where(mid, jnp.where(low, partner + 4, partner - 4), jnp.where(low, partner + 8, partner - 8)),
        jnp.where(mid, jnp.where(low, partner + 8, partner - 8), jnp.where(low, partner + 12, partner - 12)),
    ]
    origin = jnp.clip(jnp.stack(origin), 0, devices - 1).astype(jnp.int32)
    if early_work is not None:
        return pieces, jnp.stack(valid), origin, early
    return pieces, jnp.stack(valid), origin


def sum_over_rows(value):
    devices = lax.axis_size("row")
    if devices != 16:
        if devices & (devices - 1):
            return lax.psum(value, "row")
        stride = 1
        while stride < devices:
            value = value + lax.ppermute(value, "row", [(i, i ^ stride) for i in range(devices)])
            stride *= 2
        return value
    me = lax.axis_index("row")
    got = {0: value}
    for m in (1, 2, 3):
        got[m] = lax.ppermute(value, "row", [(i, i ^ m) for i in range(devices)])
    place = me & 3
    total = None
    for k in range(4):
        member = got[0]
        for m in (1, 2, 3):
            member = jnp.where((k ^ place) == m, got[m], member)
        total = member if total is None else total + member
    value = total
    for stride in (4, 8):
        value = value + lax.ppermute(value, "row", [(i, i ^ stride) for i in range(devices)])
    return value


def shards(
    embeddings,
    local_scale,
    degree_scale,
    lanczos_block,
    previous_block,
    previous_coupling,
    tile_plan,
    tile_counts,
):
    width, own = embeddings.shape
    devices = lax.axis_size("row")
    total_rows = devices * own
    slots = tile_plan.shape[0]
    chip_split = devices == 16
    twin = [(r, r ^ 1) for r in range(devices)]
    weighted = (degree_scale[None, :] * lanczos_block).astype(jnp.bfloat16)
    plan_len = 2 * slots + 1
    plan_row = jnp.concatenate([tile_plan.reshape(-1), tile_counts]).astype(jnp.bfloat16)
    if chip_split:
        plan_row = jnp.concatenate([plan_row, lax.ppermute(plan_row, "row", twin)])
    plan_row = jnp.pad(plan_row, (0, own - plan_row.shape[0]))
    packed = jnp.concatenate(
        [embeddings, weighted, local_scale[None, :], plan_row[None, :]], axis=0
    )
    packed = jnp.pad(packed, ((0, -packed.shape[0] % (8 if chip_split else 2 * LANCZOS)), (0, 0)))
    rows = packed.shape[0]
    if chip_split:
        twin_piece = lax.ppermute(packed, "row", twin)
        twin_terms = lax.ppermute(
            jnp.concatenate([lanczos_block, degree_scale[None, :]]), "row", twin
        )
        rows_x = jnp.concatenate([embeddings, twin_piece[:width]], axis=1)
        rows_scale = jnp.concatenate([local_scale, twin_piece[width + LANCZOS]])
    else:
        rows_x, rows_scale = embeddings, local_scale
    norm_rows = jnp.sum(jnp.square(rows_x.astype(jnp.float32)), axis=0)[:, None]
    log2e = 1.0 / math.log(2.0)
    recip_rows = (-log2e / rows_scale.astype(jnp.float32))[:, None]
    own_terms = ((rows_x * 2).T, norm_rows, recip_rows)
    if chip_split:
        def early_work(first, first_valid):
            return list_product(first_valid, own_terms, first, width, rows, split=True)

        pieces, valid, origin, early = gather_pieces(packed, early_work)
    else:
        pieces, valid, origin = gather_pieces(packed)

    plan_at = width + LANCZOS + 1
    copies = 2 if chip_split else 1
    plans = jnp.concatenate([p.reshape(-1, rows, own)[:, plan_at, : copies * plan_len] for p in pieces])
    plans = plans.astype(jnp.int32).reshape(-1, plan_len)
    counts = plans[:, 2 * slots]
    pairs = plans[:, : 2 * slots].reshape(-1, slots, 2)
    live = jnp.arange(slots, dtype=jnp.int32)[None, :] < counts[:, None]
    row_block = pairs[..., 0].reshape(-1)[:, None]
    col_block = pairs[..., 1].reshape(-1)[:, None]
    live = live.reshape(-1)[:, None]
    my_block = (lax.axis_index("row") * own) // BLK
    piece_block = ((origin * own) // BLK)[None, :]
    hit = live & (
        ((row_block == my_block) & (col_block == piece_block))
        | ((col_block == my_block) & (row_block == piece_block))
    )
    flags = jnp.any(hit, axis=0)
    if valid is not None:
        flags = flags & valid
    flags = flags.astype(jnp.int32)

    if chip_split:
        head = early.shape[0]
        summed = list_product(flags[head:], own_terms, pieces[head:], width, rows)
        summed = summed + jnp.sum(jnp.where(flags[:head, None, None] != 0, early, 0.0), axis=0)
    else:
        summed = own_rows_product(flags, own_terms, pieces[0].reshape(devices, rows, own), width)
    if chip_split:
        chip_lanes = jnp.concatenate([lanczos_block, twin_terms[:LANCZOS]], axis=1)
        chip_scale = jnp.concatenate([degree_scale, twin_terms[LANCZOS]])
        partial_value = lax.dot_general(
            chip_lanes, summed * (chip_scale[None, :] / math.sqrt(total_rows)),
            (((1,), (1,)), ((), ())), precision=HIGHEST,
        )
        summed = summed[:, :own] + lax.ppermute(summed[:, own:], "row", twin)
        scaled = summed * (degree_scale[None, :] / math.sqrt(total_rows))
    else:
        scaled = summed * (degree_scale[None, :] / math.sqrt(total_rows))
        partial_value = lax.dot_general(
            lanczos_block, scaled, (((1,), (1,)), ((), ())), precision=HIGHEST
        )
    coupling = sum_over_rows(partial_value) / total_rows
    projected = lax.dot_general(
        coupling, lanczos_block, (((0,), (0,)), ((), ())), precision=HIGHEST
    )
    result = scaled - projected - jnp.dot(previous_coupling, previous_block, precision=HIGHEST)
    return (result, coupling)


def solution(mesh):
    in_specs = (
        P(None, ("cohort", "row")),
        P(("cohort", "row")),
        P(("cohort", "row")),
        P(None, ("cohort", "row")),
        P(None, ("cohort", "row")),
        P("cohort", None),
        P(("cohort", "row"), None),
        P(("cohort", "row")),
    )
    out_specs = (P(None, ("cohort", "row")), P("cohort", None))
    return jax.shard_map(shards, mesh=mesh, in_specs=in_specs, out_specs=out_specs, check_vma=False)
```

```python
import functools
import math

import jax
import jax.numpy as jnp
from jax import lax
from jax.experimental import pallas as pl
from jax.experimental.pallas import tpu as pltpu
from jax.sharding import PartitionSpec as P

LANCZOS = 16
BLK = 1024


HIGHEST = lax.Precision.HIGHEST


def piece_terms(width, x_cols, w_cols, xo_ref, norm_rows, recip_rows):
    x_wide = x_cols.astype(jnp.float32)
    norm_cols = jnp.sum(x_wide * x_wide, axis=0, keepdims=True)
    recip_cols = 1.0 / w_cols[LANCZOS : LANCZOS + 1, :].astype(jnp.float32)
    twice_inner = jnp.dot(xo_ref[...], x_cols, preferred_element_type=jnp.float32)
    distance = (norm_rows + norm_cols) - twice_inner
    weights = jnp.exp2(distance * (recip_rows * recip_cols)).astype(jnp.bfloat16)
    return lax.dot_general(
        w_cols[:LANCZOS, :], weights, (((1,), (1,)), ((), ())),
        preferred_element_type=jnp.float32,
    )


def affinity_kernel(width, per, flag_ref, xo_ref, no_ref, ro_ref, x_ref, w_ref, out_ref):
    s = pl.program_id(0)

    @pl.when(s == 0)
    def _():
        out_ref[...] = jnp.zeros_like(out_ref)

    for k in range(per):

        @pl.when(flag_ref[s * per + k] != 0)
        def _():
            out_ref[...] += piece_terms(
                width, x_ref[k, :width, :], w_ref[k],
                xo_ref, no_ref[...], ro_ref[...],
            )


def list_kernel(width, rows, counts, split, flag_ref, xo_ref, terms_ref, *refs):
    out_ref = refs[-1]
    row_terms = jnp.transpose(terms_ref[...])
    norm_rows, recip_rows = row_terms[:, 0:1], row_terms[:, 1:2]
    if not split:
        out_ref[...] = jnp.zeros_like(out_ref)
    slot = 0
    for ref, count in zip(refs[:-1], counts):
        for k in range(count):
            base = k * rows

            def term(ref=ref, base=base):
                return piece_terms(
                    width,
                    ref[base : base + width, :],
                    ref[base + width : base + width + LANCZOS + 1, :],
                    xo_ref, norm_rows, recip_rows,
                )

            if split:
                z = lax.axis_index("row") // 4
                middle = (z == 1) | (z == 2)
                keep = [True, True, middle, True, middle, ~middle, True][slot]
                keep = jnp.asarray(keep)

                @pl.when(keep)
                def _(term=term, slot=slot):
                    out_ref[slot] = term()

                @pl.when(jnp.logical_not(keep))
                def _(slot=slot):
                    out_ref[slot] = jnp.zeros(out_ref.shape[1:], jnp.float32)

            else:

                @pl.when(flag_ref[slot] != 0)
                def _(term=term):
                    out_ref[...] += term()

            slot += 1


def list_product(flags, own_terms, pieces, width, rows, split=False):
    twice_own_t, norm_own, recip_own = own_terms
    own = twice_own_t.shape[0]
    counts = [p.shape[0] // rows for p in pieces]
    shape = (sum(counts), LANCZOS, own) if split else (LANCZOS, own)
    vmem = pl.BlockSpec(memory_space=pltpu.VMEM)
    row_terms = jnp.concatenate(
        [norm_own.reshape(1, own), recip_own.reshape(1, own), jnp.zeros((6, own), jnp.float32)]
    )
    cols = pieces[0].shape[1]
    slots = sum(counts)
    cost = pl.CostEstimate(
        flops=slots * 2 * own * cols * (width + LANCZOS),
        transcendentals=slots * own * cols,
        bytes_accessed=sum(p.size * 2 for p in pieces) + int(math.prod(shape)) * 4,
    )
    return pl.pallas_call(
        functools.partial(list_kernel, width, rows, counts, split),
        cost_estimate=cost,
        in_specs=[pl.BlockSpec(memory_space=pltpu.SMEM)] + [vmem] * (2 + len(pieces)),
        out_specs=vmem,
        out_shape=jax.ShapeDtypeStruct(shape, jnp.float32),
    )(flags, twice_own_t, row_terms, *pieces)


def own_rows_product(flags, own_terms, mine, width):
    twice_own_t, norm_own, recip_own = own_terms
    own = twice_own_t.shape[0]
    slots, rows, cols = mine.shape
    per = 2 if slots % 2 == 0 else 1
    lanes_row = width // LANCZOS
    x_spec = pl.BlockSpec((per, rows, cols), lambda s, m: (s, 0, 0))
    w_spec = pl.BlockSpec((per, 2 * LANCZOS, cols), lambda s, m: (s, lanes_row // 2, 0))
    grid_spec = pltpu.PrefetchScalarGridSpec(
        num_scalar_prefetch=1,
        grid=(slots // per,),
        in_specs=[
            pl.BlockSpec((own, width), lambda s, m: (0, 0)),
            pl.BlockSpec((own, 1), lambda s, m: (0, 0)),
            pl.BlockSpec((own, 1), lambda s, m: (0, 0)),
            x_spec, w_spec,
        ],
        out_specs=pl.BlockSpec((LANCZOS, own), lambda s, m: (0, 0)),
    )
    return pl.pallas_call(
        functools.partial(affinity_kernel, width, per),
        grid_spec=grid_spec,
        out_shape=jax.ShapeDtypeStruct((LANCZOS, own), jnp.float32),
    )(flags, twice_own_t, norm_own, recip_own, mine, mine)


def gather_pieces(packed, early_work=None):
    devices = lax.axis_size("row")
    me = lax.axis_index("row")
    if devices != 16:
        pieces = lax.all_gather(packed, "row", axis=0, tiled=False)
        return [pieces], None, jnp.arange(devices, dtype=jnp.int32)
    zone = [r // 4 for r in range(16)]
    pairs_swap = [(r, r ^ 4) for r in range(16)]
    inner_swap = [(r, r + 4) for r in range(16) if zone[r] == 1] + [
        (r, r - 4) for r in range(16) if zone[r] == 2
    ]
    outward = [(r, r - 4) for r in range(16) if zone[r] == 1] + [
        (r, r + 4) for r in range(16) if zone[r] == 2
    ]
    across = [(r, r ^ 2) for r in range(16)]
    z = me // 4
    partner = me ^ 2
    mid = (z == 1) | (z == 2)
    low = z <= 1

    swap1 = lax.ppermute(packed, "row", pairs_swap)
    inner1 = lax.ppermute(packed, "row", inner_swap)
    across1 = lax.ppermute(packed, "row", across)
    swap1, inner1 = lax.optimization_barrier((swap1, inner1))
    inner2 = lax.ppermute(swap1, "row", inner_swap)
    out2 = lax.ppermute(inner1, "row", outward)
    across2 = lax.ppermute(swap1, "row", across)
    out3 = lax.ppermute(inner2, "row", outward)
    across3 = lax.ppermute(jnp.where(mid, inner1, out2), "row", across)
    last = jnp.where(mid, inner2, out3)
    one = jnp.ones((), bool)
    early = None
    if early_work is not None:
        early = early_work([packed, swap1, inner1, across1, inner2, out2, across2],
                           jnp.stack([one, one, mid, one, mid, ~mid, one]))
        last, early = lax.optimization_barrier((last, early))
    across4 = lax.ppermute(last, "row", across)

    pieces = [packed, swap1, inner1, across1, inner2, out2, across2, out3, across3, across4]
    valid = [one, one, mid, one, mid, ~mid, one, ~mid, one, one]
    origin = [
        me, me ^ 4, jnp.where(low, me + 4, me - 4), partner,
        jnp.where(low, me + 8, me - 8), jnp.where(low, me + 8, me - 8), partner ^ 4,
        jnp.where(low, me + 12, me - 12),
        jnp.where(mid, jnp.where(low, partner + 4, partner - 4), jnp.where(low, partner + 8, partner - 8)),
        jnp.where(mid, jnp.where(low, partner + 8, partner - 8), jnp.where(low, partner + 12, partner - 12)),
    ]
    origin = jnp.clip(jnp.stack(origin), 0, devices - 1).astype(jnp.int32)
    if early_work is not None:
        return pieces, jnp.stack(valid), origin, early
    return pieces, jnp.stack(valid), origin


def sum_over_rows(value):
    devices = lax.axis_size("row")
    if devices != 16:
        if devices & (devices - 1):
            return lax.psum(value, "row")
        stride = 1
        while stride < devices:
            value = value + lax.ppermute(value, "row", [(i, i ^ stride) for i in range(devices)])
            stride *= 2
        return value
    me = lax.axis_index("row")
    for shift in (0, 2):
        got = {0: value}
        for m in (1, 2, 3):
            got[m] = lax.ppermute(value, "row", [(i, i ^ (m << shift)) for i in range(devices)])
        place = (me >> shift) & 3
        total = None
        for k in range(4):
            member = got[0]
            for m in (1, 2, 3):
                member = jnp.where((k ^ place) == m, got[m], member)
            total = member if total is None else total + member
        value = total
    return value


def shards(
    embeddings,
    local_scale,
    degree_scale,
    lanczos_block,
    previous_block,
    previous_coupling,
    tile_plan,
    tile_counts,
):
    width, own = embeddings.shape
    devices = lax.axis_size("row")
    total_rows = devices * own
    slots = tile_plan.shape[0]
    chip_split = devices == 16
    twin = [(r, r ^ 1) for r in range(devices)]
    weighted = (degree_scale[None, :] * lanczos_block).astype(jnp.bfloat16)
    plan_len = 2 * slots + 1
    plan_row = jnp.concatenate([tile_plan.reshape(-1), tile_counts]).astype(jnp.bfloat16)
    if chip_split:
        plan_row = jnp.concatenate([plan_row, lax.ppermute(plan_row, "row", twin)])
    plan_row = jnp.pad(plan_row, (0, own - plan_row.shape[0]))
    packed = jnp.concatenate(
        [embeddings, weighted, local_scale[None, :], plan_row[None, :]], axis=0
    )
    packed = jnp.pad(packed, ((0, -packed.shape[0] % (8 if chip_split else 2 * LANCZOS)), (0, 0)))
    rows = packed.shape[0]
    if chip_split:
        twin_piece = lax.ppermute(packed, "row", twin)
        twin_terms = lax.ppermute(
            jnp.concatenate([lanczos_block, degree_scale[None, :]]), "row", twin
        )
        rows_x = jnp.concatenate([embeddings, twin_piece[:width]], axis=1)
        rows_scale = jnp.concatenate([local_scale, twin_piece[width + LANCZOS]])
    else:
        rows_x, rows_scale = embeddings, local_scale
    norm_rows = jnp.sum(jnp.square(rows_x.astype(jnp.float32)), axis=0)[:, None]
    log2e = 1.0 / math.log(2.0)
    recip_rows = (-log2e / rows_scale.astype(jnp.float32))[:, None]
    own_terms = ((rows_x * 2).T, norm_rows, recip_rows)
    if chip_split:
        def early_work(first, first_valid):
            return list_product(jnp.ones((len(first),), jnp.int32), own_terms, first, width, rows, split=True)

        pieces, valid, origin, early = gather_pieces(packed, early_work)
    else:
        pieces, valid, origin = gather_pieces(packed)

    plan_at = width + LANCZOS + 1
    copies = 2 if chip_split else 1
    plans = jnp.concatenate([p.reshape(-1, rows, own)[:, plan_at, : copies * plan_len] for p in pieces])
    plans = plans.astype(jnp.int32).reshape(-1, plan_len)
    counts = plans[:, 2 * slots]
    pairs = plans[:, : 2 * slots].reshape(-1, slots, 2)
    live = jnp.arange(slots, dtype=jnp.int32)[None, :] < counts[:, None]
    row_block = pairs[..., 0].reshape(-1)[:, None]
    col_block = pairs[..., 1].reshape(-1)[:, None]
    live = live.reshape(-1)[:, None]
    my_block = (lax.axis_index("row") * own) // BLK
    piece_block = ((origin * own) // BLK)[None, :]
    hit = live & (
        ((row_block == my_block) & (col_block == piece_block))
        | ((col_block == my_block) & (row_block == piece_block))
    )
    flags = jnp.any(hit, axis=0)
    if valid is not None:
        flags = flags & valid
    flags = flags.astype(jnp.int32)

    if chip_split:
        head = early.shape[0]
        summed = list_product(flags[head:], own_terms, pieces[head:], width, rows)
        summed = summed + jnp.sum(jnp.where(flags[:head, None, None] != 0, early, 0.0), axis=0)
    else:
        summed = own_rows_product(flags, own_terms, pieces[0].reshape(devices, rows, own), width)
    if chip_split:
        chip_lanes = jnp.concatenate([lanczos_block, twin_terms[:LANCZOS]], axis=1)
        chip_scale = jnp.concatenate([degree_scale, twin_terms[LANCZOS]])
        partial_value = lax.dot_general(
            chip_lanes, summed * (chip_scale[None, :] / math.sqrt(total_rows)),
            (((1,), (1,)), ((), ())), precision=HIGHEST,
        )
        summed = summed[:, :own] + lax.ppermute(summed[:, own:], "row", twin)
        scaled = summed * (degree_scale[None, :] / math.sqrt(total_rows))
    else:
        scaled = summed * (degree_scale[None, :] / math.sqrt(total_rows))
        partial_value = lax.dot_general(
            lanczos_block, scaled, (((1,), (1,)), ((), ())), precision=HIGHEST
        )
    coupling = sum_over_rows(partial_value) / total_rows
    projected = lax.dot_general(
        coupling, lanczos_block, (((0,), (0,)), ((), ())), precision=HIGHEST
    )
    result = scaled - projected - jnp.dot(previous_coupling, previous_block, precision=HIGHEST)
    return (result, coupling)


def solution(mesh):
    in_specs = (
        P(None, ("cohort", "row")),
        P(("cohort", "row")),
        P(("cohort", "row")),
        P(None, ("cohort", "row")),
        P(None, ("cohort", "row")),
        P("cohort", None),
        P(("cohort", "row"), None),
        P(("cohort", "row")),
    )
    out_specs = (P(None, ("cohort", "row")), P("cohort", None))
    return jax.shard_map(shards, mesh=mesh, in_specs=in_specs, out_specs=out_specs, check_vma=False)
```

```python
import functools
import math

import jax
import jax.numpy as jnp
from jax import lax
from jax.experimental import pallas as pl
from jax.experimental.pallas import tpu as pltpu
from jax.sharding import PartitionSpec as P

LANCZOS = 16
BLK = 1024


HIGHEST = lax.Precision.HIGHEST


def piece_terms(width, x_cols, w_cols, xo_ref, norm_rows, recip_rows):
    x_wide = x_cols.astype(jnp.float32)
    norm_cols = jnp.sum(x_wide * x_wide, axis=0, keepdims=True)
    recip_cols = 1.0 / w_cols[LANCZOS : LANCZOS + 1, :].astype(jnp.float32)
    twice_inner = jnp.dot(xo_ref[...], x_cols, preferred_element_type=jnp.float32)
    distance = (norm_rows + norm_cols) - twice_inner
    weights = jnp.exp2(distance * (recip_rows * recip_cols)).astype(jnp.bfloat16)
    return lax.dot_general(
        w_cols[:LANCZOS, :], weights, (((1,), (1,)), ((), ())),
        preferred_element_type=jnp.float32,
    )


def affinity_kernel(width, per, flag_ref, xo_ref, no_ref, ro_ref, x_ref, w_ref, out_ref):
    s = pl.program_id(0)

    @pl.when(s == 0)
    def _():
        out_ref[...] = jnp.zeros_like(out_ref)

    for k in range(per):

        @pl.when(flag_ref[s * per + k] != 0)
        def _():
            out_ref[...] += piece_terms(
                width, x_ref[k, :width, :], w_ref[k],
                xo_ref, no_ref[...], ro_ref[...],
            )


def list_kernel(width, rows, counts, split, offset, flag_ref, xo_ref, terms_ref, *refs):
    out_ref = refs[-1]
    row_terms = jnp.transpose(terms_ref[...])
    norm_rows, recip_rows = row_terms[:, 0:1], row_terms[:, 1:2]
    if not split:
        out_ref[...] = jnp.zeros_like(out_ref)
    slot = offset
    for ref, count in zip(refs[:-1], counts):
        for k in range(count):
            base = k * rows

            def term(ref=ref, base=base):
                return piece_terms(
                    width,
                    ref[base : base + width, :],
                    ref[base + width : base + width + LANCZOS + 1, :],
                    xo_ref, norm_rows, recip_rows,
                )

            if split:
                z = lax.axis_index("row") // 4
                middle = (z == 1) | (z == 2)
                keep = [True, True, middle, True, middle, ~middle, True][slot - offset]
                keep = jnp.asarray(keep)

                @pl.when(keep)
                def _(term=term, slot=slot):
                    out_ref[slot - offset] = term()

                @pl.when(jnp.logical_not(keep))
                def _(slot=slot):
                    out_ref[slot - offset] = jnp.zeros(out_ref.shape[1:], jnp.float32)

            else:

                @pl.when(flag_ref[slot] != 0)
                def _(term=term):
                    out_ref[...] += term()

            slot += 1


def list_product(flags, own_terms, pieces, width, rows, split=False, offset=0):
    twice_own_t, norm_own, recip_own = own_terms
    own = twice_own_t.shape[0]
    counts = [p.shape[0] // rows for p in pieces]
    shape = (sum(counts), LANCZOS, own) if split else (LANCZOS, own)
    vmem = pl.BlockSpec(memory_space=pltpu.VMEM)
    row_terms = jnp.concatenate(
        [norm_own.reshape(1, own), recip_own.reshape(1, own), jnp.zeros((6, own), jnp.float32)]
    )
    cols = pieces[0].shape[1]
    slots = sum(counts)
    cost = pl.CostEstimate(
        flops=slots * 2 * own * cols * (width + LANCZOS),
        transcendentals=slots * own * cols,
        bytes_accessed=sum(p.size * 2 for p in pieces) + int(math.prod(shape)) * 4,
    )
    return pl.pallas_call(
        functools.partial(list_kernel, width, rows, counts, split, offset),
        cost_estimate=cost,
        in_specs=[pl.BlockSpec(memory_space=pltpu.SMEM)] + [vmem] * (2 + len(pieces)),
        out_specs=vmem,
        out_shape=jax.ShapeDtypeStruct(shape, jnp.float32),
    )(flags, twice_own_t, row_terms, *pieces)


def own_rows_product(flags, own_terms, mine, width):
    twice_own_t, norm_own, recip_own = own_terms
    own = twice_own_t.shape[0]
    slots, rows, cols = mine.shape
    per = 2 if slots % 2 == 0 else 1
    lanes_row = width // LANCZOS
    x_spec = pl.BlockSpec((per, rows, cols), lambda s, m: (s, 0, 0))
    w_spec = pl.BlockSpec((per, 2 * LANCZOS, cols), lambda s, m: (s, lanes_row // 2, 0))
    grid_spec = pltpu.PrefetchScalarGridSpec(
        num_scalar_prefetch=1,
        grid=(slots // per,),
        in_specs=[
            pl.BlockSpec((own, width), lambda s, m: (0, 0)),
            pl.BlockSpec((own, 1), lambda s, m: (0, 0)),
            pl.BlockSpec((own, 1), lambda s, m: (0, 0)),
            x_spec, w_spec,
        ],
        out_specs=pl.BlockSpec((LANCZOS, own), lambda s, m: (0, 0)),
    )
    return pl.pallas_call(
        functools.partial(affinity_kernel, width, per),
        grid_spec=grid_spec,
        out_shape=jax.ShapeDtypeStruct((LANCZOS, own), jnp.float32),
    )(flags, twice_own_t, norm_own, recip_own, mine, mine)


def gather_pieces(packed, early_work=None):
    devices = lax.axis_size("row")
    me = lax.axis_index("row")
    if devices != 16:
        pieces = lax.all_gather(packed, "row", axis=0, tiled=False)
        return [pieces], None, jnp.arange(devices, dtype=jnp.int32)
    zone = [r // 4 for r in range(16)]
    pairs_swap = [(r, r ^ 4) for r in range(16)]
    inner_swap = [(r, r + 4) for r in range(16) if zone[r] == 1] + [
        (r, r - 4) for r in range(16) if zone[r] == 2
    ]
    outward = [(r, r - 4) for r in range(16) if zone[r] == 1] + [
        (r, r + 4) for r in range(16) if zone[r] == 2
    ]
    across = [(r, r ^ 2) for r in range(16)]
    z = me // 4
    partner = me ^ 2
    mid = (z == 1) | (z == 2)
    low = z <= 1

    swap1 = lax.ppermute(packed, "row", pairs_swap)
    inner1 = lax.ppermute(packed, "row", inner_swap)
    across1 = lax.ppermute(packed, "row", across)
    swap1, inner1 = lax.optimization_barrier((swap1, inner1))
    inner2 = lax.ppermute(swap1, "row", inner_swap)
    out2 = lax.ppermute(inner1, "row", outward)
    across2 = lax.ppermute(swap1, "row", across)
    out3 = lax.ppermute(inner2, "row", outward)
    across3 = lax.ppermute(jnp.where(mid, inner1, out2), "row", across)
    last = jnp.where(mid, inner2, out3)
    one = jnp.ones((), bool)
    early = None
    if early_work is not None:
        early = early_work([packed, swap1, inner1, across1, inner2, out2, across2],
                           jnp.stack([one, one, mid, one, mid, ~mid, one]))
        last, early = lax.optimization_barrier((last, early))
    across4 = lax.ppermute(last, "row", across)

    pieces = [packed, swap1, inner1, across1, inner2, out2, across2, out3, across3, across4]
    valid = [one, one, mid, one, mid, ~mid, one, ~mid, one, one]
    origin = [
        me, me ^ 4, jnp.where(low, me + 4, me - 4), partner,
        jnp.where(low, me + 8, me - 8), jnp.where(low, me + 8, me - 8), partner ^ 4,
        jnp.where(low, me + 12, me - 12),
        jnp.where(mid, jnp.where(low, partner + 4, partner - 4), jnp.where(low, partner + 8, partner - 8)),
        jnp.where(mid, jnp.where(low, partner + 8, partner - 8), jnp.where(low, partner + 12, partner - 12)),
    ]
    origin = jnp.clip(jnp.stack(origin), 0, devices - 1).astype(jnp.int32)
    if early_work is not None:
        return pieces, jnp.stack(valid), origin, early
    return pieces, jnp.stack(valid), origin


def sum_over_rows(value):
    devices = lax.axis_size("row")
    if devices != 16:
        if devices & (devices - 1):
            return lax.psum(value, "row")
        stride = 1
        while stride < devices:
            value = value + lax.ppermute(value, "row", [(i, i ^ stride) for i in range(devices)])
            stride *= 2
        return value
    me = lax.axis_index("row")
    for shift in (0, 2):
        got = {0: value}
        for m in (1, 2, 3):
            got[m] = lax.ppermute(value, "row", [(i, i ^ (m << shift)) for i in range(devices)])
        place = (me >> shift) & 3
        total = None
        for k in range(4):
            member = got[0]
            for m in (1, 2, 3):
                member = jnp.where((k ^ place) == m, got[m], member)
            total = member if total is None else total + member
        value = total
    return value


def shards(
    embeddings,
    local_scale,
    degree_scale,
    lanczos_block,
    previous_block,
    previous_coupling,
    tile_plan,
    tile_counts,
):
    width, own = embeddings.shape
    devices = lax.axis_size("row")
    total_rows = devices * own
    slots = tile_plan.shape[0]
    chip_split = devices == 16
    twin = [(r, r ^ 1) for r in range(devices)]
    weighted = (degree_scale[None, :] * lanczos_block).astype(jnp.bfloat16)
    plan_len = 2 * slots + 1
    plan_row = jnp.concatenate([tile_plan.reshape(-1), tile_counts]).astype(jnp.bfloat16)
    if chip_split:
        plan_row = jnp.concatenate([plan_row, lax.ppermute(plan_row, "row", twin)])
    plan_row = jnp.pad(plan_row, (0, own - plan_row.shape[0]))
    packed = jnp.concatenate(
        [embeddings, weighted, local_scale[None, :], plan_row[None, :]], axis=0
    )
    packed = jnp.pad(packed, ((0, -packed.shape[0] % (8 if chip_split else 2 * LANCZOS)), (0, 0)))
    rows = packed.shape[0]
    if chip_split:
        twin_piece = lax.ppermute(packed, "row", twin)
        twin_terms = lax.ppermute(
            jnp.concatenate([lanczos_block, degree_scale[None, :]]), "row", twin
        )
        rows_x = jnp.concatenate([embeddings, twin_piece[:width]], axis=1)
        rows_scale = jnp.concatenate([local_scale, twin_piece[width + LANCZOS]])
    else:
        rows_x, rows_scale = embeddings, local_scale
    norm_rows = jnp.sum(jnp.square(rows_x.astype(jnp.float32)), axis=0)[:, None]
    log2e = 1.0 / math.log(2.0)
    recip_rows = (-log2e / rows_scale.astype(jnp.float32))[:, None]
    own_terms = ((rows_x * 2).T, norm_rows, recip_rows)
    if chip_split:
        def early_work(first, first_valid):
            return list_product(jnp.ones((len(first),), jnp.int32), own_terms, first, width, rows, split=True)

        pieces, valid, origin, early = gather_pieces(packed, early_work)
    else:
        pieces, valid, origin = gather_pieces(packed)

    plan_at = width + LANCZOS + 1
    copies = 2 if chip_split else 1
    plans = jnp.concatenate([p.reshape(-1, rows, own)[:, plan_at, : copies * plan_len] for p in pieces])
    plans = plans.astype(jnp.int32).reshape(-1, plan_len)
    counts = plans[:, 2 * slots]
    pairs = plans[:, : 2 * slots].reshape(-1, slots, 2)
    live = jnp.arange(slots, dtype=jnp.int32)[None, :] < counts[:, None]
    row_block = pairs[..., 0].reshape(-1)[:, None]
    col_block = pairs[..., 1].reshape(-1)[:, None]
    live = live.reshape(-1)[:, None]
    my_block = (lax.axis_index("row") * own) // BLK
    piece_block = ((origin * own) // BLK)[None, :]
    hit = live & (
        ((row_block == my_block) & (col_block == piece_block))
        | ((col_block == my_block) & (row_block == piece_block))
    )
    flags = jnp.any(hit, axis=0)
    if valid is not None:
        flags = flags & valid
    flags = flags.astype(jnp.int32)

    if chip_split:
        head = early.shape[0]
        summed = list_product(flags, own_terms, pieces[head:], width, rows, offset=head)
        summed = summed + jnp.sum(jnp.where(flags[:head, None, None] != 0, early, 0.0), axis=0)
    else:
        summed = own_rows_product(flags, own_terms, pieces[0].reshape(devices, rows, own), width)
    if chip_split:
        chip_lanes = jnp.concatenate([lanczos_block, twin_terms[:LANCZOS]], axis=1)
        chip_scale = jnp.concatenate([degree_scale, twin_terms[LANCZOS]])
        partial_value = lax.dot_general(
            chip_lanes, summed * (chip_scale[None, :] / math.sqrt(total_rows)),
            (((1,), (1,)), ((), ())), precision=HIGHEST,
        )
        summed = summed[:, :own] + lax.ppermute(summed[:, own:], "row", twin)
        scaled = summed * (degree_scale[None, :] / math.sqrt(total_rows))
    else:
        scaled = summed * (degree_scale[None, :] / math.sqrt(total_rows))
        partial_value = lax.dot_general(
            lanczos_block, scaled, (((1,), (1,)), ((), ())), precision=HIGHEST
        )
    coupling = sum_over_rows(partial_value) / total_rows
    projected = lax.dot_general(
        coupling, lanczos_block, (((0,), (0,)), ((), ())), precision=HIGHEST
    )
    result = scaled - projected - jnp.dot(previous_coupling, previous_block, precision=HIGHEST)
    return (result, coupling)


def solution(mesh):
    in_specs = (
        P(None, ("cohort", "row")),
        P(("cohort", "row")),
        P(("cohort", "row")),
        P(None, ("cohort", "row")),
        P(None, ("cohort", "row")),
        P("cohort", None),
        P(("cohort", "row"), None),
        P(("cohort", "row")),
    )
    out_specs = (P(None, ("cohort", "row")), P("cohort", None))
    return jax.shard_map(shards, mesh=mesh, in_specs=in_specs, out_specs=out_specs, check_vma=False)
```
